32 devices in a mesh: rep: 2 (over x), seq: 4 (over y, core), head: 4 (over z).
Axes of the slice: x: 2, y: 2, z: 4, core: 2. Of those that a mesh axis runs over, the one named last changes fastest.
Arguments:
- query_rows: bfloat16 [2048, 8192], P(('rep', 'seq'), 'head'), parts along dimension 0, may hold values from -128 to 128
- span_kv: bfloat16 [2, 2048, 1024], P(None, ('rep', 'seq'), 'head'), parts along dimension 1, may hold values from -6 to 6
- cache_kv: bfloat16 [2, 4096, 1024], P(None, ('rep', 'seq'), 'head'), parts along dimension 1, may hold values from -6 to 6
- cache_len: int32 [8], P(('rep', 'seq')), parts along dimension 0, may hold values from 1 to 512, 1024 in all
Outputs:
- attended: bfloat16 [2048, 8192], P(('rep', 'seq'), 'head'), parts along dimension 0
The draws below stay inside these ranges and needn't reach their ends.
There are 2 independent parts, one for each index of `rep`. The reference program is written for one: setup_inputs(seed, part) draws one part's arguments, and reference() takes and returns one part's arrays. A program takes and returns all parts, laid end to end along the dimension named above; each array names one. Nothing has to cross between parts.
Inputs may be any that keep to these rules, and one draw needn't show every extreme that they name: `cache_len`: the earlier prompt is the filled slots of the instances in order; every instance has at least one filled slot and some instance is full.
All inputs are finite; a program needn't handle non-finite values. No bound on the sum of `cache_len` on one device may be relied on, other than what follows from the above.
Results may differ from the reference program's by a relative error of at most 0.007.
Values may be sent and summed in bfloat16 or wider, within the bound.
No kernel may reach another device: no remote copies, remote signals or barrier semaphores. Data moves between devices by JAX's collectives and lax.ppermute only.
A program may use at most 64 MiB of HBM per device.

```python
import math
import jax
import jax.numpy as jnp
import numpy as np
from jax import lax

HQ = 64
KVH = 8
HD = 128
C_DEV = 512
NEW = 1024
CACHE = 2048
N_SEQ = 4


def key_table(key):
    base = jnp.clip(jax.random.normal(jax.random.fold_in(key, 11), (CACHE, KVH * HD), jnp.float32), -6.0, 6.0)
    return base


def draw_cache_kv(key, part):
    keys = key_table(key)
    values = jnp.clip(jax.random.normal(jax.random.fold_in(key, 12), (CACHE, KVH * HD), jnp.float32), -6.0, 6.0)
    return jnp.stack([keys, values], axis=0).astype(jnp.bfloat16)


def draw_query_rows(key, part):
    base = jnp.clip(jax.random.normal(jax.random.fold_in(key, 13), (NEW, HQ * HD), jnp.float32), -6.0, 6.0)
    return base.astype(jnp.bfloat16)


def level_of(stream_key, dims, cuts, least, top_value):
    factor_of, own = 1.0, jax.random.fold_in(stream_key, 6)
    for position, blocks in cuts:
        draws = jnp.exp(jax.random.uniform(jax.random.fold_in(own, position), (blocks,), jnp.float32, least / len(cuts), top_value / len(cuts)))
        factor_of = factor_of * jnp.repeat(draws, dims[position] // blocks).reshape([-1 if axis == position else 1 for axis in range(len(dims))])
    return factor_of


def length_profile(count, total, bound, skew):
    loads = [(1 << 20) // math.isqrt(rank ** skew) + 1 for rank in range(2, count + 1)]
    surplus, holding = total - bound - (count - 1), [1] * (count - 1)
    while surplus > 0:
        movable = [i for i in range(count - 1) if holding[i] < bound]
        mass, remaining = sum([loads[i] for i in movable]), surplus
        for i in movable:
            extra = min(bound - holding[i], max(1, remaining * loads[i] // mass), surplus)
            holding[i] = holding[i] + extra
            surplus = surplus - extra
    return np.array([bound] + holding)


def ragged_sizes(stream_key, number_of, total, bound, lean):
    if number_of == 2:
        one = jax.random.randint(stream_key, (), max(1, total - bound), min(bound, total - 1) + 1)
        return jnp.stack([one, total - one])
    sizes = jnp.asarray(length_profile(number_of, total, bound, lean), jnp.int32)
    pairs = (number_of - 1) // 2
    source_of, receiver = sizes[1:1 + 2 * pairs:2], sizes[2:2 + 2 * pairs:2]
    slack = jnp.minimum(source_of - 1, bound - receiver)
    moved = jax.random.randint(jax.random.fold_in(stream_key, 1), (pairs,), 0, 1 << 20) % (slack + 1)
    sizes = sizes.at[1:1 + 2 * pairs:2].set(source_of - moved).at[2:2 + 2 * pairs:2].set(receiver + moved)
    return sizes[jax.random.permutation(jax.random.fold_in(stream_key, 2), number_of)]


def gaussian(rng, shape, deviation, reach, cuts=(), held_as=jnp.bfloat16):
    entries = jax.random.normal(rng, shape, jnp.float32) * deviation
    if len(cuts) > 0:
        entries = level_of(rng, shape, cuts, -0.22, 0.18) * entries
    return jnp.clip(entries, min=-reach, max=reach).astype(held_as)


def setup_inputs(seed: int = 0, part: int = 0) -> dict:
    arg_keys = jax.random.split(jax.random.key(seed), 5)
    part_keys = jax.random.split(jax.random.fold_in(arg_keys[4], part), 5)
    query_rows = draw_query_rows(jax.random.fold_in(jax.random.fold_in(arg_keys[4], part), 71), part)
    span_kv = gaussian(part_keys[1], (2, NEW, KVH * HD), 1.0, 6.0, ((1, 4), (2, 4)))
    cache_kv = draw_cache_kv(jax.random.fold_in(jax.random.fold_in(arg_keys[4], part), 71), part)
    cache_len = ragged_sizes(part_keys[3], N_SEQ, C_DEV * N_SEQ // 2, C_DEV, 2).astype(jnp.int32)
    return {"query_rows": query_rows, "span_kv": span_kv, "cache_kv": cache_kv, "cache_len": cache_len}


def reference(query_rows, span_kv, cache_kv, cache_len):
    new_count = query_rows.shape[0]
    cache_count = cache_kv.shape[1]
    all_keys = jnp.concatenate([cache_kv[0], span_kv[0]], axis=0)
    all_values = jnp.concatenate([cache_kv[1], span_kv[1]], axis=0)
    slots = jnp.arange(cache_count, dtype=jnp.int32)
    filled = (slots % C_DEV) < cache_len[slots // C_DEV]
    positions = jnp.arange(new_count, dtype=jnp.int32)
    visible = jnp.concatenate([jnp.broadcast_to(filled[None, :], (new_count, cache_count)),
                               positions[None, :] <= positions[:, None]], axis=1)
    q_group = HQ // KVH

    def one_head(head_index):
        head_query = lax.dynamic_slice_in_dim(query_rows, head_index * HD, HD, 1)
        kv_index = head_index // q_group
        head_keys = lax.dynamic_slice_in_dim(all_keys, kv_index * HD, HD, 1)
        head_values = lax.dynamic_slice_in_dim(all_values, kv_index * HD, HD, 1)
        scores = jnp.dot(head_query, head_keys.T, preferred_element_type=jnp.float32) * (HD ** -0.5)
        scores = jnp.where(visible, scores, jnp.float32(-1e30))
        peak = jnp.max(scores, axis=1, keepdims=True)
        weights = jnp.where(visible, jnp.exp(scores - peak), jnp.float32(0.0))
        norm_sum = jnp.sum(weights, axis=1, keepdims=True)
        mixed = jnp.dot(weights.astype(jnp.bfloat16), head_values, preferred_element_type=jnp.float32) / norm_sum
        return mixed.astype(jnp.bfloat16)

    heads_out = lax.map(one_head, jnp.arange(HQ, dtype=jnp.int32))
    return jnp.transpose(heads_out, (1, 0, 2)).reshape(new_count, HQ * HD)
```

```python
import functools

import jax
import jax.numpy as jnp
from jax import lax
from jax.experimental import pallas as pl
from jax.experimental.pallas import tpu as pltpu
from jax.sharding import PartitionSpec as P

HD = 128
NEG = -1e30
BK_CACHE = 128
BK_SPAN = 128


def attn_kernel(lens_ref, own_ref, q_ref, ck_ref, cv_ref, sk_ref, sv_ref, o_ref, *, n_seq, c_dev, t_rows):
    own = own_ref[0]
    q = q_ref[...]
    scale = HD ** (-0.5)

    def step(start, bk, k_ref, v_ref, carry, limit=None, causal=False):
        m_prev, l_prev, acc_prev = carry
        k = k_ref[pl.ds(start, bk), :]
        v = v_ref[pl.ds(start, bk), :]
        s = lax.dot_general(q, k, (((1,), (1,)), ((), ())), preferred_element_type=jnp.float32) * scale
        if limit is not None:
            cols = lax.broadcasted_iota(jnp.int32, s.shape, 1)
            s = jnp.where(cols < limit, s, NEG)
        if causal:
            cols = lax.broadcasted_iota(jnp.int32, s.shape, 1) + start
            rows = lax.broadcasted_iota(jnp.int32, s.shape, 0) + own * t_rows
            s = jnp.where(cols <= rows, s, NEG)
        m_new = jnp.maximum(m_prev, jnp.max(s, axis=1, keepdims=True))
        alpha = jnp.exp(m_prev - m_new)
        p = jnp.exp(s - m_new)
        l_new = alpha * l_prev + jnp.sum(p, axis=1, keepdims=True)
        acc_new = alpha * acc_prev + jnp.dot(p.astype(v.dtype), v, preferred_element_type=jnp.float32)
        return m_new, l_new, acc_new

    carry = (
        jnp.full((t_rows, 1), NEG, jnp.float32),
        jnp.zeros((t_rows, 1), jnp.float32),
        jnp.zeros((t_rows, HD), jnp.float32),
    )
    for inst in range(n_seq):
        length = lens_ref[inst]
        n_full = length // BK_CACHE
        rem = length - n_full * BK_CACHE
        base = inst * c_dev

        def full_block(b, c, base=base):
            start = pl.multiple_of(base + b * BK_CACHE, BK_CACHE)
            return step(start, BK_CACHE, ck_ref, cv_ref, c)

        carry = lax.fori_loop(0, n_full, full_block, carry)

        def part_block(c, base=base, n_full=n_full, rem=rem):
            start = pl.multiple_of(base + n_full * BK_CACHE, BK_CACHE)
            return step(start, BK_CACHE, ck_ref, cv_ref, c, limit=rem)

        carry = lax.cond(rem > 0, part_block, lambda c: c, carry)

    n_before = own * (t_rows // BK_SPAN)

    def span_block(b, c):
        start = pl.multiple_of(b * BK_SPAN, BK_SPAN)
        return step(start, BK_SPAN, sk_ref, sv_ref, c)

    carry = lax.fori_loop(0, n_before, span_block, carry)
    for d in range(t_rows // BK_SPAN):
        start = pl.multiple_of(own * t_rows + d * BK_SPAN, BK_SPAN)
        carry = step(start, BK_SPAN, sk_ref, sv_ref, carry, causal=True)

    m_fin, l_fin, acc_fin = carry
    o_ref[...] = (acc_fin / l_fin).astype(o_ref.dtype)


def attention(lens, own, q, ck, sk):
    t_rows, q_width = q.shape
    kv_width = ck.shape[2]
    kv_local = kv_width // HD
    group = q_width // kv_width
    n_seq = lens.shape[0]
    c_rows = ck.shape[1]
    s_rows = sk.shape[1]
    c_dev = c_rows // n_seq
    kernel = functools.partial(attn_kernel, n_seq=n_seq, c_dev=c_dev, t_rows=t_rows)
    grid_spec = pltpu.PrefetchScalarGridSpec(
        num_scalar_prefetch=2,
        grid=(kv_local, group),
        in_specs=[
            pl.BlockSpec((t_rows, HD), lambda k, g, *_: (0, k * group + g)),
            pl.BlockSpec((None, c_rows, HD), lambda k, g, *_: (0, 0, k)),
            pl.BlockSpec((None, c_rows, HD), lambda k, g, *_: (1, 0, k)),
            pl.BlockSpec((None, s_rows, HD), lambda k, g, *_: (0, 0, k)),
            pl.BlockSpec((None, s_rows, HD), lambda k, g, *_: (1, 0, k)),
        ],
        out_specs=pl.BlockSpec((t_rows, HD), lambda k, g, *_: (0, k * group + g)),
    )
    return pl.pallas_call(
        kernel,
        out_shape=jax.ShapeDtypeStruct((t_rows, q_width), q.dtype),
        grid_spec=grid_spec,
        compiler_params=pltpu.CompilerParams(dimension_semantics=("arbitrary", "arbitrary")),
    )(lens, own, q, ck, ck, sk, sk)


def body(query_rows, span_kv, cache_kv, cache_len):
    own = lax.axis_index("seq").astype(jnp.int32).reshape(1)
    lens = lax.all_gather(cache_len, "seq", axis=0, tiled=True)
    ck = lax.all_gather(cache_kv, "seq", axis=1, tiled=True)
    sk = lax.all_gather(span_kv, "seq", axis=1, tiled=True)
    return attention(lens, own, query_rows, ck, sk)


def solution(mesh):
    in_specs = (
        P(("rep", "seq"), "head"),
        P(None, ("rep", "seq"), "head"),
        P(None, ("rep", "seq"), "head"),
        P(("rep", "seq")),
    )
    out_specs = P(("rep", "seq"), "head")
    return jax.shard_map(body, mesh=mesh, in_specs=in_specs, out_specs=out_specs, check_vma=False)
```

```python
import functools

import jax
import jax.numpy as jnp
from jax import lax
from jax.experimental import pallas as pl
from jax.experimental.pallas import tpu as pltpu
from jax.sharding import PartitionSpec as P

HD = 128
NEG = -1e30
BK = 128


def attn_kernel(lens_ref, own_ref, q_ref, ck_ref, cv_ref, sk_ref, sv_ref, o_ref, m_ref, l_ref, acc_ref, *,
                n_seq, c_dev, t_rows, group):
    own = own_ref[0]
    scale = HD ** (-0.5)
    m_ref[...] = jnp.full(m_ref.shape, NEG, jnp.float32)
    l_ref[...] = jnp.zeros(l_ref.shape, jnp.float32)
    acc_ref[...] = jnp.zeros(acc_ref.shape, jnp.float32)

    def step(start, k_ref, v_ref, limit=None, causal=False):
        k = k_ref[pl.ds(start, BK), :]
        v_t = v_ref[pl.ds(start, BK), :].T
        mask = None
        if limit is not None:
            mask = lax.broadcasted_iota(jnp.int32, (BK, t_rows), 0) < limit
        if causal:
            keys = lax.broadcasted_iota(jnp.int32, (BK, t_rows), 0) + start
            rows = lax.broadcasted_iota(jnp.int32, (BK, t_rows), 1) + own * t_rows
            mask = keys <= rows
        for g in range(group):
            qg = q_ref[:, g * HD:(g + 1) * HD]
            s = lax.dot_general(k, qg, (((1,), (1,)), ((), ())), preferred_element_type=jnp.float32) * scale
            if mask is not None:
                s = jnp.where(mask, s, NEG)
            m_prev = m_ref[g]
            m_new = jnp.maximum(m_prev, jnp.max(s, axis=0, keepdims=True))
            alpha = jnp.exp(m_prev - m_new)
            p = jnp.exp(s - m_new)
            l_ref[g] = alpha * l_ref[g] + jnp.sum(p, axis=0, keepdims=True)
            acc_ref[g] = alpha * acc_ref[g] + jnp.dot(v_t, p.astype(v_t.dtype), preferred_element_type=jnp.float32)
            m_ref[g] = m_new

    def run(n, start_of, k_ref, v_ref):
        def loop_body(b, c):
            step(pl.multiple_of(start_of(b), BK), k_ref, v_ref)
            return c
        lax.fori_loop(0, n, loop_body, 0)

    for inst in range(n_seq):
        length = lens_ref[inst]
        n_full = length // BK
        rem = length - n_full * BK
        base = inst * c_dev
        run(n_full, lambda b, base=base: base + b * BK, ck_ref, cv_ref)

        @pl.when(rem > 0)
        def _(base=base, n_full=n_full, rem=rem):
            step(pl.multiple_of(base + n_full * BK, BK), ck_ref, cv_ref, limit=rem)

    run(own * (t_rows // BK), lambda b: b * BK, sk_ref, sv_ref)
    for d in range(t_rows // BK):
        step(pl.multiple_of(own * t_rows + d * BK, BK), sk_ref, sv_ref, causal=True)

    for g in range(group):
        o_ref[:, g * HD:(g + 1) * HD] = (acc_ref[g] / l_ref[g]).T.astype(o_ref.dtype)


def attention(lens, own, q, ck, sk):
    t_rows, q_width = q.shape
    kv_width = ck.shape[2]
    kv_local = kv_width // HD
    group = q_width // kv_width
    n_seq = lens.shape[0]
    c_rows = ck.shape[1]
    s_rows = sk.shape[1]
    c_dev = c_rows // n_seq
    kernel = functools.partial(attn_kernel, n_seq=n_seq, c_dev=c_dev, t_rows=t_rows, group=group)
    grid_spec = pltpu.PrefetchScalarGridSpec(
        num_scalar_prefetch=2,
        grid=(kv_local,),
        in_specs=[
            pl.BlockSpec((t_rows, group * HD), lambda k, *_: (0, k)),
            pl.BlockSpec((None, c_rows, HD), lambda k, *_: (0, 0, k)),
            pl.BlockSpec((None, c_rows, HD), lambda k, *_: (1, 0, k)),
            pl.BlockSpec((None, s_rows, HD), lambda k, *_: (0, 0, k)),
            pl.BlockSpec((None, s_rows, HD), lambda k, *_: (1, 0, k)),
        ],
        out_specs=pl.BlockSpec((t_rows, group * HD), lambda k, *_: (0, k)),
        scratch_shapes=[
            pltpu.VMEM((group, 1, t_rows), jnp.float32),
            pltpu.VMEM((group, 1, t_rows), jnp.float32),
            pltpu.VMEM((group, HD, t_rows), jnp.float32),
        ],
    )
    return pl.pallas_call(
        kernel,
        out_shape=jax.ShapeDtypeStruct((t_rows, q_width), q.dtype),
        grid_spec=grid_spec,
        compiler_params=pltpu.CompilerParams(dimension_semantics=("arbitrary",)),
    )(lens, own, q, ck, ck, sk, sk)


def body(query_rows, span_kv, cache_kv, cache_len):
    own = lax.axis_index("seq").astype(jnp.int32).reshape(1)
    lens = lax.all_gather(cache_len, "seq", axis=0, tiled=True)
    ck = lax.all_gather(cache_kv, "seq", axis=1, tiled=True)
    sk = lax.all_gather(span_kv, "seq", axis=1, tiled=True)
    return attention(lens, own, query_rows, ck, sk)


def solution(mesh):
    in_specs = (
        P(("rep", "seq"), "head"),
        P(None, ("rep", "seq"), "head"),
        P(None, ("rep", "seq"), "head"),
        P(("rep", "seq")),
    )
    out_specs = P(("rep", "seq"), "head")
    return jax.shard_map(body, mesh=mesh, in_specs=in_specs, out_specs=out_specs, check_vma=False)
```

```python
import functools

import jax
import jax.numpy as jnp
from jax import lax
from jax.experimental import pallas as pl
from jax.experimental.pallas import tpu as pltpu
from jax.sharding import PartitionSpec as P

HD = 128
NEG = -1e30
BK = 128


def step_kernel(sc_ref, q_ref, ck_ref, cv_ref, sk_ref, sv_ref, *rest, t_rows, group, first, last):
    if first:
        o_refs, (m_ref, l_ref, acc_ref) = rest[:-3], rest[-3:]
    else:
        m_in, l_in, acc_in = rest[:3]
        o_refs, (m_ref, l_ref, acc_ref) = rest[3:-3], rest[-3:]
    length = sc_ref[0]
    origin = sc_ref[1]
    own = sc_ref[2]
    scale = HD ** (-0.5)
    if first:
        m_ref[...] = jnp.full(m_ref.shape, NEG, jnp.float32)
        l_ref[...] = jnp.zeros(l_ref.shape, jnp.float32)
        acc_ref[...] = jnp.zeros(acc_ref.shape, jnp.float32)
    else:
        m_ref[...] = m_in[...]
        l_ref[...] = l_in[...]
        acc_ref[...] = acc_in[...]

    def step(start, k_ref, v_ref, limit=None, causal=False):
        k = k_ref[pl.ds(start, BK), :]
        v_t = v_ref[pl.ds(start, BK), :].T
        mask = None
        if limit is not None:
            mask = lax.broadcasted_iota(jnp.int32, (BK, t_rows), 0) < limit
        if causal:
            keys = lax.broadcasted_iota(jnp.int32, (BK, t_rows), 0) + start
            rows = lax.broadcasted_iota(jnp.int32, (BK, t_rows), 1)
            mask = keys <= rows
        for g in range(group):
            qg = q_ref[:, g * HD:(g + 1) * HD]
            s = lax.dot_general(k, qg, (((1,), (1,)), ((), ())), preferred_element_type=jnp.float32) * scale
            if mask is not None:
                s = jnp.where(mask, s, NEG)
            m_prev = m_ref[g]
            m_new = jnp.maximum(m_prev, jnp.max(s, axis=0, keepdims=True))
            alpha = jnp.exp(m_prev - m_new)
            p = jnp.exp(s - m_new)
            l_ref[g] = alpha * l_ref[g] + jnp.sum(p, axis=0, keepdims=True)
            acc_ref[g] = alpha * acc_ref[g] + jnp.dot(v_t, p.astype(v_t.dtype), preferred_element_type=jnp.float32)
            m_ref[g] = m_new

    n_full = length // BK
    rem = length - n_full * BK

    def loop_body(b, c):
        step(pl.multiple_of(b * BK, BK), ck_ref, cv_ref)
        return c

    lax.fori_loop(0, n_full, loop_body, 0)

    @pl.when(rem > 0)
    def _():
        step(pl.multiple_of(n_full * BK, BK), ck_ref, cv_ref, limit=rem)

    @pl.when(origin < own)
    def _():
        for d in range(t_rows // BK):
            step(d * BK, sk_ref, sv_ref)

    @pl.when(origin == own)
    def _():
        for d in range(t_rows // BK):
            step(d * BK, sk_ref, sv_ref, causal=True)

    if last:
        (o_ref,) = o_refs
        for g in range(group):
            o_ref[:, g * HD:(g + 1) * HD] = (acc_ref[g] / l_ref[g]).T.astype(o_ref.dtype)
    else:
        mo, lo, ao = o_refs
        mo[...] = m_ref[...]
        lo[...] = l_ref[...]
        ao[...] = acc_ref[...]


def attn_step(sc, q, cache, span, state, first, last):
    t_rows, q_width = q.shape
    kv_width = cache.shape[2]
    kv_local = kv_width // HD
    group = q_width // kv_width
    c_rows = cache.shape[1]
    s_rows = span.shape[1]
    heads = kv_local * group
    kernel = functools.partial(step_kernel, t_rows=t_rows, group=group, first=first, last=last)
    st_specs = [
        pl.BlockSpec((group, 1, t_rows), lambda k, *_: (k, 0, 0)),
        pl.BlockSpec((group, 1, t_rows), lambda k, *_: (k, 0, 0)),
        pl.BlockSpec((group, HD, t_rows), lambda k, *_: (k, 0, 0)),
    ]
    st_shapes = [
        jax.ShapeDtypeStruct((heads, 1, t_rows), jnp.float32),
        jax.ShapeDtypeStruct((heads, 1, t_rows), jnp.float32),
        jax.ShapeDtypeStruct((heads, HD, t_rows), jnp.float32),
    ]
    in_specs = [
        pl.BlockSpec((t_rows, group * HD), lambda k, *_: (0, k)),
        pl.BlockSpec((None, c_rows, HD), lambda k, *_: (0, 0, k)),
        pl.BlockSpec((None, c_rows, HD), lambda k, *_: (1, 0, k)),
        pl.BlockSpec((None, s_rows, HD), lambda k, *_: (0, 0, k)),
        pl.BlockSpec((None, s_rows, HD), lambda k, *_: (1, 0, k)),
    ]
    args = [sc, q, cache, cache, span, span]
    if not first:
        in_specs += st_specs
        args += list(state)
    if last:
        out_specs = pl.BlockSpec((t_rows, group * HD), lambda k, *_: (0, k))
        out_shape = jax.ShapeDtypeStruct((t_rows, q_width), q.dtype)
    else:
        out_specs = st_specs
        out_shape = st_shapes
    keys = c_rows + s_rows
    cost = pl.CostEstimate(
        flops=4 * heads * t_rows * keys * HD,
        transcendentals=heads * t_rows * keys,
        bytes_accessed=2 * (t_rows * q_width + 2 * keys * kv_width) + 8 * heads * t_rows * (HD + 2),
    )
    grid_spec = pltpu.PrefetchScalarGridSpec(
        num_scalar_prefetch=1,
        grid=(kv_local,),
        in_specs=in_specs,
        out_specs=out_specs,
        scratch_shapes=[
            pltpu.VMEM((group, 1, t_rows), jnp.float32),
            pltpu.VMEM((group, 1, t_rows), jnp.float32),
            pltpu.VMEM((group, HD, t_rows), jnp.float32),
        ],
    )
    return pl.pallas_call(
        kernel,
        out_shape=out_shape,
        grid_spec=grid_spec,
        compiler_params=pltpu.CompilerParams(dimension_semantics=("arbitrary",)),
        cost_estimate=cost,
    )(*args)


def body(query_rows, span_kv, cache_kv, cache_len):
    n = lax.psum(1, "seq")
    own = lax.axis_index("seq").astype(jnp.int32)
    right = [(i, (i + 1) % n) for i in range(n)]
    left = [(i, (i - 1) % n) for i in range(n)]
    n_right = n // 2
    n_left = n - 1 - n_right

    def pack(length, origin):
        return jnp.stack([length.reshape(()), origin, own]).astype(jnp.int32)

    local = (cache_kv, span_kv, cache_len)
    blocks = [(local, own)]
    r_blk, l_blk = local, local
    sends = []
    for k in range(1, max(n_right, n_left) + 1):
        if k <= n_right:
            r_blk = tuple(lax.ppermute(x, "seq", right) for x in r_blk)
            blocks.append((r_blk, (own - k) % n))
        if k <= n_left:
            l_blk = tuple(lax.ppermute(x, "seq", left) for x in l_blk)
            blocks.append((l_blk, (own + k) % n))
    state = None
    for i, ((cache, span, length), origin) in enumerate(blocks):
        sc = pack(length, origin)
        state = attn_step(sc, query_rows, cache, span, state, first=(i == 0), last=(i == len(blocks) - 1))
    return state


def solution(mesh):
    in_specs = (
        P(("rep", "seq"), "head"),
        P(None, ("rep", "seq"), "head"),
        P(None, ("rep", "seq"), "head"),
        P(("rep", "seq")),
    )
    out_specs = P(("rep", "seq"), "head")
    return jax.shard_map(body, mesh=mesh, in_specs=in_specs, out_specs=out_specs, check_vma=False)
```

```python
import functools

import jax
import jax.numpy as jnp
from jax import lax
from jax.experimental import pallas as pl
from jax.experimental.pallas import tpu as pltpu
from jax.sharding import PartitionSpec as P

HD = 128
NEG = -1e30
BK = 256


def step_kernel(sc_ref, q_ref, *refs, ninst, t_rows, group, first, last):
    inst_refs = [refs[4 * i:4 * i + 4] for i in range(ninst)]
    rest = refs[4 * ninst:]
    if first:
        state_in = None
    else:
        state_in, rest = rest[:3], rest[3:]
    qs_ref, m_ref, l_ref, acc_ref = rest[-4:]
    o_refs = rest[:-4]
    own = sc_ref[2 * ninst]
    scale = HD ** (-0.5)
    rows_all = group * t_rows
    reps = BK // 128
    for g in range(group):
        qs_ref[g * t_rows:(g + 1) * t_rows, :] = q_ref[:, g * HD:(g + 1) * HD]
    if first:
        m_ref[...] = jnp.full(m_ref.shape, NEG, jnp.float32)
        l_ref[...] = jnp.zeros(l_ref.shape, jnp.float32)
        acc_ref[...] = jnp.zeros(acc_ref.shape, jnp.float32)
    else:
        m_ref[...] = state_in[0][...]
        l_ref[...] = state_in[1][...]
        acc_ref[...] = state_in[2][...]

    def step(start, k_ref, v_ref, limit=None, causal=False):
        k = k_ref[pl.ds(start, BK), :]
        v = v_ref[pl.ds(start, BK), :]
        s = lax.dot_general(qs_ref[...], k, (((1,), (1,)), ((), ())), preferred_element_type=jnp.float32) * scale
        if limit is not None:
            mask = lax.broadcasted_iota(jnp.int32, (rows_all, BK), 1) < limit
            s = jnp.where(mask, s, NEG)
        if causal:
            cols = lax.broadcasted_iota(jnp.int32, (t_rows, BK), 1) + start
            rows = lax.broadcasted_iota(jnp.int32, (t_rows, BK), 0)
            mask = jnp.concatenate([cols <= rows] * group, axis=0)
            s = jnp.where(mask, s, NEG)
        m_prev = m_ref[...]
        m_new = jnp.maximum(m_prev, jnp.max(s, axis=1, keepdims=True))
        alpha = jnp.exp(m_prev - m_new)
        m_wide = m_new if reps == 1 else jnp.concatenate([m_new] * reps, axis=1)
        p = jnp.exp(s - m_wide)
        p_sum = p[:, :128]
        for r in range(1, reps):
            p_sum = p_sum + p[:, r * 128:(r + 1) * 128]
        l_ref[...] = alpha * l_ref[...] + p_sum
        acc_ref[...] = alpha * acc_ref[...] + jnp.dot(p.astype(v.dtype), v, preferred_element_type=jnp.float32)
        m_ref[...] = m_new

    for i, (ck_ref, cv_ref, sk_ref, sv_ref) in enumerate(inst_refs):
        length = sc_ref[i]
        origin = sc_ref[ninst + i]
        n_full = length // BK
        rem = length - n_full * BK

        def loop_body(b, c, ck_ref=ck_ref, cv_ref=cv_ref):
            step(pl.multiple_of(b * BK, BK), ck_ref, cv_ref)
            return c

        lax.fori_loop(0, n_full, loop_body, 0)

        @pl.when(rem > 0)
        def _(ck_ref=ck_ref, cv_ref=cv_ref, n_full=n_full, rem=rem):
            step(pl.multiple_of(n_full * BK, BK), ck_ref, cv_ref, limit=rem)

        @pl.when(origin < own)
        def _(sk_ref=sk_ref, sv_ref=sv_ref):
            for d in range(t_rows // BK):
                step(d * BK, sk_ref, sv_ref)

        @pl.when(origin == own)
        def _(sk_ref=sk_ref, sv_ref=sv_ref):
            for d in range(t_rows // BK):
                step(d * BK, sk_ref, sv_ref, causal=True)

    if last:
        (o_ref,) = o_refs
        out = acc_ref[...] / jnp.sum(l_ref[...], axis=1, keepdims=True)
        for g in range(group):
            o_ref[:, g * HD:(g + 1) * HD] = out[g * t_rows:(g + 1) * t_rows].astype(o_ref.dtype)
    else:
        o_refs[0][...] = m_ref[...]
        o_refs[1][...] = l_ref[...]
        o_refs[2][...] = acc_ref[...]


def attn_call(sc, q, insts, state, first, last):
    t_rows, q_width = q.shape
    kv_width = insts[0][0].shape[2]
    kv_local = kv_width // HD
    group = q_width // kv_width
    c_rows = insts[0][0].shape[1]
    s_rows = insts[0][1].shape[1]
    rows_all = group * t_rows
    ninst = len(insts)
    kernel = functools.partial(step_kernel, ninst=ninst, t_rows=t_rows, group=group, first=first, last=last)
    st_spec = pl.BlockSpec((rows_all, 128), lambda k, *_: (k, 0))
    st_shape = jax.ShapeDtypeStruct((kv_local * rows_all, 128), jnp.float32)
    in_specs = [pl.BlockSpec((t_rows, group * HD), lambda k, *_: (0, k))]
    args = [sc, q]
    for cache, span in insts:
        in_specs += [
            pl.BlockSpec((None, c_rows, HD), lambda k, *_: (0, 0, k)),
            pl.BlockSpec((None, c_rows, HD), lambda k, *_: (1, 0, k)),
            pl.BlockSpec((None, s_rows, HD), lambda k, *_: (0, 0, k)),
            pl.BlockSpec((None, s_rows, HD), lambda k, *_: (1, 0, k)),
        ]
        args += [cache, cache, span, span]
    if not first:
        in_specs += [st_spec] * 3
        args += list(state)
    if last:
        out_specs = pl.BlockSpec((t_rows, group * HD), lambda k, *_: (0, k))
        out_shape = jax.ShapeDtypeStruct((t_rows, q_width), q.dtype)
    else:
        out_specs = [st_spec] * 3
        out_shape = [st_shape] * 3
    keys = ninst * (c_rows + s_rows)
    heads = kv_local * group
    cost = pl.CostEstimate(
        flops=4 * heads * t_rows * keys * HD,
        transcendentals=heads * t_rows * keys,
        bytes_accessed=2 * t_rows * q_width + 4 * keys * kv_width + 24 * kv_local * rows_all * 128,
    )
    grid_spec = pltpu.PrefetchScalarGridSpec(
        num_scalar_prefetch=1,
        grid=(kv_local,),
        in_specs=in_specs,
        out_specs=out_specs,
        scratch_shapes=[
            pltpu.VMEM((rows_all, HD), q.dtype),
            pltpu.VMEM((rows_all, 128), jnp.float32),
            pltpu.VMEM((rows_all, 128), jnp.float32),
            pltpu.VMEM((rows_all, HD), jnp.float32),
        ],
    )
    return pl.pallas_call(
        kernel,
        out_shape=out_shape,
        grid_spec=grid_spec,
        compiler_params=pltpu.CompilerParams(dimension_semantics=("arbitrary",)),
        cost_estimate=cost,
    )(*args)


def chain_need(n, first_pairs, hops):
    need = []
    for k in range(len(hops)):
        keep = []
        for src in range(n):
            origin = first_pairs[src]
            dst = src
            for j in range(k + 1):
                dst = hops[j](dst)
            later = [dst, dst ^ 1]
            d = dst
            for j in range(k + 1, len(hops)):
                d = hops[j](d)
                later += [d, d ^ 1]
            if any(x > origin for x in later):
                keep.append(src)
        need.append(keep)
    return need


def body(query_rows, span_kv, cache_kv, cache_len):
    n = lax.psum(1, "seq")
    own = lax.axis_index("seq").astype(jnp.int32)
    n_chips = n // 2
    partner = [(i, i ^ 1) for i in range(n)]

    def send(x, fn, keep=None):
        pairs = [(i, fn(i)) for i in range(n) if keep is None or i in keep]
        return lax.ppermute(x, "seq", pairs)

    def to_partner(blk, origin_of, need_span):
        cache, span, length = blk
        keep = [i for i in range(n) if need_span(i)]
        return (send(cache, lambda i: i ^ 1), send(span, lambda i: i ^ 1, keep), send(length, lambda i: i ^ 1))

    local = (cache_kv, span_kv, cache_len)
    part = to_partner(local, None, lambda i: i < (i ^ 1))
    phases = [[(local, own), (part, own ^ 1)]]
    k_right = n_chips // 2
    k_left = n_chips - 1 - k_right
    for sign, count in ((2, k_right), (-2, k_left)):
        blk = local
        for k in range(1, count + 1):
            def hop(i, k=k):
                return (i + sign) % n
            def origin_at(i, k=k):
                return (i - sign * (k - 1)) % n
            keep = []
            for i in range(n):
                o = origin_at(i)
                d = i
                ok = False
                for j in range(k, count + 1):
                    d = (d + sign) % n
                    if d > o or (d ^ 1) > o:
                        ok = True
                if ok:
                    keep.append(i)
            cache, span, length = blk
            blk = (send(cache, hop), send(span, hop, keep), send(length, hop))
            origin = (own - sign * k) % n
            fwd_keep = [i for i in range(n) if (i ^ 1) > (i - sign * k) % n]
            cache, span, length = blk
            fwd = (send(cache, lambda i: i ^ 1), send(span, lambda i: i ^ 1, fwd_keep), send(length, lambda i: i ^ 1))
            phases.append([(blk, origin), (fwd, origin ^ 1)])
    state = None
    for pi, phase in enumerate(phases):
        lens = [b[2].reshape(1) for b, _ in phase]
        origins = [jnp.asarray(o, jnp.int32).reshape(1) for _, o in phase]
        sc = jnp.concatenate(lens + origins + [own.reshape(1)]).astype(jnp.int32)
        insts = [(b[0], b[1]) for b, _ in phase]
        state = attn_call(sc, query_rows, insts, state, first=(pi == 0), last=(pi == len(phases) - 1))
    return state


def solution(mesh):
    in_specs = (
        P(("rep", "seq"), "head"),
        P(None, ("rep", "seq"), "head"),
        P(None, ("rep", "seq"), "head"),
        P(("rep", "seq")),
    )
    out_specs = P(("rep", "seq"), "head")
    return jax.shard_map(body, mesh=mesh, in_specs=in_specs, out_specs=out_specs, check_vma=False)
```

```python
import functools

import jax
import jax.numpy as jnp
from jax import lax
from jax.experimental import pallas as pl
from jax.experimental.pallas import tpu as pltpu
from jax.sharding import PartitionSpec as P

HD = 128
NEG = -1e30
BK = 256


def step_kernel(sc_ref, q_ref, *refs, ninst, t_rows, group, first, last):
    inst_refs = [refs[4 * i:4 * i + 4] for i in range(ninst)]
    rest = refs[4 * ninst:]
    if first:
        state_in = None
    else:
        state_in, rest = rest[:3], rest[3:]
    qs_ref, m_ref, l_ref, acc_ref = rest[-4:]
    o_refs = rest[:-4]
    own = sc_ref[2 * ninst]
    scale = HD ** (-0.5)
    rows_all = group * t_rows
    reps = BK // 128
    for g in range(group):
        qs_ref[g * t_rows:(g + 1) * t_rows, :] = q_ref[:, g * HD:(g + 1) * HD]
    if first:
        m_ref[...] = jnp.full(m_ref.shape, NEG, jnp.float32)
        l_ref[...] = jnp.zeros(l_ref.shape, jnp.float32)
        acc_ref[...] = jnp.zeros(acc_ref.shape, jnp.float32)
    else:
        m_ref[...] = state_in[0][...]
        l_ref[...] = state_in[1][...]
        acc_ref[...] = state_in[2][...]

    def step(start, k_ref, v_ref, limit=None, causal=False):
        k = k_ref[pl.ds(start, BK), :]
        v = v_ref[pl.ds(start, BK), :]
        s = lax.dot_general(qs_ref[...], k, (((1,), (1,)), ((), ())), preferred_element_type=jnp.float32) * scale
        if limit is not None:
            mask = lax.broadcasted_iota(jnp.int32, (rows_all, BK), 1) < limit
            s = jnp.where(mask, s, NEG)
        if causal:
            cols = lax.broadcasted_iota(jnp.int32, (t_rows, BK), 1) + start
            rows = lax.broadcasted_iota(jnp.int32, (t_rows, BK), 0)
            mask = jnp.concatenate([cols <= rows] * group, axis=0)
            s = jnp.where(mask, s, NEG)
        m_prev = m_ref[...]
        m_new = jnp.maximum(m_prev, jnp.max(s, axis=1, keepdims=True))
        alpha = jnp.exp(m_prev - m_new)
        m_wide = m_new if reps == 1 else jnp.concatenate([m_new] * reps, axis=1)
        p = jnp.exp(s - m_wide)
        p_sum = p[:, :128]
        for r in range(1, reps):
            p_sum = p_sum + p[:, r * 128:(r + 1) * 128]
        l_ref[...] = alpha * l_ref[...] + p_sum
        acc_ref[...] = alpha * acc_ref[...] + jnp.dot(p.astype(v.dtype), v, preferred_element_type=jnp.float32)
        m_ref[...] = m_new

    for i, (ck_ref, cv_ref, sk_ref, sv_ref) in enumerate(inst_refs):
        length = sc_ref[i]
        origin = sc_ref[ninst + i]
        n_full = length // BK
        rem = length - n_full * BK

        def loop_body(b, c, ck_ref=ck_ref, cv_ref=cv_ref):
            step(pl.multiple_of(b * BK, BK), ck_ref, cv_ref)
            return c

        lax.fori_loop(0, n_full, loop_body, 0)

        @pl.when(rem > 0)
        def _(ck_ref=ck_ref, cv_ref=cv_ref, n_full=n_full, rem=rem):
            step(pl.multiple_of(n_full * BK, BK), ck_ref, cv_ref, limit=rem)

        @pl.when(origin < own)
        def _(sk_ref=sk_ref, sv_ref=sv_ref):
            for d in range(t_rows // BK):
                step(d * BK, sk_ref, sv_ref)

        @pl.when(origin == own)
        def _(sk_ref=sk_ref, sv_ref=sv_ref):
            for d in range(t_rows // BK):
                step(d * BK, sk_ref, sv_ref, causal=True)

    if last:
        (o_ref,) = o_refs
        out = acc_ref[...] / jnp.sum(l_ref[...], axis=1, keepdims=True)
        for g in range(group):
            o_ref[:, g * HD:(g + 1) * HD] = out[g * t_rows:(g + 1) * t_rows].astype(o_ref.dtype)
    else:
        o_refs[0][...] = m_ref[...]
        o_refs[1][...] = l_ref[...]
        o_refs[2][...] = acc_ref[...]


def attn_call(sc, q, insts, state, first, last):
    t_rows, q_width = q.shape
    kv_width = insts[0][0].shape[2]
    kv_local = kv_width // HD
    group = q_width // kv_width
    c_rows = insts[0][0].shape[1]
    s_rows = insts[0][1].shape[1]
    rows_all = group * t_rows
    ninst = len(insts)
    kernel = functools.partial(step_kernel, ninst=ninst, t_rows=t_rows, group=group, first=first, last=last)
    st_spec = pl.BlockSpec((rows_all, 128), lambda k, *_: (k, 0))
    st_shape = jax.ShapeDtypeStruct((kv_local * rows_all, 128), jnp.float32)
    in_specs = [pl.BlockSpec((t_rows, group * HD), lambda k, *_: (0, k))]
    args = [sc, q]
    for cache, span in insts:
        in_specs += [
            pl.BlockSpec((None, c_rows, HD), lambda k, *_: (0, 0, k)),
            pl.BlockSpec((None, c_rows, HD), lambda k, *_: (1, 0, k)),
            pl.BlockSpec((None, s_rows, HD), lambda k, *_: (0, 0, k)),
            pl.BlockSpec((None, s_rows, HD), lambda k, *_: (1, 0, k)),
        ]
        args += [cache, cache, span, span]
    if not first:
        in_specs += [st_spec] * 3
        args += list(state)
    if last:
        out_specs = pl.BlockSpec((t_rows, group * HD), lambda k, *_: (0, k))
        out_shape = jax.ShapeDtypeStruct((t_rows, q_width), q.dtype)
    else:
        out_specs = [st_spec] * 3
        out_shape = [st_shape] * 3
    keys = ninst * (c_rows + s_rows)
    heads = kv_local * group
    cost = pl.CostEstimate(
        flops=4 * heads * t_rows * keys * HD,
        transcendentals=heads * t_rows * keys,
        bytes_accessed=2 * t_rows * q_width + 4 * keys * kv_width + 24 * kv_local * rows_all * 128,
    )
    grid_spec = pltpu.PrefetchScalarGridSpec(
        num_scalar_prefetch=1,
        grid=(kv_local,),
        in_specs=in_specs,
        out_specs=out_specs,
        scratch_shapes=[
            pltpu.VMEM((rows_all, HD), q.dtype),
            pltpu.VMEM((rows_all, 128), jnp.float32),
            pltpu.VMEM((rows_all, 128), jnp.float32),
            pltpu.VMEM((rows_all, HD), jnp.float32),
        ],
    )
    return pl.pallas_call(
        kernel,
        out_shape=out_shape,
        grid_spec=grid_spec,
        compiler_params=pltpu.CompilerParams(dimension_semantics=("arbitrary",)),
        cost_estimate=cost,
    )(*args)


def chain_need(n, first_pairs, hops):
    need = []
    for k in range(len(hops)):
        keep = []
        for src in range(n):
            origin = first_pairs[src]
            dst = src
            for j in range(k + 1):
                dst = hops[j](dst)
            later = [dst, dst ^ 1]
            d = dst
            for j in range(k + 1, len(hops)):
                d = hops[j](d)
                later += [d, d ^ 1]
            if any(x > origin for x in later):
                keep.append(src)
        need.append(keep)
    return need


def body(query_rows, span_kv, cache_kv, cache_len):
    n = lax.psum(1, "seq")
    own = lax.axis_index("seq").astype(jnp.int32)
    n_chips = n // 2
    partner = [(i, i ^ 1) for i in range(n)]

    def send(x, fn, keep=None):
        pairs = [(i, fn(i)) for i in range(n) if keep is None or i in keep]
        return lax.ppermute(x, "seq", pairs)

    def to_partner(blk, origin_of, need_span):
        cache, span, length = blk
        keep = [i for i in range(n) if need_span(i)]
        return (send(cache, lambda i: i ^ 1), send(span, lambda i: i ^ 1, keep), send(length, lambda i: i ^ 1))

    local = (cache_kv, span_kv, cache_len)
    part = to_partner(local, None, lambda i: i < (i ^ 1))
    state = None
    n_calls = n_chips
    calls = [0]

    def run(phase, state):
        lens = [b[2].reshape(1) for b, _ in phase]
        origins = [jnp.asarray(o, jnp.int32).reshape(1) for _, o in phase]
        sc = jnp.concatenate(lens + origins + [own.reshape(1)]).astype(jnp.int32)
        insts = [(b[0], b[1]) for b, _ in phase]
        first = calls[0] == 0
        calls[0] += 1
        return attn_call(sc, query_rows, insts, state, first=first, last=(calls[0] == n_calls))

    k_right = n_chips // 2
    k_left = n_chips - 1 - k_right
    hops = []
    for sign, count in ((2, k_right), (-2, k_left)):
        blk = local
        for k in range(1, count + 1):
            def hop(i, sign=sign):
                return (i + sign) % n
            keep = []
            for i in range(n):
                o = (i - sign * (k - 1)) % n
                d = i
                ok = False
                for j in range(k, count + 1):
                    d = (d + sign) % n
                    if d > o or (d ^ 1) > o:
                        ok = True
                if ok:
                    keep.append(i)
            cache, span, length = blk
            blk = (send(cache, hop), send(span, hop, keep), send(length, hop))
            hops.append((blk, sign, k))
    state = run([(local, own), (part, own ^ 1)], state)
    for blk, sign, k in hops:
        state, blk = lax.optimization_barrier((state, blk))
        origin = (own - sign * k) % n
        fwd_keep = [i for i in range(n) if (i ^ 1) > (i - sign * k) % n]
        cache, span, length = blk
        fwd = (send(cache, lambda i: i ^ 1), send(span, lambda i: i ^ 1, fwd_keep), send(length, lambda i: i ^ 1))
        state = run([(blk, origin), (fwd, origin ^ 1)], state)
    return state


def solution(mesh):
    in_specs = (
        P(("rep", "seq"), "head"),
        P(None, ("rep", "seq"), "head"),
        P(None, ("rep", "seq"), "head"),
        P(("rep", "seq")),
    )
    out_specs = P(("rep", "seq"), "head")
    return jax.shard_map(body, mesh=mesh, in_specs=in_specs, out_specs=out_specs, check_vma=False)
```

```python
import functools

import jax
import jax.numpy as jnp
from jax import lax
from jax.experimental import pallas as pl
from jax.experimental.pallas import tpu as pltpu
from jax.sharding import PartitionSpec as P

HD = 128
NEG = -1e30
BK = 256


def step_kernel(sc_ref, q_ref, *refs, ninst, t_rows, group, first, last):
    inst_refs = [refs[4 * i:4 * i + 4] for i in range(ninst)]
    rest = refs[4 * ninst:]
    if first:
        state_in = None
    else:
        state_in, rest = rest[:3], rest[3:]
    qs_ref, m_ref, l_ref, acc_ref = rest[-4:]
    o_refs = rest[:-4]
    own = sc_ref[2 * ninst]
    scale = HD ** (-0.5)
    rows_all = group * t_rows
    reps = BK // 128
    for g in range(group):
        qs_ref[g * t_rows:(g + 1) * t_rows, :] = q_ref[:, g * HD:(g + 1) * HD]
    if first:
        m_ref[...] = jnp.full(m_ref.shape, NEG, jnp.float32)
        l_ref[...] = jnp.zeros(l_ref.shape, jnp.float32)
        acc_ref[...] = jnp.zeros(acc_ref.shape, jnp.float32)
    else:
        m_ref[...] = state_in[0][...]
        l_ref[...] = state_in[1][...]
        acc_ref[...] = state_in[2][...]

    def step(start, k_ref, v_ref, limit=None, causal=False):
        k = k_ref[pl.ds(start, BK), :]
        v = v_ref[pl.ds(start, BK), :]
        s = lax.dot_general(qs_ref[...], k, (((1,), (1,)), ((), ())), preferred_element_type=jnp.float32) * scale
        if limit is not None:
            mask = lax.broadcasted_iota(jnp.int32, (rows_all, BK), 1) < limit
            s = jnp.where(mask, s, NEG)
        if causal:
            cols = lax.broadcasted_iota(jnp.int32, (t_rows, BK), 1) + start
            rows = lax.broadcasted_iota(jnp.int32, (t_rows, BK), 0)
            mask = jnp.concatenate([cols <= rows] * group, axis=0)
            s = jnp.where(mask, s, NEG)
        m_prev = m_ref[...]
        m_new = jnp.maximum(m_prev, jnp.max(s, axis=1, keepdims=True))
        alpha = jnp.exp(m_prev - m_new)
        m_wide = m_new if reps == 1 else jnp.concatenate([m_new] * reps, axis=1)
        p = jnp.exp(s - m_wide)
        p_sum = p[:, :128]
        for r in range(1, reps):
            p_sum = p_sum + p[:, r * 128:(r + 1) * 128]
        l_ref[...] = alpha * l_ref[...] + p_sum
        acc_ref[...] = alpha * acc_ref[...] + jnp.dot(p.astype(v.dtype), v, preferred_element_type=jnp.float32)
        m_ref[...] = m_new

    for i, (ck_ref, cv_ref, sk_ref, sv_ref) in enumerate(inst_refs):
        length = sc_ref[i]
        origin = sc_ref[ninst + i]
        n_full = length // BK
        rem = length - n_full * BK

        def loop_body(b, c, ck_ref=ck_ref, cv_ref=cv_ref):
            step(pl.multiple_of(b * BK, BK), ck_ref, cv_ref)
            return c

        lax.fori_loop(0, n_full, loop_body, 0)

        @pl.when(rem > 0)
        def _(ck_ref=ck_ref, cv_ref=cv_ref, n_full=n_full, rem=rem):
            step(pl.multiple_of(n_full * BK, BK), ck_ref, cv_ref, limit=rem)

        @pl.when(origin < own)
        def _(sk_ref=sk_ref, sv_ref=sv_ref):
            for d in range(t_rows // BK):
                step(d * BK, sk_ref, sv_ref)

        @pl.when(origin == own)
        def _(sk_ref=sk_ref, sv_ref=sv_ref):
            for d in range(t_rows // BK):
                step(d * BK, sk_ref, sv_ref, causal=True)

    if last:
        (o_ref,) = o_refs
        out = acc_ref[...] / jnp.sum(l_ref[...], axis=1, keepdims=True)
        for g in range(group):
            o_ref[:, g * HD:(g + 1) * HD] = out[g * t_rows:(g + 1) * t_rows].astype(o_ref.dtype)
    else:
        o_refs[0][...] = m_ref[...]
        o_refs[1][...] = l_ref[...]
        o_refs[2][...] = acc_ref[...]


def attn_call(sc, q, insts, rows, state, first, last):
    t_rows, q_width = q.shape
    kv_width = insts[0][0].shape[2]
    kv_local = kv_width // HD
    group = q_width // kv_width
    c_rows, s_rows = rows
    rows_all = group * t_rows
    ninst = len(insts)
    kernel = functools.partial(step_kernel, ninst=ninst, t_rows=t_rows, group=group, first=first, last=last)
    st_spec = pl.BlockSpec((rows_all, 128), lambda k, *_: (k, 0))
    st_shape = jax.ShapeDtypeStruct((kv_local * rows_all, 128), jnp.float32)
    in_specs = [pl.BlockSpec((t_rows, group * HD), lambda k, *_: (0, k))]
    args = [sc, q]
    for cache, span, srow in insts:
        in_specs += [
            pl.BlockSpec((None, c_rows, HD), lambda k, *_: (0, 0, k)),
            pl.BlockSpec((None, c_rows, HD), lambda k, *_: (1, 0, k)),
            pl.BlockSpec((None, s_rows, HD), lambda k, *_, srow=srow: (0, srow, k)),
            pl.BlockSpec((None, s_rows, HD), lambda k, *_, srow=srow: (1, srow, k)),
        ]
        args += [cache, cache, span, span]
    if not first:
        in_specs += [st_spec] * 3
        args += list(state)
    if last:
        out_specs = pl.BlockSpec((t_rows, group * HD), lambda k, *_: (0, k))
        out_shape = jax.ShapeDtypeStruct((t_rows, q_width), q.dtype)
    else:
        out_specs = [st_spec] * 3
        out_shape = [st_shape] * 3
    keys = ninst * (c_rows + s_rows)
    heads = kv_local * group
    cost = pl.CostEstimate(
        flops=4 * heads * t_rows * keys * HD,
        transcendentals=heads * t_rows * keys,
        bytes_accessed=2 * t_rows * q_width + 4 * keys * kv_width + 24 * kv_local * rows_all * 128,
    )
    grid_spec = pltpu.PrefetchScalarGridSpec(
        num_scalar_prefetch=1,
        grid=(kv_local,),
        in_specs=in_specs,
        out_specs=out_specs,
        scratch_shapes=[
            pltpu.VMEM((rows_all, HD), q.dtype),
            pltpu.VMEM((rows_all, 128), jnp.float32),
            pltpu.VMEM((rows_all, 128), jnp.float32),
            pltpu.VMEM((rows_all, HD), jnp.float32),
        ],
    )
    return pl.pallas_call(
        kernel,
        out_shape=out_shape,
        grid_spec=grid_spec,
        compiler_params=pltpu.CompilerParams(dimension_semantics=("arbitrary",)),
        cost_estimate=cost,
    )(*args)


def chain_need(n, first_pairs, hops):
    need = []
    for k in range(len(hops)):
        keep = []
        for src in range(n):
            origin = first_pairs[src]
            dst = src
            for j in range(k + 1):
                dst = hops[j](dst)
            later = [dst, dst ^ 1]
            d = dst
            for j in range(k + 1, len(hops)):
                d = hops[j](d)
                later += [d, d ^ 1]
            if any(x > origin for x in later):
                keep.append(src)
        need.append(keep)
    return need


def body(query_rows, span_kv, cache_kv, cache_len):
    n = lax.psum(1, "seq")
    own = lax.axis_index("seq").astype(jnp.int32)
    n_chips = n // 2
    c_rows = cache_kv.shape[1]
    s_rows = span_kv.shape[1]
    kv_width = cache_kv.shape[2]
    length = cache_len.reshape(())
    tag = jnp.zeros((2, 16, kv_width), cache_kv.dtype)
    tag = tag.at[0, 0, 0].set((length // 64).astype(cache_kv.dtype))
    tag = tag.at[0, 0, 1].set((length % 64).astype(cache_kv.dtype))
    merged = jnp.concatenate([cache_kv, span_kv, tag], axis=1)
    srow = c_rows // s_rows

    def send(x, fn):
        return lax.ppermute(x, "seq", [(i, fn(i)) for i in range(n)])

    def length_of(blk):
        hi = blk[0, c_rows + s_rows, 0].astype(jnp.int32)
        lo = blk[0, c_rows + s_rows, 1].astype(jnp.int32)
        return hi * 64 + lo

    calls = [0]

    def run(phase, state):
        lens = [jnp.asarray(ln, jnp.int32).reshape(1) for _, ln, _ in phase]
        origins = [jnp.asarray(o, jnp.int32).reshape(1) for _, _, o in phase]
        sc = jnp.concatenate(lens + origins + [own.reshape(1)]).astype(jnp.int32)
        insts = [b for b, _, _ in phase]
        first = calls[0] == 0
        calls[0] += 1
        return attn_call(sc, query_rows, insts, (c_rows, s_rows), state, first=first, last=(calls[0] == n_chips))

    part = send(merged, lambda i: i ^ 1)
    k_right = n_chips // 2
    k_left = n_chips - 1 - k_right
    hops = []
    for sign, count in ((2, k_right), (-2, k_left)):
        blk = merged
        for k in range(1, count + 1):
            blk = send(blk, lambda i, sign=sign: (i + sign) % n)
            hops.append((blk, sign, k))
    state = run([((cache_kv, span_kv, 0), length, own), ((part, part, srow), length_of(part), own ^ 1)], None)
    for blk, sign, k in hops:
        state, blk = lax.optimization_barrier((state, blk))
        origin = (own - sign * k) % n
        fwd = send(blk, lambda i: i ^ 1)
        state = run([((blk, blk, srow), length_of(blk), origin), ((fwd, fwd, srow), length_of(fwd), origin ^ 1)], state)
    return state


def solution(mesh):
    in_specs = (
        P(("rep", "seq"), "head"),
        P(None, ("rep", "seq"), "head"),
        P(None, ("rep", "seq"), "head"),
        P(("rep", "seq")),
    )
    out_specs = P(("rep", "seq"), "head")
    return jax.shard_map(body, mesh=mesh, in_specs=in_specs, out_specs=out_specs, check_vma=False)
```

```python
import functools

import jax
import jax.numpy as jnp
from jax import lax
from jax.experimental import pallas as pl
from jax.experimental.pallas import tpu as pltpu
from jax.sharding import PartitionSpec as P

HD = 128
NEG = -1e30
BK = 256


def step_kernel(sc_ref, q_ref, *refs, ninst, t_rows, group, first, last):
    inst_refs = [refs[4 * i:4 * i + 4] for i in range(ninst)]
    rest = refs[4 * ninst:]
    if first:
        state_in = None
    else:
        state_in, rest = rest[:3], rest[3:]
    qs_ref, m_ref, l_ref, acc_ref = rest[-4:]
    o_refs = rest[:-4]
    own = sc_ref[2 * ninst]
    scale = HD ** (-0.5) * 1.4426950408889634
    rows_all = group * t_rows
    reps = BK // 128
    for g in range(group):
        qs_ref[g * t_rows:(g + 1) * t_rows, :] = q_ref[:, g * HD:(g + 1) * HD]
    if first:
        m_ref[...] = jnp.full(m_ref.shape, NEG, jnp.float32)
        l_ref[...] = jnp.zeros(l_ref.shape, jnp.float32)
        acc_ref[...] = jnp.zeros(acc_ref.shape, jnp.float32)
    else:
        m_ref[...] = state_in[0][...]
        l_ref[...] = state_in[1][...]
        acc_ref[...] = state_in[2][...]

    def step(start, k_ref, v_ref, limit=None, causal=False):
        k = k_ref[pl.ds(start, BK), :]
        v = v_ref[pl.ds(start, BK), :]
        s = lax.dot_general(qs_ref[...], k, (((1,), (1,)), ((), ())), preferred_element_type=jnp.float32) * scale
        if limit is not None:
            mask = lax.broadcasted_iota(jnp.int32, (rows_all, BK), 1) < limit
            s = jnp.where(mask, s, NEG)
        if causal:
            cols = lax.broadcasted_iota(jnp.int32, (t_rows, BK), 1) + start
            rows = lax.broadcasted_iota(jnp.int32, (t_rows, BK), 0)
            mask = jnp.concatenate([cols <= rows] * group, axis=0)
            s = jnp.where(mask, s, NEG)
        m_prev = m_ref[...]
        m_new = jnp.maximum(m_prev, jnp.max(s, axis=1, keepdims=True))
        alpha = jnp.exp2(m_prev - m_new)
        m_wide = m_new if reps == 1 else jnp.concatenate([m_new] * reps, axis=1)
        p = jnp.exp2(s - m_wide)
        p_sum = p[:, :128]
        for r in range(1, reps):
            p_sum = p_sum + p[:, r * 128:(r + 1) * 128]
        l_ref[...] = alpha * l_ref[...] + p_sum
        acc_ref[...] = alpha * acc_ref[...] + jnp.dot(p.astype(v.dtype), v, preferred_element_type=jnp.float32)
        m_ref[...] = m_new

    for i, (ck_ref, cv_ref, sk_ref, sv_ref) in enumerate(inst_refs):
        length = sc_ref[i]
        origin = sc_ref[ninst + i]
        n_full = length // BK
        rem = length - n_full * BK

        def loop_body(b, c, ck_ref=ck_ref, cv_ref=cv_ref):
            step(pl.multiple_of(b * BK, BK), ck_ref, cv_ref)
            return c

        lax.fori_loop(0, n_full, loop_body, 0)

        @pl.when(rem > 0)
        def _(ck_ref=ck_ref, cv_ref=cv_ref, n_full=n_full, rem=rem):
            step(pl.multiple_of(n_full * BK, BK), ck_ref, cv_ref, limit=rem)

        @pl.when(origin < own)
        def _(sk_ref=sk_ref, sv_ref=sv_ref):
            for d in range(t_rows // BK):
                step(d * BK, sk_ref, sv_ref)

        @pl.when(origin == own)
        def _(sk_ref=sk_ref, sv_ref=sv_ref):
            for d in range(t_rows // BK):
                step(d * BK, sk_ref, sv_ref, causal=True)

    if last:
        (o_ref,) = o_refs
        out = acc_ref[...] / jnp.sum(l_ref[...], axis=1, keepdims=True)
        for g in range(group):
            o_ref[:, g * HD:(g + 1) * HD] = out[g * t_rows:(g + 1) * t_rows].astype(o_ref.dtype)
    else:
        o_refs[0][...] = m_ref[...]
        o_refs[1][...] = l_ref[...]
        o_refs[2][...] = acc_ref[...]


def attn_call(sc, q, insts, rows, state, first, last):
    t_rows, q_width = q.shape
    kv_width = insts[0][0].shape[2]
    kv_local = kv_width // HD
    group = q_width // kv_width
    c_rows, s_rows = rows
    rows_all = group * t_rows
    ninst = len(insts)
    kernel = functools.partial(step_kernel, ninst=ninst, t_rows=t_rows, group=group, first=first, last=last)
    st_spec = pl.BlockSpec((rows_all, 128), lambda k, *_: (k, 0))
    st_shape = jax.ShapeDtypeStruct((kv_local * rows_all, 128), jnp.float32)
    in_specs = [pl.BlockSpec((t_rows, group * HD), lambda k, *_: (0, k))]
    args = [sc, q]
    for cache, span, srow in insts:
        in_specs += [
            pl.BlockSpec((None, c_rows, HD), lambda k, *_: (0, 0, k)),
            pl.BlockSpec((None, c_rows, HD), lambda k, *_: (1, 0, k)),
            pl.BlockSpec((None, s_rows, HD), lambda k, *_, srow=srow: (0, srow, k)),
            pl.BlockSpec((None, s_rows, HD), lambda k, *_, srow=srow: (1, srow, k)),
        ]
        args += [cache, cache, span, span]
    if not first:
        in_specs += [st_spec] * 3
        args += list(state)
    if last:
        out_specs = pl.BlockSpec((t_rows, group * HD), lambda k, *_: (0, k))
        out_shape = jax.ShapeDtypeStruct((t_rows, q_width), q.dtype)
    else:
        out_specs = [st_spec] * 3
        out_shape = [st_shape] * 3
    keys = ninst * (c_rows + s_rows)
    heads = kv_local * group
    cost = pl.CostEstimate(
        flops=4 * heads * t_rows * keys * HD,
        transcendentals=heads * t_rows * keys,
        bytes_accessed=2 * t_rows * q_width + 4 * keys * kv_width + 24 * kv_local * rows_all * 128,
    )
    grid_spec = pltpu.PrefetchScalarGridSpec(
        num_scalar_prefetch=1,
        grid=(kv_local,),
        in_specs=in_specs,
        out_specs=out_specs,
        scratch_shapes=[
            pltpu.VMEM((rows_all, HD), q.dtype),
            pltpu.VMEM((rows_all, 128), jnp.float32),
            pltpu.VMEM((rows_all, 128), jnp.float32),
            pltpu.VMEM((rows_all, HD), jnp.float32),
        ],
    )
    return pl.pallas_call(
        kernel,
        out_shape=out_shape,
        grid_spec=grid_spec,
        compiler_params=pltpu.CompilerParams(dimension_semantics=("arbitrary",)),
        cost_estimate=cost,
    )(*args)


def chain_need(n, first_pairs, hops):
    need = []
    for k in range(len(hops)):
        keep = []
        for src in range(n):
            origin = first_pairs[src]
            dst = src
            for j in range(k + 1):
                dst = hops[j](dst)
            later = [dst, dst ^ 1]
            d = dst
            for j in range(k + 1, len(hops)):
                d = hops[j](d)
                later += [d, d ^ 1]
            if any(x > origin for x in later):
                keep.append(src)
        need.append(keep)
    return need


def body(query_rows, span_kv, cache_kv, cache_len):
    n = lax.psum(1, "seq")
    own = lax.axis_index("seq").astype(jnp.int32)
    n_chips = n // 2
    c_rows = cache_kv.shape[1]
    s_rows = span_kv.shape[1]
    kv_width = cache_kv.shape[2]
    length = cache_len.reshape(())
    tag = jnp.zeros((2, 16, kv_width), cache_kv.dtype)
    tag = tag.at[0, 0, 0].set((length // 64).astype(cache_kv.dtype))
    tag = tag.at[0, 0, 1].set((length % 64).astype(cache_kv.dtype))
    merged = jnp.concatenate([cache_kv, span_kv, tag], axis=1)
    srow = c_rows // s_rows

    def send(x, fn):
        return lax.ppermute(x, "seq", [(i, fn(i)) for i in range(n)])

    def length_of(blk):
        hi = blk[0, c_rows + s_rows, 0].astype(jnp.int32)
        lo = blk[0, c_rows + s_rows, 1].astype(jnp.int32)
        return hi * 64 + lo

    calls = [0]

    def run(phase, state):
        lens = [jnp.asarray(ln, jnp.int32).reshape(1) for _, ln, _ in phase]
        origins = [jnp.asarray(o, jnp.int32).reshape(1) for _, _, o in phase]
        sc = jnp.concatenate(lens + origins + [own.reshape(1)]).astype(jnp.int32)
        insts = [b for b, _, _ in phase]
        first = calls[0] == 0
        calls[0] += 1
        return attn_call(sc, query_rows, insts, (c_rows, s_rows), state, first=first, last=(calls[0] == n_chips))

    part = send(merged, lambda i: i ^ 1)
    k_right = n_chips // 2
    k_left = n_chips - 1 - k_right
    hops = []
    for sign, count in ((2, k_right), (-2, k_left)):
        blk = merged
        for k in range(1, count + 1):
            blk = send(blk, lambda i, sign=sign: (i + sign) % n)
            hops.append((blk, sign, k))
    state = run([((cache_kv, span_kv, 0), length, own), ((part, part, srow), length_of(part), own ^ 1)], None)
    for blk, sign, k in hops:
        state, blk = lax.optimization_barrier((state, blk))
        origin = (own - sign * k) % n
        fwd = send(blk, lambda i: i ^ 1)
        state = run([((blk, blk, srow), length_of(blk), origin), ((fwd, fwd, srow), length_of(fwd), origin ^ 1)], state)
    return state


def solution(mesh):
    in_specs = (
        P(("rep", "seq"), "head"),
        P(None, ("rep", "seq"), "head"),
        P(None, ("rep", "seq"), "head"),
        P(("rep", "seq")),
    )
    out_specs = P(("rep", "seq"), "head")
    return jax.shard_map(body, mesh=mesh, in_specs=in_specs, out_specs=out_specs, check_vma=False)
```

```python
import functools

import jax
import jax.numpy as jnp
from jax import lax
from jax.experimental import pallas as pl
from jax.experimental.pallas import tpu as pltpu
from jax.sharding import PartitionSpec as P

HD = 128
NEG = -1e30
BK = 256


def step_kernel(sc_ref, q_ref, *refs, ninst, t_rows, group, first, last):
    inst_refs = [refs[4 * i:4 * i + 4] for i in range(ninst)]
    rest = refs[4 * ninst:]
    if first:
        state_in = None
    else:
        state_in, rest = rest[:3], rest[3:]
    qs_ref, m_ref, l_ref, acc_ref = rest[-4:]
    o_refs = rest[:-4]
    own = sc_ref[2 * ninst]
    scale = HD ** (-0.5) * 1.4426950408889634
    rows_all = group * t_rows
    reps = BK // 128
    for g in range(group):
        qs_ref[g * t_rows:(g + 1) * t_rows, :] = q_ref[:, g * HD:(g + 1) * HD]
    if first:
        m_ref[...] = jnp.full(m_ref.shape, NEG, jnp.float32)
        l_ref[...] = jnp.zeros(l_ref.shape, jnp.float32)
        acc_ref[...] = jnp.zeros(acc_ref.shape, jnp.float32)
    else:
        m_ref[...] = state_in[0][...]
        l_ref[...] = state_in[1][...]
        acc_ref[...] = state_in[2][...]

    def step(start, k_ref, v_ref, limit=None, causal=False):
        k = k_ref[pl.ds(start, BK), :]
        v = v_ref[pl.ds(start, BK), :]
        s = lax.dot_general(qs_ref[...], k, (((1,), (1,)), ((), ())), preferred_element_type=jnp.float32) * scale
        if limit is not None:
            mask = lax.broadcasted_iota(jnp.int32, (rows_all, BK), 1) < limit
            s = jnp.where(mask, s, NEG)
        if causal:
            cols = lax.broadcasted_iota(jnp.int32, (t_rows, BK), 1) + start
            rows = lax.broadcasted_iota(jnp.int32, (t_rows, BK), 0)
            mask = jnp.concatenate([cols <= rows] * group, axis=0)
            s = jnp.where(mask, s, NEG)
        m_prev = m_ref[...]
        m_new = jnp.maximum(m_prev, jnp.max(s, axis=1, keepdims=True))
        alpha = jnp.exp2(m_prev - m_new)
        m_wide = m_new if reps == 1 else jnp.concatenate([m_new] * reps, axis=1)
        p = jnp.exp2(s - m_wide)
        p_sum = p[:, :128]
        for r in range(1, reps):
            p_sum = p_sum + p[:, r * 128:(r + 1) * 128]
        l_ref[...] = alpha * l_ref[...] + p_sum
        acc_ref[...] = alpha * acc_ref[...] + jnp.dot(p.astype(v.dtype), v, preferred_element_type=jnp.float32)
        m_ref[...] = m_new

    for i, (ck_ref, cv_ref, sk_ref, sv_ref) in enumerate(inst_refs):
        length = sc_ref[i]
        origin = sc_ref[ninst + i]
        n_full = length // BK
        rem = length - n_full * BK

        def loop_body(b, c, ck_ref=ck_ref, cv_ref=cv_ref):
            step(pl.multiple_of(b * BK, BK), ck_ref, cv_ref)
            return c

        lax.fori_loop(0, n_full, loop_body, 0)

        @pl.when(rem > 0)
        def _(ck_ref=ck_ref, cv_ref=cv_ref, n_full=n_full, rem=rem):
            step(pl.multiple_of(n_full * BK, BK), ck_ref, cv_ref, limit=rem)

        @pl.when(origin < own)
        def _(sk_ref=sk_ref, sv_ref=sv_ref):
            for d in range(t_rows // BK):
                step(d * BK, sk_ref, sv_ref)

        @pl.when(origin == own)
        def _(sk_ref=sk_ref, sv_ref=sv_ref):
            for d in range(t_rows // BK):
                step(d * BK, sk_ref, sv_ref, causal=True)

    if last:
        (o_ref,) = o_refs
        out = acc_ref[...] / jnp.sum(l_ref[...], axis=1, keepdims=True)
        for g in range(group):
            o_ref[:, g * HD:(g + 1) * HD] = out[g * t_rows:(g + 1) * t_rows].astype(o_ref.dtype)
    else:
        o_refs[0][...] = m_ref[...]
        o_refs[1][...] = l_ref[...]
        o_refs[2][...] = acc_ref[...]


def attn_call(sc, q, insts, rows, state, first, last):
    t_rows, q_width = q.shape
    kv_width = insts[0][0].shape[2]
    kv_local = kv_width // HD
    group = q_width // kv_width
    c_rows, s_rows = rows
    rows_all = group * t_rows
    ninst = len(insts)
    kernel = functools.partial(step_kernel, ninst=ninst, t_rows=t_rows, group=group, first=first, last=last)
    st_spec = pl.BlockSpec((rows_all, 128), lambda k, *_: (k, 0))
    st_shape = jax.ShapeDtypeStruct((kv_local * rows_all, 128), jnp.float32)
    in_specs = [pl.BlockSpec((t_rows, group * HD), lambda k, *_: (0, k))]
    args = [sc, q]
    for cache, span, srow in insts:
        in_specs += [
            pl.BlockSpec((None, c_rows, HD), lambda k, *_: (0, 0, k)),
            pl.BlockSpec((None, c_rows, HD), lambda k, *_: (1, 0, k)),
            pl.BlockSpec((None, s_rows, HD), lambda k, *_, srow=srow: (0, srow, k)),
            pl.BlockSpec((None, s_rows, HD), lambda k, *_, srow=srow: (1, srow, k)),
        ]
        args += [cache, cache, span, span]
    if not first:
        in_specs += [st_spec] * 3
        args += list(state)
    if last:
        out_specs = pl.BlockSpec((t_rows, group * HD), lambda k, *_: (0, k))
        out_shape = jax.ShapeDtypeStruct((t_rows, q_width), q.dtype)
    else:
        out_specs = [st_spec] * 3
        out_shape = [st_shape] * 3
    keys = ninst * (c_rows + s_rows)
    heads = kv_local * group
    cost = pl.CostEstimate(
        flops=4 * heads * t_rows * keys * HD,
        transcendentals=heads * t_rows * keys,
        bytes_accessed=2 * t_rows * q_width + 4 * keys * kv_width + 24 * kv_local * rows_all * 128,
    )
    grid_spec = pltpu.PrefetchScalarGridSpec(
        num_scalar_prefetch=1,
        grid=(kv_local,),
        in_specs=in_specs,
        out_specs=out_specs,
        scratch_shapes=[
            pltpu.VMEM((rows_all, HD), q.dtype),
            pltpu.VMEM((rows_all, 128), jnp.float32),
            pltpu.VMEM((rows_all, 128), jnp.float32),
            pltpu.VMEM((rows_all, HD), jnp.float32),
        ],
    )
    return pl.pallas_call(
        kernel,
        out_shape=out_shape,
        grid_spec=grid_spec,
        compiler_params=pltpu.CompilerParams(dimension_semantics=("arbitrary",)),
        cost_estimate=cost,
    )(*args)


def chain_need(n, first_pairs, hops):
    need = []
    for k in range(len(hops)):
        keep = []
        for src in range(n):
            origin = first_pairs[src]
            dst = src
            for j in range(k + 1):
                dst = hops[j](dst)
            later = [dst, dst ^ 1]
            d = dst
            for j in range(k + 1, len(hops)):
                d = hops[j](d)
                later += [d, d ^ 1]
            if any(x > origin for x in later):
                keep.append(src)
        need.append(keep)
    return need


def body(query_rows, span_kv, cache_kv, cache_len):
    n = lax.psum(1, "seq")
    own = lax.axis_index("seq").astype(jnp.int32)
    n_chips = n // 2
    c_rows = cache_kv.shape[1]
    s_rows = span_kv.shape[1]
    kv_width = cache_kv.shape[2]
    length = cache_len.reshape(())
    tag = jnp.zeros((2, 16, kv_width), cache_kv.dtype)
    tag = tag.at[0, 0, 0].set((length // 64).astype(cache_kv.dtype))
    tag = tag.at[0, 0, 1].set((length % 64).astype(cache_kv.dtype))
    merged = jnp.concatenate([cache_kv, span_kv, tag], axis=1)
    srow = c_rows // s_rows

    def send(x, fn):
        return lax.ppermute(x, "seq", [(i, fn(i)) for i in range(n)])

    def length_of(blk):
        hi = blk[0, c_rows + s_rows, 0].astype(jnp.int32)
        lo = blk[0, c_rows + s_rows, 1].astype(jnp.int32)
        return hi * 64 + lo

    calls = [0]

    def run(phase, state):
        lens = [jnp.asarray(ln, jnp.int32).reshape(1) for _, ln, _ in phase]
        origins = [jnp.asarray(o, jnp.int32).reshape(1) for _, _, o in phase]
        sc = jnp.concatenate(lens + origins + [own.reshape(1)]).astype(jnp.int32)
        insts = [b for b, _, _ in phase]
        first = calls[0] == 0
        calls[0] += 1
        return attn_call(sc, query_rows, insts, (c_rows, s_rows), state, first=first, last=(calls[0] == 2 * n_chips - 1))

    part = send(merged, lambda i: i ^ 1)
    k_right = n_chips // 2
    k_left = n_chips - 1 - k_right
    hops = []
    for sign, count in ((2, k_right), (-2, k_left)):
        blk = merged
        for k in range(1, count + 1):
            blk = send(blk, lambda i, sign=sign: (i + sign) % n)
            hops.append((blk, sign, k))
    state = run([((cache_kv, span_kv, 0), length, own), ((part, part, srow), length_of(part), own ^ 1)], None)
    for blk, sign, k in hops:
        state, blk = lax.optimization_barrier((state, blk))
        origin = (own - sign * k) % n
        fwd = send(blk, lambda i: i ^ 1)
        state = run([((blk, blk, srow), length_of(blk), origin)], state)
        state, fwd = lax.optimization_barrier((state, fwd))
        state = run([((fwd, fwd, srow), length_of(fwd), origin ^ 1)], state)
    return state


def solution(mesh):
    in_specs = (
        P(("rep", "seq"), "head"),
        P(None, ("rep", "seq"), "head"),
        P(None, ("rep", "seq"), "head"),
        P(("rep", "seq")),
    )
    out_specs = P(("rep", "seq"), "head")
    return jax.shard_map(body, mesh=mesh, in_specs=in_specs, out_specs=out_specs, check_vma=False)
```

```python
import functools

import jax
import jax.numpy as jnp
from jax import lax
from jax.experimental import pallas as pl
from jax.experimental.pallas import tpu as pltpu
from jax.sharding import PartitionSpec as P

HD = 128
NEG = -1e30
BK = 256


def step_kernel(sc_ref, q_ref, *refs, kinds, t_rows, group, first, last):
    ninst = len(kinds)
    inst_refs = []
    pos = 0
    for has_cache, has_span in kinds:
        c = refs[pos:pos + 2] if has_cache else None
        pos += 2 if has_cache else 0
        sp = refs[pos:pos + 2] if has_span else None
        pos += 2 if has_span else 0
        inst_refs.append((c, sp))
    rest = refs[pos:]
    if first:
        state_in = None
    else:
        state_in, rest = rest[:3], rest[3:]
    qs_ref, m_ref, l_ref, acc_ref = rest[-4:]
    o_refs = rest[:-4]
    own = sc_ref[2 * ninst]
    scale = HD ** (-0.5) * 1.4426950408889634
    rows_all = group * t_rows
    reps = BK // 128
    for g in range(group):
        qs_ref[g * t_rows:(g + 1) * t_rows, :] = q_ref[:, g * HD:(g + 1) * HD]
    if first:
        m_ref[...] = jnp.full(m_ref.shape, NEG, jnp.float32)
        l_ref[...] = jnp.zeros(l_ref.shape, jnp.float32)
        acc_ref[...] = jnp.zeros(acc_ref.shape, jnp.float32)
    else:
        m_ref[...] = state_in[0][...]
        l_ref[...] = state_in[1][...]
        acc_ref[...] = state_in[2][...]

    def step(start, k_ref, v_ref, limit=None, causal=False):
        k = k_ref[pl.ds(start, BK), :]
        v = v_ref[pl.ds(start, BK), :]
        s = lax.dot_general(qs_ref[...], k, (((1,), (1,)), ((), ())), preferred_element_type=jnp.float32) * scale
        if limit is not None:
            mask = lax.broadcasted_iota(jnp.int32, (rows_all, BK), 1) < limit
            s = jnp.where(mask, s, NEG)
        if causal:
            cols = lax.broadcasted_iota(jnp.int32, (t_rows, BK), 1) + start
            rows = lax.broadcasted_iota(jnp.int32, (t_rows, BK), 0)
            mask = jnp.concatenate([cols <= rows] * group, axis=0)
            s = jnp.where(mask, s, NEG)
        m_prev = m_ref[...]
        m_new = jnp.maximum(m_prev, jnp.max(s, axis=1, keepdims=True))
        alpha = jnp.exp2(m_prev - m_new)
        m_wide = m_new if reps == 1 else jnp.concatenate([m_new] * reps, axis=1)
        p = jnp.exp2(s - m_wide)
        p_sum = p[:, :128]
        for r in range(1, reps):
            p_sum = p_sum + p[:, r * 128:(r + 1) * 128]
        l_ref[...] = alpha * l_ref[...] + p_sum
        acc_ref[...] = alpha * acc_ref[...] + jnp.dot(p.astype(v.dtype), v, preferred_element_type=jnp.float32)
        m_ref[...] = m_new

    for i, (c_refs, s_refs) in enumerate(inst_refs):
        length = sc_ref[i]
        origin = sc_ref[ninst + i]
        if c_refs is not None:
            ck_ref, cv_ref = c_refs
            n_full = length // BK
            rem = length - n_full * BK

            def loop_body(b, c, ck_ref=ck_ref, cv_ref=cv_ref):
                step(pl.multiple_of(b * BK, BK), ck_ref, cv_ref)
                return c

            lax.fori_loop(0, n_full, loop_body, 0)

            @pl.when(rem > 0)
            def _(ck_ref=ck_ref, cv_ref=cv_ref, n_full=n_full, rem=rem):
                step(pl.multiple_of(n_full * BK, BK), ck_ref, cv_ref, limit=rem)

        if s_refs is not None:
            sk_ref, sv_ref = s_refs
            @pl.when(origin < own)
            def _(sk_ref=sk_ref, sv_ref=sv_ref):
                for d in range(t_rows // BK):
                    step(d * BK, sk_ref, sv_ref)

            @pl.when(origin == own)
            def _(sk_ref=sk_ref, sv_ref=sv_ref):
                for d in range(t_rows // BK):
                    step(d * BK, sk_ref, sv_ref, causal=True)

    if last:
        (o_ref,) = o_refs
        out = acc_ref[...] / jnp.sum(l_ref[...], axis=1, keepdims=True)
        for g in range(group):
            o_ref[:, g * HD:(g + 1) * HD] = out[g * t_rows:(g + 1) * t_rows].astype(o_ref.dtype)
    else:
        o_refs[0][...] = m_ref[...]
        o_refs[1][...] = l_ref[...]
        o_refs[2][...] = acc_ref[...]


def attn_call(sc, q, insts, rows, state, first, last):
    kinds = tuple((c is not None, sp is not None) for c, sp, _ in insts)
    t_rows, q_width = q.shape
    kv_width = next(c if c is not None else sp for c, sp, _ in insts).shape[2]
    kv_local = kv_width // HD
    group = q_width // kv_width
    c_rows, s_rows = rows
    rows_all = group * t_rows
    ninst = len(insts)
    kernel = functools.partial(step_kernel, kinds=kinds, t_rows=t_rows, group=group, first=first, last=last)
    st_spec = pl.BlockSpec((rows_all, 128), lambda k, *_: (k, 0))
    st_shape = jax.ShapeDtypeStruct((kv_local * rows_all, 128), jnp.float32)
    in_specs = [pl.BlockSpec((t_rows, group * HD), lambda k, *_: (0, k))]
    args = [sc, q]
    for cache, span, srow in insts:
        if cache is not None:
            in_specs += [
                pl.BlockSpec((None, c_rows, HD), lambda k, *_: (0, 0, k)),
                pl.BlockSpec((None, c_rows, HD), lambda k, *_: (1, 0, k)),
            ]
            args += [cache, cache]
        if span is not None:
            in_specs += [
                pl.BlockSpec((None, s_rows, HD), lambda k, *_, srow=srow: (0, srow, k)),
                pl.BlockSpec((None, s_rows, HD), lambda k, *_, srow=srow: (1, srow, k)),
            ]
            args += [span, span]
    if not first:
        in_specs += [st_spec] * 3
        args += list(state)
    if last:
        out_specs = pl.BlockSpec((t_rows, group * HD), lambda k, *_: (0, k))
        out_shape = jax.ShapeDtypeStruct((t_rows, q_width), q.dtype)
    else:
        out_specs = [st_spec] * 3
        out_shape = [st_shape] * 3
    keys = sum(c_rows * kc + s_rows * ks for kc, ks in kinds)
    heads = kv_local * group
    cost = pl.CostEstimate(
        flops=4 * heads * t_rows * keys * HD,
        transcendentals=heads * t_rows * keys,
        bytes_accessed=2 * t_rows * q_width + 4 * keys * kv_width + 24 * kv_local * rows_all * 128,
    )
    grid_spec = pltpu.PrefetchScalarGridSpec(
        num_scalar_prefetch=1,
        grid=(kv_local,),
        in_specs=in_specs,
        out_specs=out_specs,
        scratch_shapes=[
            pltpu.VMEM((rows_all, HD), q.dtype),
            pltpu.VMEM((rows_all, 128), jnp.float32),
            pltpu.VMEM((rows_all, 128), jnp.float32),
            pltpu.VMEM((rows_all, HD), jnp.float32),
        ],
    )
    return pl.pallas_call(
        kernel,
        out_shape=out_shape,
        grid_spec=grid_spec,
        compiler_params=pltpu.CompilerParams(dimension_semantics=("arbitrary",)),
        cost_estimate=cost,
    )(*args)


def chain_need(n, first_pairs, hops):
    need = []
    for k in range(len(hops)):
        keep = []
        for src in range(n):
            origin = first_pairs[src]
            dst = src
            for j in range(k + 1):
                dst = hops[j](dst)
            later = [dst, dst ^ 1]
            d = dst
            for j in range(k + 1, len(hops)):
                d = hops[j](d)
                later += [d, d ^ 1]
            if any(x > origin for x in later):
                keep.append(src)
        need.append(keep)
    return need


def body(query_rows, span_kv, cache_kv, cache_len):
    n = lax.psum(1, "seq")
    own = lax.axis_index("seq").astype(jnp.int32)
    n_chips = n // 2
    c_rows = cache_kv.shape[1]
    s_rows = span_kv.shape[1]
    kv_width = cache_kv.shape[2]
    length = cache_len.reshape(())
    tag = jnp.zeros((2, 16, kv_width), cache_kv.dtype)
    tag = tag.at[0, 0, 0].set((length // 64).astype(cache_kv.dtype))
    tag = tag.at[0, 0, 1].set((length % 64).astype(cache_kv.dtype))
    merged = jnp.concatenate([cache_kv, span_kv, tag], axis=1)
    srow = c_rows // s_rows

    def send(x, fn, keep=None):
        return lax.ppermute(x, "seq", [(i, fn(i)) for i in range(n) if keep is None or i in keep])

    def length_of(blk, row):
        hi = blk[0, row, 0].astype(jnp.int32)
        lo = blk[0, row, 1].astype(jnp.int32)
        return hi * 64 + lo

    calls = [0]
    n_calls = n_chips

    def run(phase, state):
        lens = [jnp.asarray(ln, jnp.int32).reshape(1) for _, ln, _ in phase]
        origins = [jnp.asarray(o, jnp.int32).reshape(1) for _, _, o in phase]
        sc = jnp.concatenate(lens + origins + [own.reshape(1)]).astype(jnp.int32)
        insts = [b for b, _, _ in phase]
        first = calls[0] == 0
        calls[0] += 1
        return attn_call(sc, query_rows, insts, (c_rows, s_rows), state, first=first, last=(calls[0] == n_calls))

    part = send(merged, lambda i: i ^ 1)
    k_right = n_chips // 2
    k_left = n_chips - 1 - k_right
    hops = []
    early = []
    for sign, count in ((2, k_right), (-2, k_left)):
        c_blk = jnp.concatenate([cache_kv, tag], axis=1)
        s_blk = span_kv
        for k in range(1, count + 1):
            def hop(i, sign=sign):
                return (i + sign) % n
            keep = []
            for i in range(n):
                o = (i - sign * (k - 1)) % n
                d = i
                ok = False
                for j in range(k, count + 1):
                    d = (d + sign) % n
                    if d > o or (d ^ 1) > o:
                        ok = True
                if ok:
                    keep.append(i)
            s_blk = send(s_blk, hop, keep)
            if k == 1:
                s_blk, c_blk = lax.optimization_barrier((s_blk, c_blk))
            c_blk = send(c_blk, hop)
            hops.append((c_blk, s_blk, sign, k))
    phase0 = [((cache_kv, span_kv, 0), length, own), ((part, part, srow), length_of(part, c_rows + s_rows), own ^ 1)]
    later = []
    for c_blk, s_blk, sign, k in hops:
        origin = (own - sign * k) % n
        fwd_keep = [i for i in range(n) if (i ^ 1) > (i - sign * k) % n]
        if k == 1:
            s_fwd = send(s_blk, lambda i: i ^ 1, fwd_keep)
            phase0 += [((None, s_blk, 0), 0, origin), ((None, s_fwd, 0), 0, origin ^ 1)]
            later.append((c_blk, None, None, sign, k))
        else:
            later.append((c_blk, s_blk, fwd_keep, sign, k))
    state = run(phase0, None)
    for c_blk, s_blk, fwd_keep, sign, k in later:
        if s_blk is None:
            state, c_blk = lax.optimization_barrier((state, c_blk))
        else:
            state, c_blk, s_blk = lax.optimization_barrier((state, c_blk, s_blk))
        origin = (own - sign * k) % n
        c_fwd = send(c_blk, lambda i: i ^ 1)
        ph = [((c_blk, None, 0), length_of(c_blk, c_rows), origin), ((c_fwd, None, 0), length_of(c_fwd, c_rows), origin ^ 1)]
        if s_blk is not None:
            s_fwd = send(s_blk, lambda i: i ^ 1, fwd_keep)
            ph += [((None, s_blk, 0), 0, origin), ((None, s_fwd, 0), 0, origin ^ 1)]
        state = run(ph, state)
    return state


def solution(mesh):
    in_specs = (
        P(("rep", "seq"), "head"),
        P(None, ("rep", "seq"), "head"),
        P(None, ("rep", "seq"), "head"),
        P(("rep", "seq")),
    )
    out_specs = P(("rep", "seq"), "head")
    return jax.shard_map(body, mesh=mesh, in_specs=in_specs, out_specs=out_specs, check_vma=False)
```

```python
import functools

import jax
import jax.numpy as jnp
from jax import lax
from jax.experimental import pallas as pl
from jax.experimental.pallas import tpu as pltpu
from jax.sharding import PartitionSpec as P

HD = 128
NEG = -1e30
BK = 256


def step_kernel(sc_ref, q_ref, *refs, ninst, t_rows, group, first, last):
    inst_refs = [refs[4 * i:4 * i + 4] for i in range(ninst)]
    rest = refs[4 * ninst:]
    if first:
        state_in = None
    else:
        state_in, rest = rest[:3], rest[3:]
    qs_ref, m_ref, l_ref, acc_ref = rest[-4:]
    o_refs = rest[:-4]
    own = sc_ref[2 * ninst]
    scale = HD ** (-0.5) * 1.4426950408889634
    rows_all = group * t_rows
    reps = BK // 128
    for g in range(group):
        qs_ref[g * t_rows:(g + 1) * t_rows, :] = q_ref[:, g * HD:(g + 1) * HD]
    if first:
        m_ref[...] = jnp.full(m_ref.shape, NEG, jnp.float32)
        l_ref[...] = jnp.zeros(l_ref.shape, jnp.float32)
        acc_ref[...] = jnp.zeros(acc_ref.shape, jnp.float32)
    else:
        m_ref[...] = state_in[0][...]
        l_ref[...] = state_in[1][...]
        acc_ref[...] = state_in[2][...]

    def step(start, k_ref, v_ref, limit=None, causal=False):
        k = k_ref[pl.ds(start, BK), :]
        v = v_ref[pl.ds(start, BK), :]
        s = lax.dot_general(qs_ref[...], k, (((1,), (1,)), ((), ())), preferred_element_type=jnp.float32) * scale
        if limit is not None:
            mask = lax.broadcasted_iota(jnp.int32, (rows_all, BK), 1) < limit
            s = jnp.where(mask, s, NEG)
        if causal:
            cols = lax.broadcasted_iota(jnp.int32, (t_rows, BK), 1) + start
            rows = lax.broadcasted_iota(jnp.int32, (t_rows, BK), 0)
            mask = jnp.concatenate([cols <= rows] * group, axis=0)
            s = jnp.where(mask, s, NEG)
        m_prev = m_ref[...]
        m_new = jnp.maximum(m_prev, jnp.max(s, axis=1, keepdims=True))
        alpha = jnp.exp2(m_prev - m_new)
        m_wide = m_new if reps == 1 else jnp.concatenate([m_new] * reps, axis=1)
        p = jnp.exp2(s - m_wide)
        p_sum = p[:, :128]
        for r in range(1, reps):
            p_sum = p_sum + p[:, r * 128:(r + 1) * 128]
        l_ref[...] = alpha * l_ref[...] + p_sum
        acc_ref[...] = alpha * acc_ref[...] + jnp.dot(p.astype(v.dtype), v, preferred_element_type=jnp.float32)
        m_ref[...] = m_new

    for i, (ck_ref, cv_ref, sk_ref, sv_ref) in enumerate(inst_refs):
        length = sc_ref[i]
        origin = sc_ref[ninst + i]
        n_full = length // BK
        rem = length - n_full * BK

        def loop_body(b, c, ck_ref=ck_ref, cv_ref=cv_ref):
            step(pl.multiple_of(b * BK, BK), ck_ref, cv_ref)
            return c

        lax.fori_loop(0, n_full, loop_body, 0)

        @pl.when(rem > 0)
        def _(ck_ref=ck_ref, cv_ref=cv_ref, n_full=n_full, rem=rem):
            step(pl.multiple_of(n_full * BK, BK), ck_ref, cv_ref, limit=rem)

        @pl.when(origin < own)
        def _(sk_ref=sk_ref, sv_ref=sv_ref):
            for d in range(t_rows // BK):
                step(d * BK, sk_ref, sv_ref)

        @pl.when(origin == own)
        def _(sk_ref=sk_ref, sv_ref=sv_ref):
            for d in range(t_rows // BK):
                step(d * BK, sk_ref, sv_ref, causal=True)

    if last:
        (o_ref,) = o_refs
        out = acc_ref[...] / jnp.sum(l_ref[...], axis=1, keepdims=True)
        for g in range(group):
            o_ref[:, g * HD:(g + 1) * HD] = out[g * t_rows:(g + 1) * t_rows].astype(o_ref.dtype)
    else:
        o_refs[0][...] = m_ref[...]
        o_refs[1][...] = l_ref[...]
        o_refs[2][...] = acc_ref[...]


def attn_call(sc, q, insts, rows, state, first, last):
    t_rows, q_width = q.shape
    kv_width = insts[0][0].shape[2]
    kv_local = kv_width // HD
    group = q_width // kv_width
    c_rows, s_rows = rows
    rows_all = group * t_rows
    ninst = len(insts)
    kernel = functools.partial(step_kernel, ninst=ninst, t_rows=t_rows, group=group, first=first, last=last)
    st_spec = pl.BlockSpec((rows_all, 128), lambda k, *_: (k, 0))
    st_shape = jax.ShapeDtypeStruct((kv_local * rows_all, 128), jnp.float32)
    in_specs = [pl.BlockSpec((t_rows, group * HD), lambda k, *_: (0, k))]
    args = [sc, q]
    for cache, span, srow in insts:
        in_specs += [
            pl.BlockSpec((None, c_rows, HD), lambda k, *_: (0, 0, k)),
            pl.BlockSpec((None, c_rows, HD), lambda k, *_: (1, 0, k)),
            pl.BlockSpec((None, s_rows, HD), lambda k, *_, srow=srow: (0, srow, k)),
            pl.BlockSpec((None, s_rows, HD), lambda k, *_, srow=srow: (1, srow, k)),
        ]
        args += [cache, cache, span, span]
    if not first:
        in_specs += [st_spec] * 3
        args += list(state)
    if last:
        out_specs = pl.BlockSpec((t_rows, group * HD), lambda k, *_: (0, k))
        out_shape = jax.ShapeDtypeStruct((t_rows, q_width), q.dtype)
    else:
        out_specs = [st_spec] * 3
        out_shape = [st_shape] * 3
    keys = ninst * (c_rows + s_rows)
    heads = kv_local * group
    cost = pl.CostEstimate(
        flops=4 * heads * t_rows * keys * HD,
        transcendentals=heads * t_rows * keys,
        bytes_accessed=2 * t_rows * q_width + 4 * keys * kv_width + 24 * kv_local * rows_all * 128,
    )
    grid_spec = pltpu.PrefetchScalarGridSpec(
        num_scalar_prefetch=1,
        grid=(kv_local,),
        in_specs=in_specs,
        out_specs=out_specs,
        scratch_shapes=[
            pltpu.VMEM((rows_all, HD), q.dtype),
            pltpu.VMEM((rows_all, 128), jnp.float32),
            pltpu.VMEM((rows_all, 128), jnp.float32),
            pltpu.VMEM((rows_all, HD), jnp.float32),
        ],
    )
    return pl.pallas_call(
        kernel,
        out_shape=out_shape,
        grid_spec=grid_spec,
        compiler_params=pltpu.CompilerParams(dimension_semantics=("arbitrary",)),
        cost_estimate=cost,
    )(*args)


def chain_need(n, first_pairs, hops):
    need = []
    for k in range(len(hops)):
        keep = []
        for src in range(n):
            origin = first_pairs[src]
            dst = src
            for j in range(k + 1):
                dst = hops[j](dst)
            later = [dst, dst ^ 1]
            d = dst
            for j in range(k + 1, len(hops)):
                d = hops[j](d)
                later += [d, d ^ 1]
            if any(x > origin for x in later):
                keep.append(src)
        need.append(keep)
    return need


def body(query_rows, span_kv, cache_kv, cache_len):
    n = lax.psum(1, "seq")
    own = lax.axis_index("seq").astype(jnp.int32)
    n_chips = n // 2
    c_rows = cache_kv.shape[1]
    s_rows = span_kv.shape[1]
    kv_width = cache_kv.shape[2]
    length = cache_len.reshape(())
    tag = jnp.zeros((2, 16, kv_width), cache_kv.dtype)
    tag = tag.at[0, 0, 0].set((length // 64).astype(cache_kv.dtype))
    tag = tag.at[0, 0, 1].set((length % 64).astype(cache_kv.dtype))
    tail = jnp.concatenate([span_kv, tag], axis=1)

    def send(x, fn):
        return lax.ppermute(x, "seq", [(i, fn(i)) for i in range(n)])

    def length_of(blk):
        hi = blk[0, s_rows, 0].astype(jnp.int32)
        lo = blk[0, s_rows, 1].astype(jnp.int32)
        return hi * 64 + lo

    calls = [0]

    def run(phase, state):
        lens = [jnp.asarray(ln, jnp.int32).reshape(1) for _, ln, _ in phase]
        origins = [jnp.asarray(o, jnp.int32).reshape(1) for _, _, o in phase]
        sc = jnp.concatenate(lens + origins + [own.reshape(1)]).astype(jnp.int32)
        insts = [b for b, _, _ in phase]
        first = calls[0] == 0
        calls[0] += 1
        return attn_call(sc, query_rows, insts, (c_rows, s_rows), state, first=first, last=(calls[0] == n_chips))

    k_right = n_chips // 2
    k_left = n_chips - 1 - k_right
    hops = []
    for sign, count in ((2, k_right), (-2, k_left)):
        blk = (cache_kv, tail)
        for k in range(1, count + 1):
            blk = tuple(send(x, lambda i, sign=sign: (i + sign) % n) for x in blk)
            hops.append((blk, sign, k))
    part = tuple(send(x, lambda i: i ^ 1) for x in (cache_kv, tail))
    state = run([((cache_kv, span_kv, 0), length, own), ((part[0], part[1], 0), length_of(part[1]), own ^ 1)], None)
    for blk, sign, k in hops:
        state, blk = lax.optimization_barrier((state, blk))
        origin = (own - sign * k) % n
        fwd = tuple(send(x, lambda i: i ^ 1) for x in blk)
        state = run([((blk[0], blk[1], 0), length_of(blk[1]), origin), ((fwd[0], fwd[1], 0), length_of(fwd[1]), origin ^ 1)], state)
    return state


def solution(mesh):
    in_specs = (
        P(("rep", "seq"), "head"),
        P(None, ("rep", "seq"), "head"),
        P(None, ("rep", "seq"), "head"),
        P(("rep", "seq")),
    )
    out_specs = P(("rep", "seq"), "head")
    return jax.shard_map(body, mesh=mesh, in_specs=in_specs, out_specs=out_specs, check_vma=False)
```

```python
import functools

import jax
import jax.numpy as jnp
from jax import lax
from jax.experimental import pallas as pl
from jax.experimental.pallas import tpu as pltpu
from jax.sharding import PartitionSpec as P

HD = 128
NEG = -1e30
BK = 256


def step_kernel(sc_ref, q_ref, *refs, ninst, t_rows, group, first, last):
    inst_refs = [refs[4 * i:4 * i + 4] for i in range(ninst)]
    rest = refs[4 * ninst:]
    if first:
        state_in = None
    else:
        state_in, rest = rest[:3], rest[3:]
    if first and last:
        o_refs, (qs_ref, m_ref, l_ref, acc_ref) = rest[:-4], rest[-4:]
    else:
        o_refs, qs_ref = rest[:-1], rest[-1]
        if last:
            m_ref, l_ref, acc_ref = state_in
        else:
            m_ref, l_ref, acc_ref = o_refs
    own = sc_ref[2 * ninst]
    scale = HD ** (-0.5) * 1.4426950408889634
    rows_all = group * t_rows
    reps = BK // 128
    for g in range(group):
        qs_ref[g * t_rows:(g + 1) * t_rows, :] = q_ref[:, g * HD:(g + 1) * HD]
    if first:
        m_ref[...] = jnp.full(m_ref.shape, NEG, jnp.float32)
        l_ref[...] = jnp.zeros(l_ref.shape, jnp.float32)
        acc_ref[...] = jnp.zeros(acc_ref.shape, jnp.float32)
    elif not last:
        m_ref[...] = state_in[0][...]
        l_ref[...] = state_in[1][...]
        acc_ref[...] = state_in[2][...]

    def step(start, k_ref, v_ref, limit=None, causal=False):
        k = k_ref[pl.ds(start, BK), :]
        v = v_ref[pl.ds(start, BK), :]
        s = lax.dot_general(qs_ref[...], k, (((1,), (1,)), ((), ())), preferred_element_type=jnp.float32) * scale
        if limit is not None:
            mask = lax.broadcasted_iota(jnp.int32, (rows_all, BK), 1) < limit
            s = jnp.where(mask, s, NEG)
        if causal:
            cols = lax.broadcasted_iota(jnp.int32, (t_rows, BK), 1) + start
            rows = lax.broadcasted_iota(jnp.int32, (t_rows, BK), 0)
            mask = jnp.concatenate([cols <= rows] * group, axis=0)
            s = jnp.where(mask, s, NEG)
        m_prev = m_ref[...]
        m_new = jnp.maximum(m_prev, jnp.max(s, axis=1, keepdims=True))
        alpha = jnp.exp2(m_prev - m_new)
        m_wide = m_new if reps == 1 else jnp.concatenate([m_new] * reps, axis=1)
        p = jnp.exp2(s - m_wide)
        p_sum = p[:, :128]
        for r in range(1, reps):
            p_sum = p_sum + p[:, r * 128:(r + 1) * 128]
        l_ref[...] = alpha * l_ref[...] + p_sum
        acc_ref[...] = alpha * acc_ref[...] + jnp.dot(p.astype(v.dtype), v, preferred_element_type=jnp.float32)
        m_ref[...] = m_new

    for i, (ck_ref, cv_ref, sk_ref, sv_ref) in enumerate(inst_refs):
        length = sc_ref[i]
        origin = sc_ref[ninst + i]
        n_full = length // BK
        rem = length - n_full * BK

        def loop_body(b, c, ck_ref=ck_ref, cv_ref=cv_ref):
            step(pl.multiple_of(b * BK, BK), ck_ref, cv_ref)
            return c

        lax.fori_loop(0, n_full, loop_body, 0)

        @pl.when(rem > 0)
        def _(ck_ref=ck_ref, cv_ref=cv_ref, n_full=n_full, rem=rem):
            step(pl.multiple_of(n_full * BK, BK), ck_ref, cv_ref, limit=rem)

        @pl.when(origin < own)
        def _(sk_ref=sk_ref, sv_ref=sv_ref):
            for d in range(t_rows // BK):
                step(d * BK, sk_ref, sv_ref)

        @pl.when(origin == own)
        def _(sk_ref=sk_ref, sv_ref=sv_ref):
            for d in range(t_rows // BK):
                step(d * BK, sk_ref, sv_ref, causal=True)

    if last:
        (o_ref,) = o_refs
        out = acc_ref[...] / jnp.sum(l_ref[...], axis=1, keepdims=True)
        for g in range(group):
            o_ref[:, g * HD:(g + 1) * HD] = out[g * t_rows:(g + 1) * t_rows].astype(o_ref.dtype)


def attn_call(sc, q, insts, rows, state, first, last):
    t_rows, q_width = q.shape
    kv_width = insts[0][0].shape[2]
    kv_local = kv_width // HD
    group = q_width // kv_width
    c_rows, s_rows = rows
    rows_all = group * t_rows
    ninst = len(insts)
    kernel = functools.partial(step_kernel, ninst=ninst, t_rows=t_rows, group=group, first=first, last=last)
    st_spec = pl.BlockSpec((rows_all, 128), lambda k, *_: (k, 0))
    st_shape = jax.ShapeDtypeStruct((kv_local * rows_all, 128), jnp.float32)
    in_specs = [pl.BlockSpec((t_rows, group * HD), lambda k, *_: (0, k))]
    args = [sc, q]
    for cache, span, srow in insts:
        in_specs += [
            pl.BlockSpec((None, c_rows, HD), lambda k, *_: (0, 0, k)),
            pl.BlockSpec((None, c_rows, HD), lambda k, *_: (1, 0, k)),
            pl.BlockSpec((None, s_rows, HD), lambda k, *_, srow=srow: (0, srow, k)),
            pl.BlockSpec((None, s_rows, HD), lambda k, *_, srow=srow: (1, srow, k)),
        ]
        args += [cache, cache, span, span]
    if not first:
        in_specs += [st_spec] * 3
        args += list(state)
    if last:
        out_specs = pl.BlockSpec((t_rows, group * HD), lambda k, *_: (0, k))
        out_shape = jax.ShapeDtypeStruct((t_rows, q_width), q.dtype)
    else:
        out_specs = [st_spec] * 3
        out_shape = [st_shape] * 3
    keys = ninst * (c_rows + s_rows)
    heads = kv_local * group
    cost = pl.CostEstimate(
        flops=4 * heads * t_rows * keys * HD,
        transcendentals=heads * t_rows * keys,
        bytes_accessed=2 * t_rows * q_width + 4 * keys * kv_width + 24 * kv_local * rows_all * 128,
    )
    grid_spec = pltpu.PrefetchScalarGridSpec(
        num_scalar_prefetch=1,
        grid=(kv_local,),
        in_specs=in_specs,
        out_specs=out_specs,
        scratch_shapes=[pltpu.VMEM((rows_all, HD), q.dtype)] + ([
            pltpu.VMEM((rows_all, 128), jnp.float32),
            pltpu.VMEM((rows_all, 128), jnp.float32),
            pltpu.VMEM((rows_all, HD), jnp.float32),
        ] if first and last else []),
    )
    return pl.pallas_call(
        kernel,
        out_shape=out_shape,
        grid_spec=grid_spec,
        compiler_params=pltpu.CompilerParams(dimension_semantics=("arbitrary",)),
        cost_estimate=cost,
    )(*args)


def chain_need(n, first_pairs, hops):
    need = []
    for k in range(len(hops)):
        keep = []
        for src in range(n):
            origin = first_pairs[src]
            dst = src
            for j in range(k + 1):
                dst = hops[j](dst)
            later = [dst, dst ^ 1]
            d = dst
            for j in range(k + 1, len(hops)):
                d = hops[j](d)
                later += [d, d ^ 1]
            if any(x > origin for x in later):
                keep.append(src)
        need.append(keep)
    return need


def body(query_rows, span_kv, cache_kv, cache_len):
    n = lax.psum(1, "seq")
    own = lax.axis_index("seq").astype(jnp.int32)
    n_chips = n // 2
    c_rows = cache_kv.shape[1]
    s_rows = span_kv.shape[1]
    kv_width = cache_kv.shape[2]
    length = cache_len.reshape(())
    tag = jnp.zeros((2, 16, kv_width), cache_kv.dtype)
    tag = tag.at[0, 0, 0].set((length // 64).astype(cache_kv.dtype))
    tag = tag.at[0, 0, 1].set((length % 64).astype(cache_kv.dtype))
    merged = jnp.concatenate([cache_kv, span_kv, tag], axis=1)
    srow = c_rows // s_rows

    def send(x, fn):
        return lax.ppermute(x, "seq", [(i, fn(i)) for i in range(n)])

    def length_of(blk):
        hi = blk[0, c_rows + s_rows, 0].astype(jnp.int32)
        lo = blk[0, c_rows + s_rows, 1].astype(jnp.int32)
        return hi * 64 + lo

    calls = [0]

    def run(phase, state):
        lens = [jnp.asarray(ln, jnp.int32).reshape(1) for _, ln, _ in phase]
        origins = [jnp.asarray(o, jnp.int32).reshape(1) for _, _, o in phase]
        sc = jnp.concatenate(lens + origins + [own.reshape(1)]).astype(jnp.int32)
        insts = [b for b, _, _ in phase]
        first = calls[0] == 0
        calls[0] += 1
        return attn_call(sc, query_rows, insts, (c_rows, s_rows), state, first=first, last=(calls[0] == n_chips))

    part = send(merged, lambda i: i ^ 1)
    k_right = n_chips // 2
    k_left = n_chips - 1 - k_right
    hops = []
    for sign, count in ((2, k_right), (-2, k_left)):
        blk = merged
        for k in range(1, count + 1):
            blk = send(blk, lambda i, sign=sign: (i + sign) % n)
            hops.append((blk, sign, k))
    state = run([((cache_kv, span_kv, 0), length, own), ((part, part, srow), length_of(part), own ^ 1)], None)
    for blk, sign, k in hops:
        state, blk = lax.optimization_barrier((state, blk))
        origin = (own - sign * k) % n
        fwd = send(blk, lambda i: i ^ 1)
        state = run([((blk, blk, srow), length_of(blk), origin), ((fwd, fwd, srow), length_of(fwd), origin ^ 1)], state)
    return state


def solution(mesh):
    in_specs = (
        P(("rep", "seq"), "head"),
        P(None, ("rep", "seq"), "head"),
        P(None, ("rep", "seq"), "head"),
        P(("rep", "seq")),
    )
    out_specs = P(("rep", "seq"), "head")
    return jax.shard_map(body, mesh=mesh, in_specs=in_specs, out_specs=out_specs, check_vma=False)
```

```python
import functools

import jax
import jax.numpy as jnp
from jax import lax
from jax.experimental import pallas as pl
from jax.experimental.pallas import tpu as pltpu
from jax.sharding import PartitionSpec as P

HD = 128
NEG = -1e30
BK = 256
VMEM_LIMIT = 64 * 1024 * 1024


def step_kernel(sc_ref, q_ref, *refs, ninst, srows, t_rows, group, first, last):
    hbm_refs = refs[:2 * ninst]
    rest = refs[2 * ninst:-2]
    kv_buf, sem = refs[-2:]
    if first:
        state_in = None
    else:
        state_in, rest = rest[:3], rest[3:]
    if first and last:
        o_refs, (qs_ref, m_ref, l_ref, acc_ref) = rest[:-4], rest[-4:]
    else:
        o_refs, qs_ref = rest[:-1], rest[-1]
        if last:
            m_ref, l_ref, acc_ref = state_in
        else:
            m_ref, l_ref, acc_ref = o_refs
    own = sc_ref[2 * ninst]
    scale = HD ** (-0.5) * 1.4426950408889634
    rows_all = group * t_rows
    reps = BK // 128
    head = pl.program_id(0)
    c_rows = kv_buf.shape[2] - t_rows
    copies = []
    for i in range(ninst):
        cache_hbm, span_hbm = hbm_refs[2 * i], hbm_refs[2 * i + 1]
        cols = pl.ds(pl.multiple_of(head * HD, HD), HD)
        for j in range(2):
            copies.append(pltpu.make_async_copy(
                cache_hbm.at[j, pl.ds(0, c_rows), cols], kv_buf.at[i, j, pl.ds(0, c_rows)], sem.at[i, j, 0]))
            copies.append(pltpu.make_async_copy(
                span_hbm.at[j, pl.ds(srows[i] * t_rows, t_rows), cols], kv_buf.at[i, j, pl.ds(c_rows, t_rows)],
                sem.at[i, j, 1]))
    for cp in copies:
        cp.start()
    for g in range(group):
        qs_ref[g * t_rows:(g + 1) * t_rows, :] = q_ref[:, g * HD:(g + 1) * HD]
    for cp in copies:
        cp.wait()
    inst_refs = []
    for i in range(ninst):
        k_all, v_all = kv_buf.at[i, 0], kv_buf.at[i, 1]
        inst_refs.append((k_all, v_all, k_all.at[pl.ds(c_rows, t_rows)], v_all.at[pl.ds(c_rows, t_rows)]))
    if first:
        m_ref[...] = jnp.full(m_ref.shape, NEG, jnp.float32)
        l_ref[...] = jnp.zeros(l_ref.shape, jnp.float32)
        acc_ref[...] = jnp.zeros(acc_ref.shape, jnp.float32)
    elif not last:
        m_ref[...] = state_in[0][...]
        l_ref[...] = state_in[1][...]
        acc_ref[...] = state_in[2][...]

    def step(start, k_ref, v_ref, limit=None, causal=False):
        k = k_ref[pl.ds(start, BK), :]
        v = v_ref[pl.ds(start, BK), :]
        s = lax.dot_general(qs_ref[...], k, (((1,), (1,)), ((), ())), preferred_element_type=jnp.float32) * scale
        if limit is not None:
            mask = lax.broadcasted_iota(jnp.int32, (rows_all, BK), 1) < limit
            s = jnp.where(mask, s, NEG)
        if causal:
            cols = lax.broadcasted_iota(jnp.int32, (t_rows, BK), 1) + start
            rows = lax.broadcasted_iota(jnp.int32, (t_rows, BK), 0)
            mask = jnp.concatenate([cols <= rows] * group, axis=0)
            s = jnp.where(mask, s, NEG)
        m_prev = m_ref[...]
        m_new = jnp.maximum(m_prev, jnp.max(s, axis=1, keepdims=True))
        alpha = jnp.exp2(m_prev - m_new)
        m_wide = m_new if reps == 1 else jnp.concatenate([m_new] * reps, axis=1)
        p = jnp.exp2(s - m_wide)
        p_sum = p[:, :128]
        for r in range(1, reps):
            p_sum = p_sum + p[:, r * 128:(r + 1) * 128]
        l_ref[...] = alpha * l_ref[...] + p_sum
        acc_ref[...] = alpha * acc_ref[...] + jnp.dot(p.astype(v.dtype), v, preferred_element_type=jnp.float32)
        m_ref[...] = m_new

    for i, (ck_ref, cv_ref, sk_ref, sv_ref) in enumerate(inst_refs):
        length = sc_ref[i]
        origin = sc_ref[ninst + i]
        n_full = length // BK
        rem = length - n_full * BK

        def loop_body(b, c, ck_ref=ck_ref, cv_ref=cv_ref):
            step(pl.multiple_of(b * BK, BK), ck_ref, cv_ref)
            return c

        lax.fori_loop(0, n_full, loop_body, 0)

        @pl.when(rem > 0)
        def _(ck_ref=ck_ref, cv_ref=cv_ref, n_full=n_full, rem=rem):
            step(pl.multiple_of(n_full * BK, BK), ck_ref, cv_ref, limit=rem)

        @pl.when(origin < own)
        def _(sk_ref=sk_ref, sv_ref=sv_ref):
            for d in range(t_rows // BK):
                step(d * BK, sk_ref, sv_ref)

        @pl.when(origin == own)
        def _(sk_ref=sk_ref, sv_ref=sv_ref):
            for d in range(t_rows // BK):
                step(d * BK, sk_ref, sv_ref, causal=True)

    if last:
        (o_ref,) = o_refs
        out = acc_ref[...] / jnp.sum(l_ref[...], axis=1, keepdims=True)
        for g in range(group):
            o_ref[:, g * HD:(g + 1) * HD] = out[g * t_rows:(g + 1) * t_rows].astype(o_ref.dtype)


def attn_call(sc, q, insts, rows, state, first, last):
    t_rows, q_width = q.shape
    kv_width = insts[0][0].shape[2]
    kv_local = kv_width // HD
    group = q_width // kv_width
    c_rows, s_rows = rows
    rows_all = group * t_rows
    ninst = len(insts)
    kernel = functools.partial(step_kernel, ninst=ninst, srows=tuple(sr for _, _, sr in insts), t_rows=t_rows,
                               group=group, first=first, last=last)
    st_spec = pl.BlockSpec((rows_all, 128), lambda k, *_: (k, 0))
    st_shape = jax.ShapeDtypeStruct((kv_local * rows_all, 128), jnp.float32)
    in_specs = [pl.BlockSpec((t_rows, group * HD), lambda k, *_: (0, k))]
    args = [sc, q]
    for cache, span, srow in insts:
        in_specs += [pl.BlockSpec(memory_space=pl.ANY), pl.BlockSpec(memory_space=pl.ANY)]
        args += [cache, span]
    if not first:
        in_specs += [st_spec] * 3
        args += list(state)
    if last:
        out_specs = pl.BlockSpec((t_rows, group * HD), lambda k, *_: (0, k))
        out_shape = jax.ShapeDtypeStruct((t_rows, q_width), q.dtype)
    else:
        out_specs = [st_spec] * 3
        out_shape = [st_shape] * 3
    keys = ninst * (c_rows + s_rows)
    heads = kv_local * group
    cost = pl.CostEstimate(
        flops=4 * heads * t_rows * keys * HD,
        transcendentals=heads * t_rows * keys,
        bytes_accessed=2 * t_rows * q_width + 4 * keys * kv_width + 24 * kv_local * rows_all * 128,
    )
    grid_spec = pltpu.PrefetchScalarGridSpec(
        num_scalar_prefetch=1,
        grid=(kv_local,),
        in_specs=in_specs,
        out_specs=out_specs,
        scratch_shapes=[pltpu.VMEM((rows_all, HD), q.dtype)] + ([
            pltpu.VMEM((rows_all, 128), jnp.float32),
            pltpu.VMEM((rows_all, 128), jnp.float32),
            pltpu.VMEM((rows_all, HD), jnp.float32),
        ] if first and last else []) + [
            pltpu.VMEM((ninst, 2, c_rows + s_rows, HD), q.dtype),
            pltpu.SemaphoreType.DMA((ninst, 2, 2)),
        ],
    )
    return pl.pallas_call(
        kernel,
        out_shape=out_shape,
        grid_spec=grid_spec,
        compiler_params=pltpu.CompilerParams(dimension_semantics=("arbitrary",), vmem_limit_bytes=VMEM_LIMIT),
        cost_estimate=cost,
    )(*args)


def chain_need(n, first_pairs, hops):
    need = []
    for k in range(len(hops)):
        keep = []
        for src in range(n):
            origin = first_pairs[src]
            dst = src
            for j in range(k + 1):
                dst = hops[j](dst)
            later = [dst, dst ^ 1]
            d = dst
            for j in range(k + 1, len(hops)):
                d = hops[j](d)
                later += [d, d ^ 1]
            if any(x > origin for x in later):
                keep.append(src)
        need.append(keep)
    return need


def body(query_rows, span_kv, cache_kv, cache_len):
    n = lax.psum(1, "seq")
    own = lax.axis_index("seq").astype(jnp.int32)
    n_chips = n // 2
    c_rows = cache_kv.shape[1]
    s_rows = span_kv.shape[1]
    kv_width = cache_kv.shape[2]
    length = cache_len.reshape(())
    tag = jnp.zeros((2, 16, kv_width), cache_kv.dtype)
    tag = tag.at[0, 0, 0].set((length // 64).astype(cache_kv.dtype))
    tag = tag.at[0, 0, 1].set((length % 64).astype(cache_kv.dtype))
    merged = jnp.concatenate([cache_kv, span_kv, tag], axis=1)
    srow = c_rows // s_rows

    def send(x, fn):
        return lax.ppermute(x, "seq", [(i, fn(i)) for i in range(n)])

    def length_of(blk):
        hi = blk[0, c_rows + s_rows, 0].astype(jnp.int32)
        lo = blk[0, c_rows + s_rows, 1].astype(jnp.int32)
        return hi * 64 + lo

    calls = [0]

    def run(phase, state):
        lens = [jnp.asarray(ln, jnp.int32).reshape(1) for _, ln, _ in phase]
        origins = [jnp.asarray(o, jnp.int32).reshape(1) for _, _, o in phase]
        sc = jnp.concatenate(lens + origins + [own.reshape(1)]).astype(jnp.int32)
        insts = [b for b, _, _ in phase]
        first = calls[0] == 0
        calls[0] += 1
        return attn_call(sc, query_rows, insts, (c_rows, s_rows), state, first=first, last=(calls[0] == n_chips))

    part = send(merged, lambda i: i ^ 1)
    k_right = n_chips // 2
    k_left = n_chips - 1 - k_right
    hops = []
    for sign, count in ((2, k_right), (-2, k_left)):
        blk = merged
        for k in range(1, count + 1):
            blk = send(blk, lambda i, sign=sign: (i + sign) % n)
            hops.append((blk, sign, k))
    state = run([((cache_kv, span_kv, 0), length, own), ((part, part, srow), length_of(part), own ^ 1)], None)
    for blk, sign, k in hops:
        state, blk = lax.optimization_barrier((state, blk))
        origin = (own - sign * k) % n
        fwd = send(blk, lambda i: i ^ 1)
        state = run([((blk, blk, srow), length_of(blk), origin), ((fwd, fwd, srow), length_of(fwd), origin ^ 1)], state)
    return state


def solution(mesh):
    in_specs = (
        P(("rep", "seq"), "head"),
        P(None, ("rep", "seq"), "head"),
        P(None, ("rep", "seq"), "head"),
        P(("rep", "seq")),
    )
    out_specs = P(("rep", "seq"), "head")
    return jax.shard_map(body, mesh=mesh, in_specs=in_specs, out_specs=out_specs, check_vma=False)
```

```python
import functools

import jax
import jax.numpy as jnp
from jax import lax
from jax.experimental import pallas as pl
from jax.experimental.pallas import tpu as pltpu
from jax.sharding import PartitionSpec as P

HD = 128
NEG = -1e30
BK = 256


def step_kernel(sc_ref, q_ref, *refs, ninst, t_rows, group, first, last):
    inst_refs = [refs[4 * i:4 * i + 4] for i in range(ninst)]
    rest = refs[4 * ninst:]
    if first:
        state_in = None
    else:
        state_in, rest = rest[:3], rest[3:]
    if first and last:
        o_refs, (qs_ref, m_ref, l_ref, acc_ref) = rest[:-4], rest[-4:]
    else:
        o_refs, qs_ref = rest[:-1], rest[-1]
        if last:
            m_ref, l_ref, acc_ref = state_in
        else:
            m_ref, l_ref, acc_ref = o_refs
    own = sc_ref[2 * ninst]
    scale = HD ** (-0.5) * 1.4426950408889634
    rows_all = group * t_rows
    reps = BK // 128
    for g in range(group):
        qs_ref[g * t_rows:(g + 1) * t_rows, :] = q_ref[:, g * HD:(g + 1) * HD]
    if first:
        m_ref[...] = jnp.full(m_ref.shape, NEG, jnp.float32)
        l_ref[...] = jnp.zeros(l_ref.shape, jnp.float32)
        acc_ref[...] = jnp.zeros(acc_ref.shape, jnp.float32)
    elif not last:
        m_ref[...] = state_in[0][...]
        l_ref[...] = state_in[1][...]
        acc_ref[...] = state_in[2][...]

    def step(start, k_ref, v_ref, limit=None, causal=False):
        k = k_ref[pl.ds(start, BK), :]
        v = v_ref[pl.ds(start, BK), :]
        s = lax.dot_general(qs_ref[...], k, (((1,), (1,)), ((), ())), preferred_element_type=jnp.float32) * scale
        if limit is not None:
            mask = lax.broadcasted_iota(jnp.int32, (rows_all, BK), 1) < limit
            s = jnp.where(mask, s, NEG)
        if causal:
            cols = lax.broadcasted_iota(jnp.int32, (t_rows, BK), 1) + start
            rows = lax.broadcasted_iota(jnp.int32, (t_rows, BK), 0)
            mask = jnp.concatenate([cols <= rows] * group, axis=0)
            s = jnp.where(mask, s, NEG)
        m_prev = m_ref[...]
        m_new = jnp.maximum(m_prev, jnp.max(s, axis=1, keepdims=True))
        alpha = jnp.exp2(m_prev - m_new)
        m_wide = m_new if reps == 1 else jnp.concatenate([m_new] * reps, axis=1)
        p = jnp.exp2(s - m_wide)
        p_sum = p[:, :128]
        for r in range(1, reps):
            p_sum = p_sum + p[:, r * 128:(r + 1) * 128]
        l_ref[...] = alpha * l_ref[...] + p_sum
        acc_ref[...] = alpha * acc_ref[...] + jnp.dot(p.astype(v.dtype), v, preferred_element_type=jnp.float32)
        m_ref[...] = m_new

    for i, (ck_ref, cv_ref, sk_ref, sv_ref) in enumerate(inst_refs):
        length = sc_ref[i]
        origin = sc_ref[ninst + i]
        n_full = length // BK
        rem = length - n_full * BK

        def loop_body(b, c, ck_ref=ck_ref, cv_ref=cv_ref):
            step(pl.multiple_of(b * BK, BK), ck_ref, cv_ref)
            return c

        lax.fori_loop(0, n_full, loop_body, 0)

        @pl.when(rem > 0)
        def _(ck_ref=ck_ref, cv_ref=cv_ref, n_full=n_full, rem=rem):
            step(pl.multiple_of(n_full * BK, BK), ck_ref, cv_ref, limit=rem)

        @pl.when(origin < own)
        def _(sk_ref=sk_ref, sv_ref=sv_ref):
            for d in range(t_rows // BK):
                step(d * BK, sk_ref, sv_ref)

        @pl.when(origin == own)
        def _(sk_ref=sk_ref, sv_ref=sv_ref):
            for d in range(t_rows // BK):
                step(d * BK, sk_ref, sv_ref, causal=True)

    if last:
        (o_ref,) = o_refs
        out = acc_ref[...] / jnp.sum(l_ref[...], axis=1, keepdims=True)
        for g in range(group):
            o_ref[:, g * HD:(g + 1) * HD] = out[g * t_rows:(g + 1) * t_rows].astype(o_ref.dtype)


def attn_call(sc, q, insts, rows, state, first, last):
    t_rows, q_width = q.shape
    kv_width = insts[0][0].shape[2]
    kv_local = kv_width // HD
    group = q_width // kv_width
    c_rows, s_rows = rows
    rows_all = group * t_rows
    ninst = len(insts)
    kernel = functools.partial(step_kernel, ninst=ninst, t_rows=t_rows, group=group, first=first, last=last)
    st_spec = pl.BlockSpec((rows_all, 128), lambda k, *_: (k, 0))
    st_shape = jax.ShapeDtypeStruct((kv_local * rows_all, 128), jnp.float32)
    in_specs = [pl.BlockSpec((t_rows, group * HD), lambda k, *_: (0, k))]
    args = [sc, q]
    for cache, span, srow in insts:
        in_specs += [
            pl.BlockSpec((None, c_rows, HD), lambda k, *_: (0, 0, k)),
            pl.BlockSpec((None, c_rows, HD), lambda k, *_: (1, 0, k)),
            pl.BlockSpec((None, s_rows, HD), lambda k, *_, srow=srow: (0, srow, k)),
            pl.BlockSpec((None, s_rows, HD), lambda k, *_, srow=srow: (1, srow, k)),
        ]
        args += [cache, cache, span, span]
    if not first:
        in_specs += [st_spec] * 3
        args += list(state)
    if last:
        out_specs = pl.BlockSpec((t_rows, group * HD), lambda k, *_: (0, k))
        out_shape = jax.ShapeDtypeStruct((t_rows, q_width), q.dtype)
    else:
        out_specs = [st_spec] * 3
        out_shape = [st_shape] * 3
    keys = ninst * (c_rows + s_rows)
    heads = kv_local * group
    cost = pl.CostEstimate(
        flops=4 * heads * t_rows * keys * HD,
        transcendentals=heads * t_rows * keys,
        bytes_accessed=2 * t_rows * q_width + 4 * keys * kv_width + 24 * kv_local * rows_all * 128,
    )
    grid_spec = pltpu.PrefetchScalarGridSpec(
        num_scalar_prefetch=1,
        grid=(kv_local,),
        in_specs=in_specs,
        out_specs=out_specs,
        scratch_shapes=[pltpu.VMEM((rows_all, HD), q.dtype)] + ([
            pltpu.VMEM((rows_all, 128), jnp.float32),
            pltpu.VMEM((rows_all, 128), jnp.float32),
            pltpu.VMEM((rows_all, HD), jnp.float32),
        ] if first and last else []),
    )
    return pl.pallas_call(
        kernel,
        out_shape=out_shape,
        grid_spec=grid_spec,
        compiler_params=pltpu.CompilerParams(dimension_semantics=("arbitrary",)),
        cost_estimate=cost,
    )(*args)


def chain_need(n, first_pairs, hops):
    need = []
    for k in range(len(hops)):
        keep = []
        for src in range(n):
            origin = first_pairs[src]
            dst = src
            for j in range(k + 1):
                dst = hops[j](dst)
            later = [dst, dst ^ 1]
            d = dst
            for j in range(k + 1, len(hops)):
                d = hops[j](d)
                later += [d, d ^ 1]
            if any(x > origin for x in later):
                keep.append(src)
        need.append(keep)
    return need


def body(query_rows, span_kv, cache_kv, cache_len):
    n = lax.psum(1, "seq")
    own = lax.axis_index("seq").astype(jnp.int32)
    n_chips = n // 2
    c_rows = cache_kv.shape[1]
    s_rows = span_kv.shape[1]
    merged = jnp.concatenate([cache_kv, span_kv], axis=1)
    srow = c_rows // s_rows

    def send(x, fn):
        return lax.ppermute(x, "seq", [(i, fn(i)) for i in range(n)])

    calls = [0]

    def run(phase, state):
        lens = [ln.reshape(1) for _, ln, _ in phase]
        origins = [jnp.asarray(o, jnp.int32).reshape(1) for _, _, o in phase]
        sc = jnp.concatenate(lens + origins + [own.reshape(1)]).astype(jnp.int32)
        insts = [b for b, _, _ in phase]
        first = calls[0] == 0
        calls[0] += 1
        return attn_call(sc, query_rows, insts, (c_rows, s_rows), state, first=first, last=(calls[0] == n_chips))

    part_len = send(cache_len, lambda i: i ^ 1)
    k_right = n_chips // 2
    k_left = n_chips - 1 - k_right
    hops = []
    for sign, count in ((2, k_right), (-2, k_left)):
        blk = merged
        for k in range(1, count + 1):
            blk = send(blk, lambda i, sign=sign: (i + sign) % n)
            shift = sign * k
            far_len = send(cache_len, lambda i, shift=shift: (i + shift) % n)
            fwd_len = send(cache_len, lambda i, shift=shift: ((i + shift) % n) ^ 1)
            hops.append((blk, far_len, fwd_len, sign, k))
    part = send(merged, lambda i: i ^ 1)
    part_len, lens_later = lax.optimization_barrier((part_len, [(h[1], h[2]) for h in hops]))
    hops = [(h[0], fl, wl, h[3], h[4]) for h, (fl, wl) in zip(hops, lens_later)]
    state = run([((cache_kv, span_kv, 0), cache_len, own), ((part, part, srow), part_len, own ^ 1)], None)
    for blk, far_len, fwd_len, sign, k in hops:
        state, blk = lax.optimization_barrier((state, blk))
        origin = (own - sign * k) % n
        fwd = send(blk, lambda i: i ^ 1)
        state = run([((blk, blk, srow), far_len, origin), ((fwd, fwd, srow), fwd_len, origin ^ 1)], state)
    return state


def solution(mesh):
    in_specs = (
        P(("rep", "seq"), "head"),
        P(None, ("rep", "seq"), "head"),
        P(None, ("rep", "seq"), "head"),
        P(("rep", "seq")),
    )
    out_specs = P(("rep", "seq"), "head")
    return jax.shard_map(body, mesh=mesh, in_specs=in_specs, out_specs=out_specs, check_vma=False)
```

```python
import functools

import jax
import jax.numpy as jnp
from jax import lax
from jax.experimental import pallas as pl
from jax.experimental.pallas import tpu as pltpu
from jax.sharding import PartitionSpec as P

HD = 128
NEG = -1e30
BK = 256


def step_kernel(sc_ref, q_ref, *refs, kinds, t_rows, group, first, last):
    ninst = len(kinds)
    inst_refs = []
    pos = 0
    for has_cache, has_span in kinds:
        c = refs[pos:pos + 2] if has_cache else None
        pos += 2 if has_cache else 0
        sp = refs[pos:pos + 2] if has_span else None
        pos += 2 if has_span else 0
        inst_refs.append((c, sp))
    rest = refs[pos:]
    if first:
        state_in = None
    else:
        state_in, rest = rest[:3], rest[3:]
    if first and last:
        o_refs, (qs_ref, m_ref, l_ref, acc_ref) = rest[:-4], rest[-4:]
    else:
        o_refs, qs_ref = rest[:-1], rest[-1]
        if last:
            m_ref, l_ref, acc_ref = state_in
        else:
            m_ref, l_ref, acc_ref = o_refs
    own = sc_ref[2 * ninst]
    scale = HD ** (-0.5) * 1.4426950408889634
    rows_all = group * t_rows
    reps = BK // 128
    for g in range(group):
        qs_ref[g * t_rows:(g + 1) * t_rows, :] = q_ref[:, g * HD:(g + 1) * HD]
    if first:
        m_ref[...] = jnp.full(m_ref.shape, NEG, jnp.float32)
        l_ref[...] = jnp.zeros(l_ref.shape, jnp.float32)
        acc_ref[...] = jnp.zeros(acc_ref.shape, jnp.float32)
    elif not last:
        m_ref[...] = state_in[0][...]
        l_ref[...] = state_in[1][...]
        acc_ref[...] = state_in[2][...]

    def step(start, k_ref, v_ref, limit=None, causal=False):
        k = k_ref[pl.ds(start, BK), :]
        v = v_ref[pl.ds(start, BK), :]
        s = lax.dot_general(qs_ref[...], k, (((1,), (1,)), ((), ())), preferred_element_type=jnp.float32) * scale
        if limit is not None:
            mask = lax.broadcasted_iota(jnp.int32, (rows_all, BK), 1) < limit
            s = jnp.where(mask, s, NEG)
        if causal:
            cols = lax.broadcasted_iota(jnp.int32, (t_rows, BK), 1) + start
            rows = lax.broadcasted_iota(jnp.int32, (t_rows, BK), 0)
            mask = jnp.concatenate([cols <= rows] * group, axis=0)
            s = jnp.where(mask, s, NEG)
        m_prev = m_ref[...]
        m_new = jnp.maximum(m_prev, jnp.max(s, axis=1, keepdims=True))
        alpha = jnp.exp2(m_prev - m_new)
        m_wide = m_new if reps == 1 else jnp.concatenate([m_new] * reps, axis=1)
        p = jnp.exp2(s - m_wide)
        p_sum = p[:, :128]
        for r in range(1, reps):
            p_sum = p_sum + p[:, r * 128:(r + 1) * 128]
        l_ref[...] = alpha * l_ref[...] + p_sum
        acc_ref[...] = alpha * acc_ref[...] + jnp.dot(p.astype(v.dtype), v, preferred_element_type=jnp.float32)
        m_ref[...] = m_new

    for i, (c_refs, s_refs) in enumerate(inst_refs):
        length = sc_ref[i]
        origin = sc_ref[ninst + i]
        if c_refs is not None:
            ck_ref, cv_ref = c_refs
            n_full = length // BK
            rem = length - n_full * BK

            def loop_body(b, c, ck_ref=ck_ref, cv_ref=cv_ref):
                step(pl.multiple_of(b * BK, BK), ck_ref, cv_ref)
                return c

            lax.fori_loop(0, n_full, loop_body, 0)

            @pl.when(rem > 0)
            def _(ck_ref=ck_ref, cv_ref=cv_ref, n_full=n_full, rem=rem):
                step(pl.multiple_of(n_full * BK, BK), ck_ref, cv_ref, limit=rem)

        if s_refs is not None:
            sk_ref, sv_ref = s_refs
            @pl.when(origin < own)
            def _(sk_ref=sk_ref, sv_ref=sv_ref):
                for d in range(t_rows // BK):
                    step(d * BK, sk_ref, sv_ref)

            @pl.when(origin == own)
            def _(sk_ref=sk_ref, sv_ref=sv_ref):
                for d in range(t_rows // BK):
                    step(d * BK, sk_ref, sv_ref, causal=True)

    if last:
        (o_ref,) = o_refs
        out = acc_ref[...] / jnp.sum(l_ref[...], axis=1, keepdims=True)
        for g in range(group):
            o_ref[:, g * HD:(g + 1) * HD] = out[g * t_rows:(g + 1) * t_rows].astype(o_ref.dtype)


def attn_call(sc, q, insts, rows, state, first, last):
    kinds = tuple((c is not None, sp is not None) for c, sp, _ in insts)
    t_rows, q_width = q.shape
    kv_width = next(c if c is not None else sp for c, sp, _ in insts).shape[2]
    kv_local = kv_width // HD
    group = q_width // kv_width
    c_rows, s_rows = rows
    rows_all = group * t_rows
    ninst = len(insts)
    kernel = functools.partial(step_kernel, kinds=kinds, t_rows=t_rows, group=group, first=first, last=last)
    st_spec = pl.BlockSpec((rows_all, 128), lambda k, *_: (k, 0))
    st_shape = jax.ShapeDtypeStruct((kv_local * rows_all, 128), jnp.float32)
    in_specs = [pl.BlockSpec((t_rows, group * HD), lambda k, *_: (0, k))]
    args = [sc, q]
    for cache, span, srow in insts:
        if cache is not None:
            in_specs += [
                pl.BlockSpec((None, c_rows, HD), lambda k, *_: (0, 0, k)),
                pl.BlockSpec((None, c_rows, HD), lambda k, *_: (1, 0, k)),
            ]
            args += [cache, cache]
        if span is not None:
            in_specs += [
                pl.BlockSpec((None, s_rows, HD), lambda k, *_, srow=srow: (0, srow, k)),
                pl.BlockSpec((None, s_rows, HD), lambda k, *_, srow=srow: (1, srow, k)),
            ]
            args += [span, span]
    if not first:
        in_specs += [st_spec] * 3
        args += list(state)
    if last:
        out_specs = pl.BlockSpec((t_rows, group * HD), lambda k, *_: (0, k))
        out_shape = jax.ShapeDtypeStruct((t_rows, q_width), q.dtype)
    else:
        out_specs = [st_spec] * 3
        out_shape = [st_shape] * 3
    keys = sum(c_rows * kc + s_rows * ks for kc, ks in kinds)
    heads = kv_local * group
    cost = pl.CostEstimate(
        flops=4 * heads * t_rows * keys * HD,
        transcendentals=heads * t_rows * keys,
        bytes_accessed=2 * t_rows * q_width + 4 * keys * kv_width + 24 * kv_local * rows_all * 128,
    )
    grid_spec = pltpu.PrefetchScalarGridSpec(
        num_scalar_prefetch=1,
        grid=(kv_local,),
        in_specs=in_specs,
        out_specs=out_specs,
        scratch_shapes=[pltpu.VMEM((rows_all, HD), q.dtype)] + ([
            pltpu.VMEM((rows_all, 128), jnp.float32),
            pltpu.VMEM((rows_all, 128), jnp.float32),
            pltpu.VMEM((rows_all, HD), jnp.float32),
        ] if first and last else []),
    )
    return pl.pallas_call(
        kernel,
        out_shape=out_shape,
        grid_spec=grid_spec,
        compiler_params=pltpu.CompilerParams(dimension_semantics=("arbitrary",)),
        cost_estimate=cost,
    )(*args)


def chain_need(n, first_pairs, hops):
    need = []
    for k in range(len(hops)):
        keep = []
        for src in range(n):
            origin = first_pairs[src]
            dst = src
            for j in range(k + 1):
                dst = hops[j](dst)
            later = [dst, dst ^ 1]
            d = dst
            for j in range(k + 1, len(hops)):
                d = hops[j](d)
                later += [d, d ^ 1]
            if any(x > origin for x in later):
                keep.append(src)
        need.append(keep)
    return need


def body(query_rows, span_kv, cache_kv, cache_len):
    n = lax.psum(1, "seq")
    own = lax.axis_index("seq").astype(jnp.int32)
    n_chips = n // 2
    c_rows = cache_kv.shape[1]
    s_rows = span_kv.shape[1]
    kv_width = cache_kv.shape[2]
    length = cache_len.reshape(())
    tag = jnp.zeros((2, 16, kv_width), cache_kv.dtype)
    tag = tag.at[0, 0, 0].set((length // 64).astype(cache_kv.dtype))
    tag = tag.at[0, 0, 1].set((length % 64).astype(cache_kv.dtype))
    merged = jnp.concatenate([cache_kv, span_kv, tag], axis=1)
    srow = c_rows // s_rows

    def send(x, fn, keep=None):
        return lax.ppermute(x, "seq", [(i, fn(i)) for i in range(n) if keep is None or i in keep])

    def length_of(blk, row):
        hi = blk[0, row, 0].astype(jnp.int32)
        lo = blk[0, row, 1].astype(jnp.int32)
        return hi * 64 + lo

    calls = [0]
    n_calls = n_chips + min(n_chips // 2, 1) + min(n_chips - 1 - n_chips // 2, 1)

    def run(phase, state):
        lens = [jnp.asarray(ln, jnp.int32).reshape(1) for _, ln, _ in phase]
        origins = [jnp.asarray(o, jnp.int32).reshape(1) for _, _, o in phase]
        sc = jnp.concatenate(lens + origins + [own.reshape(1)]).astype(jnp.int32)
        insts = [b for b, _, _ in phase]
        first = calls[0] == 0
        calls[0] += 1
        return attn_call(sc, query_rows, insts, (c_rows, s_rows), state, first=first, last=(calls[0] == n_calls))

    part = send(merged, lambda i: i ^ 1)
    k_right = n_chips // 2
    k_left = n_chips - 1 - k_right
    hops = []
    early = []
    for sign, count in ((2, k_right), (-2, k_left)):
        c_blk = jnp.concatenate([cache_kv, tag], axis=1)
        s_blk = span_kv
        for k in range(1, count + 1):
            def hop(i, sign=sign):
                return (i + sign) % n
            keep = []
            for i in range(n):
                o = (i - sign * (k - 1)) % n
                d = i
                ok = False
                for j in range(k, count + 1):
                    d = (d + sign) % n
                    if d > o or (d ^ 1) > o:
                        ok = True
                if ok:
                    keep.append(i)
            s_blk = send(s_blk, hop, keep)
            c_blk = send(c_blk, hop)
            hops.append((c_blk, s_blk, sign, k))
    phase0 = [((cache_kv, span_kv, 0), length, own), ((part, part, srow), length_of(part, c_rows + s_rows), own ^ 1)]
    later = []
    for c_blk, s_blk, sign, k in hops:
        origin = (own - sign * k) % n
        fwd_keep = [i for i in range(n) if (i ^ 1) > (i - sign * k) % n]
        if k == 1:
            early.append((s_blk, origin, fwd_keep))
            later.append((c_blk, None, None, sign, k))
        else:
            later.append((c_blk, s_blk, fwd_keep, sign, k))
    state = run(phase0, None)
    for s_blk, origin, fwd_keep in early:
        state, s_blk = lax.optimization_barrier((state, s_blk))
        s_fwd = send(s_blk, lambda i: i ^ 1, fwd_keep)
        state = run([((None, s_blk, 0), 0, origin), ((None, s_fwd, 0), 0, origin ^ 1)], state)
    for c_blk, s_blk, fwd_keep, sign, k in later:
        if s_blk is None:
            state, c_blk = lax.optimization_barrier((state, c_blk))
        else:
            state, c_blk, s_blk = lax.optimization_barrier((state, c_blk, s_blk))
        origin = (own - sign * k) % n
        c_fwd = send(c_blk, lambda i: i ^ 1)
        ph = [((c_blk, None, 0), length_of(c_blk, c_rows), origin), ((c_fwd, None, 0), length_of(c_fwd, c_rows), origin ^ 1)]
        if s_blk is not None:
            s_fwd = send(s_blk, lambda i: i ^ 1, fwd_keep)
            ph += [((None, s_blk, 0), 0, origin), ((None, s_fwd, 0), 0, origin ^ 1)]
        state = run(ph, state)
    return state


def solution(mesh):
    in_specs = (
        P(("rep", "seq"), "head"),
        P(None, ("rep", "seq"), "head"),
        P(None, ("rep", "seq"), "head"),
        P(("rep", "seq")),
    )
    out_specs = P(("rep", "seq"), "head")
    return jax.shard_map(body, mesh=mesh, in_specs=in_specs, out_specs=out_specs, check_vma=False)
```

```python
import functools

import jax
import jax.numpy as jnp
from jax import lax
from jax.experimental import pallas as pl
from jax.experimental.pallas import tpu as pltpu
from jax.sharding import PartitionSpec as P

HD = 128
NEG = -1e30
BK = 256
SPLIT = 2


def step_kernel(sc_ref, q_ref, *refs, ninst, t_rows, group, first, last):
    inst_refs = [refs[4 * i:4 * i + 4] for i in range(ninst)]
    rest = refs[4 * ninst:]
    if first:
        state_in = None
    else:
        state_in, rest = rest[:3], rest[3:]
    if first and last:
        o_refs, (qs_ref, m_ref, l_ref, acc_ref) = rest[:-4], rest[-4:]
    else:
        o_refs, qs_ref = rest[:-1], rest[-1]
        if last:
            m_ref, l_ref, acc_ref = state_in
        else:
            m_ref, l_ref, acc_ref = o_refs
    own = sc_ref[2 * ninst]
    scale = HD ** (-0.5) * 1.4426950408889634
    rows_all = group * t_rows
    reps = BK // 128
    for g in range(group):
        qs_ref[g * t_rows:(g + 1) * t_rows, :] = q_ref[:, g * HD:(g + 1) * HD]
    if first:
        m_ref[...] = jnp.full(m_ref.shape, NEG, jnp.float32)
        l_ref[...] = jnp.zeros(l_ref.shape, jnp.float32)
        acc_ref[...] = jnp.zeros(acc_ref.shape, jnp.float32)
    elif not last:
        m_ref[...] = state_in[0][...]
        l_ref[...] = state_in[1][...]
        acc_ref[...] = state_in[2][...]

    def step(start, k_ref, v_ref, limit=None, causal=False):
        k = k_ref[pl.ds(start, BK), :]
        v = v_ref[pl.ds(start, BK), :]
        s = lax.dot_general(qs_ref[...], k, (((1,), (1,)), ((), ())), preferred_element_type=jnp.float32) * scale
        if limit is not None:
            mask = lax.broadcasted_iota(jnp.int32, (rows_all, BK), 1) < limit
            s = jnp.where(mask, s, NEG)
        if causal:
            cols = lax.broadcasted_iota(jnp.int32, (t_rows, BK), 1) + start
            rows = lax.broadcasted_iota(jnp.int32, (t_rows, BK), 0)
            mask = jnp.concatenate([cols <= rows] * group, axis=0)
            s = jnp.where(mask, s, NEG)
        m_prev = m_ref[...]
        m_new = jnp.maximum(m_prev, jnp.max(s, axis=1, keepdims=True))
        alpha = jnp.exp2(m_prev - m_new)
        m_wide = m_new if reps == 1 else jnp.concatenate([m_new] * reps, axis=1)
        p = jnp.exp2(s - m_wide)
        p_sum = p[:, :128]
        for r in range(1, reps):
            p_sum = p_sum + p[:, r * 128:(r + 1) * 128]
        l_ref[...] = alpha * l_ref[...] + p_sum
        acc_ref[...] = alpha * acc_ref[...] + jnp.dot(p.astype(v.dtype), v, preferred_element_type=jnp.float32)
        m_ref[...] = m_new

    for i, (ck_ref, cv_ref, sk_ref, sv_ref) in enumerate(inst_refs):
        length = sc_ref[i]
        origin = sc_ref[ninst + i]
        n_full = length // BK
        rem = length - n_full * BK

        def loop_body(b, c, ck_ref=ck_ref, cv_ref=cv_ref):
            step(pl.multiple_of(b * BK, BK), ck_ref, cv_ref)
            return c

        lax.fori_loop(0, n_full, loop_body, 0)

        @pl.when(rem > 0)
        def _(ck_ref=ck_ref, cv_ref=cv_ref, n_full=n_full, rem=rem):
            step(pl.multiple_of(n_full * BK, BK), ck_ref, cv_ref, limit=rem)

        @pl.when(origin < own)
        def _(sk_ref=sk_ref, sv_ref=sv_ref):
            for d in range(t_rows // BK):
                step(d * BK, sk_ref, sv_ref)

        @pl.when(origin == own)
        def _(sk_ref=sk_ref, sv_ref=sv_ref):
            for d in range(t_rows // BK):
                step(d * BK, sk_ref, sv_ref, causal=True)

    if last:
        (o_ref,) = o_refs
        out = acc_ref[...] / jnp.sum(l_ref[...], axis=1, keepdims=True)
        for g in range(group):
            o_ref[:, g * HD:(g + 1) * HD] = out[g * t_rows:(g + 1) * t_rows].astype(o_ref.dtype)


def attn_call(sc, q, insts, rows, state, first, last):
    t_rows, q_width = q.shape
    kv_width = insts[0][0].shape[2]
    kv_local = kv_width // HD
    group = q_width // kv_width // SPLIT
    c_rows, s_rows = rows
    rows_all = group * t_rows
    ninst = len(insts)
    kernel = functools.partial(step_kernel, ninst=ninst, t_rows=t_rows, group=group, first=first, last=last)
    st_spec = pl.BlockSpec((rows_all, 128), lambda k, h, *_: (k * SPLIT + h, 0))
    st_shape = jax.ShapeDtypeStruct((kv_local * SPLIT * rows_all, 128), jnp.float32)
    in_specs = [pl.BlockSpec((t_rows, group * HD), lambda k, h, *_: (0, k * SPLIT + h))]
    args = [sc, q]
    for cache, span, srow in insts:
        in_specs += [
            pl.BlockSpec((None, c_rows, HD), lambda k, h, *_: (0, 0, k)),
            pl.BlockSpec((None, c_rows, HD), lambda k, h, *_: (1, 0, k)),
            pl.BlockSpec((None, s_rows, HD), lambda k, h, *_, srow=srow: (0, srow, k)),
            pl.BlockSpec((None, s_rows, HD), lambda k, h, *_, srow=srow: (1, srow, k)),
        ]
        args += [cache, cache, span, span]
    if not first:
        in_specs += [st_spec] * 3
        args += list(state)
    if last:
        out_specs = pl.BlockSpec((t_rows, group * HD), lambda k, h, *_: (0, k * SPLIT + h))
        out_shape = jax.ShapeDtypeStruct((t_rows, q_width), q.dtype)
    else:
        out_specs = [st_spec] * 3
        out_shape = [st_shape] * 3
    keys = ninst * (c_rows + s_rows)
    heads = kv_local * group * SPLIT
    cost = pl.CostEstimate(
        flops=4 * heads * t_rows * keys * HD,
        transcendentals=heads * t_rows * keys,
        bytes_accessed=2 * t_rows * q_width + 4 * keys * kv_width + 24 * kv_local * rows_all * 128,
    )
    grid_spec = pltpu.PrefetchScalarGridSpec(
        num_scalar_prefetch=1,
        grid=(kv_local, SPLIT),
        in_specs=in_specs,
        out_specs=out_specs,
        scratch_shapes=[pltpu.VMEM((rows_all, HD), q.dtype)] + ([
            pltpu.VMEM((rows_all, 128), jnp.float32),
            pltpu.VMEM((rows_all, 128), jnp.float32),
            pltpu.VMEM((rows_all, HD), jnp.float32),
        ] if first and last else []),
    )
    return pl.pallas_call(
        kernel,
        out_shape=out_shape,
        grid_spec=grid_spec,
        compiler_params=pltpu.CompilerParams(dimension_semantics=("arbitrary", "arbitrary")),
        cost_estimate=cost,
    )(*args)


def chain_need(n, first_pairs, hops):
    need = []
    for k in range(len(hops)):
        keep = []
        for src in range(n):
            origin = first_pairs[src]
            dst = src
            for j in range(k + 1):
                dst = hops[j](dst)
            later = [dst, dst ^ 1]
            d = dst
            for j in range(k + 1, len(hops)):
                d = hops[j](d)
                later += [d, d ^ 1]
            if any(x > origin for x in later):
                keep.append(src)
        need.append(keep)
    return need


def body(query_rows, span_kv, cache_kv, cache_len):
    n = lax.psum(1, "seq")
    own = lax.axis_index("seq").astype(jnp.int32)
    n_chips = n // 2
    c_rows = cache_kv.shape[1]
    s_rows = span_kv.shape[1]
    kv_width = cache_kv.shape[2]
    length = cache_len.reshape(())
    tag = jnp.zeros((2, 16, kv_width), cache_kv.dtype)
    tag = tag.at[0, 0, 0].set((length // 64).astype(cache_kv.dtype))
    tag = tag.at[0, 0, 1].set((length % 64).astype(cache_kv.dtype))
    merged = jnp.concatenate([cache_kv, span_kv, tag], axis=1)
    srow = c_rows // s_rows

    def send(x, fn):
        return lax.ppermute(x, "seq", [(i, fn(i)) for i in range(n)])

    def length_of(blk):
        hi = blk[0, c_rows + s_rows, 0].astype(jnp.int32)
        lo = blk[0, c_rows + s_rows, 1].astype(jnp.int32)
        return hi * 64 + lo

    calls = [0]

    def run(phase, state):
        lens = [jnp.asarray(ln, jnp.int32).reshape(1) for _, ln, _ in phase]
        origins = [jnp.asarray(o, jnp.int32).reshape(1) for _, _, o in phase]
        sc = jnp.concatenate(lens + origins + [own.reshape(1)]).astype(jnp.int32)
        insts = [b for b, _, _ in phase]
        first = calls[0] == 0
        calls[0] += 1
        return attn_call(sc, query_rows, insts, (c_rows, s_rows), state, first=first, last=(calls[0] == n_chips))

    part = send(merged, lambda i: i ^ 1)
    k_right = n_chips // 2
    k_left = n_chips - 1 - k_right
    hops = []
    for sign, count in ((2, k_right), (-2, k_left)):
        blk = merged
        for k in range(1, count + 1):
            blk = send(blk, lambda i, sign=sign: (i + sign) % n)
            hops.append((blk, sign, k))
    state = run([((cache_kv, span_kv, 0), length, own), ((part, part, srow), length_of(part), own ^ 1)], None)
    for blk, sign, k in hops:
        state, blk = lax.optimization_barrier((state, blk))
        origin = (own - sign * k) % n
        fwd = send(blk, lambda i: i ^ 1)
        state = run([((blk, blk, srow), length_of(blk), origin), ((fwd, fwd, srow), length_of(fwd), origin ^ 1)], state)
    return state


def solution(mesh):
    in_specs = (
        P(("rep", "seq"), "head"),
        P(None, ("rep", "seq"), "head"),
        P(None, ("rep", "seq"), "head"),
        P(("rep", "seq")),
    )
    out_specs = P(("rep", "seq"), "head")
    return jax.shard_map(body, mesh=mesh, in_specs=in_specs, out_specs=out_specs, check_vma=False)
```

```python
import functools

import jax
import jax.numpy as jnp
from jax import lax
from jax.experimental import pallas as pl
from jax.experimental.pallas import tpu as pltpu
from jax.sharding import PartitionSpec as P

HD = 128
NEG = -1e30
BK = 256


def step_kernel(sc_ref, q_ref, *refs, ninst, t_rows, group, first, last):
    inst_refs = [refs[4 * i:4 * i + 4] for i in range(ninst)]
    rest = refs[4 * ninst:]
    if first:
        state_in = None
    else:
        state_in, rest = rest[:3], rest[3:]
    if first and last:
        o_refs, (qs_ref, m_ref, l_ref, acc_ref) = rest[:-4], rest[-4:]
    else:
        o_refs, qs_ref = rest[:-1], rest[-1]
        if last:
            m_ref, l_ref, acc_ref = state_in
        else:
            m_ref, l_ref, acc_ref = o_refs
    own = sc_ref[2 * ninst]
    scale = HD ** (-0.5) * 1.4426950408889634
    rows_all = group * t_rows
    reps = BK // 128
    for g in range(group):
        qs_ref[g * t_rows:(g + 1) * t_rows, :] = q_ref[:, g * HD:(g + 1) * HD]
    if first:
        m_ref[...] = jnp.full(m_ref.shape, NEG, jnp.float32)
        l_ref[...] = jnp.zeros(l_ref.shape, jnp.float32)
        acc_ref[...] = jnp.zeros(acc_ref.shape, jnp.float32)
    elif not last:
        m_ref[...] = state_in[0][...]
        l_ref[...] = state_in[1][...]
        acc_ref[...] = state_in[2][...]

    def step(start, k_ref, v_ref, limit=None, causal=False):
        k = k_ref[pl.ds(start, BK), :]
        v = v_ref[pl.ds(start, BK), :]
        s = lax.dot_general(qs_ref[...], k, (((1,), (1,)), ((), ())), preferred_element_type=jnp.float32) * scale
        if limit is not None:
            mask = lax.broadcasted_iota(jnp.int32, (rows_all, BK), 1) < limit
            s = jnp.where(mask, s, NEG)
        if causal:
            cols = lax.broadcasted_iota(jnp.int32, (t_rows, BK), 1) + start
            rows = lax.broadcasted_iota(jnp.int32, (t_rows, BK), 0)
            mask = jnp.concatenate([cols <= rows] * group, axis=0)
            s = jnp.where(mask, s, NEG)
        m_prev = m_ref[...]
        m_new = jnp.maximum(m_prev, jnp.max(s, axis=1, keepdims=True))
        alpha = jnp.exp2(m_prev - m_new)
        m_wide = m_new if reps == 1 else jnp.concatenate([m_new] * reps, axis=1)
        p = jnp.exp2(s - m_wide)
        p_sum = p[:, :128]
        for r in range(1, reps):
            p_sum = p_sum + p[:, r * 128:(r + 1) * 128]
        l_ref[...] = alpha * l_ref[...] + p_sum
        acc_ref[...] = alpha * acc_ref[...] + jnp.dot(p.astype(v.dtype), v, preferred_element_type=jnp.float32)
        m_ref[...] = m_new

    for i, (ck_ref, cv_ref, sk_ref, sv_ref) in enumerate(inst_refs):
        length = sc_ref[i]
        origin = sc_ref[ninst + i]
        n_full = length // BK
        rem = length - n_full * BK

        def loop_body(b, c, ck_ref=ck_ref, cv_ref=cv_ref):
            step(pl.multiple_of(b * BK, BK), ck_ref, cv_ref)
            return c

        lax.fori_loop(0, n_full, loop_body, 0)

        @pl.when(rem > 0)
        def _(ck_ref=ck_ref, cv_ref=cv_ref, n_full=n_full, rem=rem):
            step(pl.multiple_of(n_full * BK, BK), ck_ref, cv_ref, limit=rem)

        @pl.when(origin < own)
        def _(sk_ref=sk_ref, sv_ref=sv_ref):
            for d in range(t_rows // BK):
                step(d * BK, sk_ref, sv_ref)

        @pl.when(origin == own)
        def _(sk_ref=sk_ref, sv_ref=sv_ref):
            for d in range(t_rows // BK):
                step(d * BK, sk_ref, sv_ref, causal=True)

    if last:
        (o_ref,) = o_refs
        out = acc_ref[...] / jnp.sum(l_ref[...], axis=1, keepdims=True)
        for g in range(group):
            o_ref[:, g * HD:(g + 1) * HD] = out[g * t_rows:(g + 1) * t_rows].astype(o_ref.dtype)


def attn_call(sc, q, insts, rows, state, first, last):
    t_rows, q_width = q.shape
    kv_width = insts[0][0].shape[2]
    kv_local = kv_width // HD
    group = q_width // kv_width
    c_rows, s_rows = rows
    rows_all = group * t_rows
    ninst = len(insts)
    kernel = functools.partial(step_kernel, ninst=ninst, t_rows=t_rows, group=group, first=first, last=last)
    st_spec = pl.BlockSpec((rows_all, 128), lambda k, *_: (k, 0))
    st_shape = jax.ShapeDtypeStruct((kv_local * rows_all, 128), jnp.float32)
    in_specs = [pl.BlockSpec((t_rows, group * HD), lambda k, *_: (0, k))]
    args = [sc, q]
    for cache, span, srow in insts:
        in_specs += [
            pl.BlockSpec((None, c_rows, HD), lambda k, *_: (0, 0, k)),
            pl.BlockSpec((None, c_rows, HD), lambda k, *_: (1, 0, k)),
            pl.BlockSpec((None, s_rows, HD), lambda k, *_, srow=srow: (0, srow, k)),
            pl.BlockSpec((None, s_rows, HD), lambda k, *_, srow=srow: (1, srow, k)),
        ]
        args += [cache, cache, span, span]
    if not first:
        in_specs += [st_spec] * 3
        args += list(state)
    if last:
        out_specs = pl.BlockSpec((t_rows, group * HD), lambda k, *_: (0, k))
        out_shape = jax.ShapeDtypeStruct((t_rows, q_width), q.dtype)
    else:
        out_specs = [st_spec] * 3
        out_shape = [st_shape] * 3
    keys = ninst * (c_rows + s_rows)
    heads = kv_local * group
    cost = pl.CostEstimate(
        flops=4 * heads * t_rows * keys * HD,
        transcendentals=heads * t_rows * keys,
        bytes_accessed=2 * t_rows * q_width + 4 * keys * kv_width + 24 * kv_local * rows_all * 128,
    )
    grid_spec = pltpu.PrefetchScalarGridSpec(
        num_scalar_prefetch=1,
        grid=(kv_local,),
        in_specs=in_specs,
        out_specs=out_specs,
        scratch_shapes=[pltpu.VMEM((rows_all, HD), q.dtype)] + ([
            pltpu.VMEM((rows_all, 128), jnp.float32),
            pltpu.VMEM((rows_all, 128), jnp.float32),
            pltpu.VMEM((rows_all, HD), jnp.float32),
        ] if first and last else []),
    )
    return pl.pallas_call(
        kernel,
        out_shape=out_shape,
        grid_spec=grid_spec,
        compiler_params=pltpu.CompilerParams(dimension_semantics=("arbitrary",)),
        cost_estimate=cost,
    )(*args)


def chain_need(n, first_pairs, hops):
    need = []
    for k in range(len(hops)):
        keep = []
        for src in range(n):
            origin = first_pairs[src]
            dst = src
            for j in range(k + 1):
                dst = hops[j](dst)
            later = [dst, dst ^ 1]
            d = dst
            for j in range(k + 1, len(hops)):
                d = hops[j](d)
                later += [d, d ^ 1]
            if any(x > origin for x in later):
                keep.append(src)
        need.append(keep)
    return need


def body(query_rows, span_kv, cache_kv, cache_len):
    n = lax.psum(1, "seq")
    own = lax.axis_index("seq").astype(jnp.int32)
    n_chips = n // 2
    c_rows = cache_kv.shape[1]
    s_rows = span_kv.shape[1]
    kv_width = cache_kv.shape[2]
    length = cache_len.reshape(())
    tag = jnp.zeros((2, 16, kv_width), cache_kv.dtype)
    tag = tag.at[0, 0, 0].set((length // 64).astype(cache_kv.dtype))
    tag = tag.at[0, 0, 1].set((length % 64).astype(cache_kv.dtype))
    merged = jnp.concatenate([cache_kv, span_kv, tag], axis=1)
    srow = c_rows // s_rows

    def send(x, fn):
        return lax.ppermute(x, "seq", [(i, fn(i)) for i in range(n)])

    def length_of(blk):
        hi = blk[0, c_rows + s_rows, 0].astype(jnp.int32)
        lo = blk[0, c_rows + s_rows, 1].astype(jnp.int32)
        return hi * 64 + lo

    calls = [0]

    def run(phase, state):
        vals = [ln for _, ln, _ in phase] + [o for _, _, o in phase] + [own]
        slots = jnp.arange(len(vals), dtype=jnp.int32)
        sc = sum(jnp.where(slots == j, jnp.asarray(v, jnp.int32).reshape(()), 0) for j, v in enumerate(vals))
        insts = [b for b, _, _ in phase]
        first = calls[0] == 0
        calls[0] += 1
        return attn_call(sc, query_rows, insts, (c_rows, s_rows), state, first=first, last=(calls[0] == n_chips))

    part = send(merged, lambda i: i ^ 1)
    k_right = n_chips // 2
    k_left = n_chips - 1 - k_right
    hops = []
    for sign, count in ((2, k_right), (-2, k_left)):
        blk = merged
        for k in range(1, count + 1):
            blk = send(blk, lambda i, sign=sign: (i + sign) % n)
            hops.append((blk, sign, k))
    state = run([((cache_kv, span_kv, 0), length, own), ((part, part, srow), length_of(part), own ^ 1)], None)
    for blk, sign, k in hops:
        state, blk = lax.optimization_barrier((state, blk))
        origin = (own - sign * k) % n
        fwd = send(blk, lambda i: i ^ 1)
        state = run([((blk, blk, srow), length_of(blk), origin), ((fwd, fwd, srow), length_of(fwd), origin ^ 1)], state)
    return state


def solution(mesh):
    in_specs = (
        P(("rep", "seq"), "head"),
        P(None, ("rep", "seq"), "head"),
        P(None, ("rep", "seq"), "head"),
        P(("rep", "seq")),
    )
    out_specs = P(("rep", "seq"), "head")
    return jax.shard_map(body, mesh=mesh, in_specs=in_specs, out_specs=out_specs, check_vma=False)
```

```python
import functools

import jax
import jax.numpy as jnp
from jax import lax
from jax.experimental import pallas as pl
from jax.experimental.pallas import tpu as pltpu
from jax.sharding import PartitionSpec as P

HD = 128
NEG = -1e30
BK = 256


def step_kernel(sc_ref, q_ref, *refs, vecs, t_rows, group, first, last):
    ninst = len(vecs)
    inst_refs = []
    pos = 0
    for vec in vecs:
        n_refs = 5 if vec else 4
        inst_refs.append(tuple(refs[pos:pos + 4]) + ((refs[pos + 4],) if vec else (None,)))
        pos += n_refs
    rest = refs[pos:]
    if first:
        state_in = None
    else:
        state_in, rest = rest[:3], rest[3:]
    if first and last:
        o_refs, (qs_ref, m_ref, l_ref, acc_ref) = rest[:-4], rest[-4:]
    else:
        o_refs, qs_ref = rest[:-1], rest[-1]
        if last:
            m_ref, l_ref, acc_ref = state_in
        else:
            m_ref, l_ref, acc_ref = o_refs
    own = sc_ref[2 * ninst]
    scale = HD ** (-0.5) * 1.4426950408889634
    rows_all = group * t_rows
    reps = BK // 128
    for g in range(group):
        qs_ref[g * t_rows:(g + 1) * t_rows, :] = q_ref[:, g * HD:(g + 1) * HD]
    if first:
        m_ref[...] = jnp.full(m_ref.shape, NEG, jnp.float32)
        l_ref[...] = jnp.zeros(l_ref.shape, jnp.float32)
        acc_ref[...] = jnp.zeros(acc_ref.shape, jnp.float32)
    elif not last:
        m_ref[...] = state_in[0][...]
        l_ref[...] = state_in[1][...]
        acc_ref[...] = state_in[2][...]

    def step(start, k_ref, v_ref, limit=None, causal=False):
        k = k_ref[pl.ds(start, BK), :]
        v = v_ref[pl.ds(start, BK), :]
        s = lax.dot_general(qs_ref[...], k, (((1,), (1,)), ((), ())), preferred_element_type=jnp.float32) * scale
        if limit is not None:
            mask = lax.broadcasted_iota(jnp.int32, (rows_all, BK), 1) < limit
            s = jnp.where(mask, s, NEG)
        if causal:
            cols = lax.broadcasted_iota(jnp.int32, (t_rows, BK), 1) + start
            rows = lax.broadcasted_iota(jnp.int32, (t_rows, BK), 0)
            mask = jnp.concatenate([cols <= rows] * group, axis=0)
            s = jnp.where(mask, s, NEG)
        m_prev = m_ref[...]
        m_new = jnp.maximum(m_prev, jnp.max(s, axis=1, keepdims=True))
        alpha = jnp.exp2(m_prev - m_new)
        m_wide = m_new if reps == 1 else jnp.concatenate([m_new] * reps, axis=1)
        p = jnp.exp2(s - m_wide)
        p_sum = p[:, :128]
        for r in range(1, reps):
            p_sum = p_sum + p[:, r * 128:(r + 1) * 128]
        l_ref[...] = alpha * l_ref[...] + p_sum
        acc_ref[...] = alpha * acc_ref[...] + jnp.dot(p.astype(v.dtype), v, preferred_element_type=jnp.float32)
        m_ref[...] = m_new

    for i, (ck_ref, cv_ref, sk_ref, sv_ref, tag_ref) in enumerate(inst_refs):
        origin = sc_ref[ninst + i]
        if tag_ref is not None:
            tag = tag_ref[0:1, :].astype(jnp.float32)
            lane = lax.broadcasted_iota(jnp.int32, tag.shape, 1)
            digits = jnp.where(lane == 0, tag * 64.0, jnp.where(lane == 1, tag, 0.0))
            length_v = jnp.sum(digits, axis=1, keepdims=True).astype(jnp.int32)
            for b in range(ck_ref.shape[0] // BK):
                step(b * BK, ck_ref, cv_ref, limit=length_v - b * BK)
        else:
            length = sc_ref[i]
            n_full = length // BK
            rem = length - n_full * BK

            def loop_body(b, c, ck_ref=ck_ref, cv_ref=cv_ref):
                step(pl.multiple_of(b * BK, BK), ck_ref, cv_ref)
                return c

            lax.fori_loop(0, n_full, loop_body, 0)

            @pl.when(rem > 0)
            def _(ck_ref=ck_ref, cv_ref=cv_ref, n_full=n_full, rem=rem):
                step(pl.multiple_of(n_full * BK, BK), ck_ref, cv_ref, limit=rem)

        @pl.when(origin < own)
        def _(sk_ref=sk_ref, sv_ref=sv_ref):
            for d in range(t_rows // BK):
                step(d * BK, sk_ref, sv_ref)

        @pl.when(origin == own)
        def _(sk_ref=sk_ref, sv_ref=sv_ref):
            for d in range(t_rows // BK):
                step(d * BK, sk_ref, sv_ref, causal=True)

    if last:
        (o_ref,) = o_refs
        out = acc_ref[...] / jnp.sum(l_ref[...], axis=1, keepdims=True)
        for g in range(group):
            o_ref[:, g * HD:(g + 1) * HD] = out[g * t_rows:(g + 1) * t_rows].astype(o_ref.dtype)


def attn_call(sc, q, insts, rows, state, first, last):
    t_rows, q_width = q.shape
    kv_width = insts[0][0].shape[2]
    kv_local = kv_width // HD
    group = q_width // kv_width
    c_rows, s_rows = rows
    rows_all = group * t_rows
    ninst = len(insts)
    kernel = functools.partial(step_kernel, vecs=tuple(v for *_, v in insts), t_rows=t_rows, group=group,
                               first=first, last=last)
    st_spec = pl.BlockSpec((rows_all, 128), lambda k, *_: (k, 0))
    st_shape = jax.ShapeDtypeStruct((kv_local * rows_all, 128), jnp.float32)
    in_specs = [pl.BlockSpec((t_rows, group * HD), lambda k, *_: (0, k))]
    args = [sc, q]
    for cache, span, srow, vec in insts:
        in_specs += [
            pl.BlockSpec((None, c_rows, HD), lambda k, *_: (0, 0, k)),
            pl.BlockSpec((None, c_rows, HD), lambda k, *_: (1, 0, k)),
            pl.BlockSpec((None, s_rows, HD), lambda k, *_, srow=srow: (0, srow, k)),
            pl.BlockSpec((None, s_rows, HD), lambda k, *_, srow=srow: (1, srow, k)),
        ]
        args += [cache, cache, span, span]
        if vec:
            tag_row = (c_rows + s_rows) // 16
            in_specs.append(pl.BlockSpec((None, 16, HD), lambda k, *_, tag_row=tag_row: (0, tag_row, 0)))
            args.append(cache)
    if not first:
        in_specs += [st_spec] * 3
        args += list(state)
    if last:
        out_specs = pl.BlockSpec((t_rows, group * HD), lambda k, *_: (0, k))
        out_shape = jax.ShapeDtypeStruct((t_rows, q_width), q.dtype)
    else:
        out_specs = [st_spec] * 3
        out_shape = [st_shape] * 3
    keys = ninst * (c_rows + s_rows)
    heads = kv_local * group
    cost = pl.CostEstimate(
        flops=4 * heads * t_rows * keys * HD,
        transcendentals=heads * t_rows * keys,
        bytes_accessed=2 * t_rows * q_width + 4 * keys * kv_width + 24 * kv_local * rows_all * 128,
    )
    grid_spec = pltpu.PrefetchScalarGridSpec(
        num_scalar_prefetch=1,
        grid=(kv_local,),
        in_specs=in_specs,
        out_specs=out_specs,
        scratch_shapes=[pltpu.VMEM((rows_all, HD), q.dtype)] + ([
            pltpu.VMEM((rows_all, 128), jnp.float32),
            pltpu.VMEM((rows_all, 128), jnp.float32),
            pltpu.VMEM((rows_all, HD), jnp.float32),
        ] if first and last else []),
    )
    return pl.pallas_call(
        kernel,
        out_shape=out_shape,
        grid_spec=grid_spec,
        compiler_params=pltpu.CompilerParams(dimension_semantics=("arbitrary",)),
        cost_estimate=cost,
    )(*args)


def chain_need(n, first_pairs, hops):
    need = []
    for k in range(len(hops)):
        keep = []
        for src in range(n):
            origin = first_pairs[src]
            dst = src
            for j in range(k + 1):
                dst = hops[j](dst)
            later = [dst, dst ^ 1]
            d = dst
            for j in range(k + 1, len(hops)):
                d = hops[j](d)
                later += [d, d ^ 1]
            if any(x > origin for x in later):
                keep.append(src)
        need.append(keep)
    return need


def body(query_rows, span_kv, cache_kv, cache_len):
    n = lax.psum(1, "seq")
    own = lax.axis_index("seq").astype(jnp.int32)
    n_chips = n // 2
    c_rows = cache_kv.shape[1]
    s_rows = span_kv.shape[1]
    kv_width = cache_kv.shape[2]
    length = cache_len.reshape(())
    tag = jnp.zeros((2, 16, kv_width), cache_kv.dtype)
    tag = tag.at[0, 0, 0].set((length // 64).astype(cache_kv.dtype))
    tag = tag.at[0, 0, 1].set((length % 64).astype(cache_kv.dtype))
    merged = jnp.concatenate([cache_kv, span_kv, tag], axis=1)
    srow = c_rows // s_rows

    def send(x, fn):
        return lax.ppermute(x, "seq", [(i, fn(i)) for i in range(n)])

    def length_of(blk):
        hi = blk[0, c_rows + s_rows, 0].astype(jnp.int32)
        lo = blk[0, c_rows + s_rows, 1].astype(jnp.int32)
        return hi * 64 + lo

    calls = [0]

    def run(phase, state):
        vals = [ln for _, ln, _ in phase] + [o for _, _, o in phase] + [own]
        slots = jnp.arange(len(vals), dtype=jnp.int32)
        sc = sum(jnp.where(slots == j, jnp.asarray(v, jnp.int32).reshape(()), 0) for j, v in enumerate(vals))
        insts = [b for b, _, _ in phase]
        first = calls[0] == 0
        calls[0] += 1
        return attn_call(sc, query_rows, insts, (c_rows, s_rows), state, first=first, last=(calls[0] == n_chips))

    part = send(merged, lambda i: i ^ 1)
    k_right = n_chips // 2
    k_left = n_chips - 1 - k_right
    hops = []
    for sign, count in ((2, k_right), (-2, k_left)):
        blk = merged
        for k in range(1, count + 1):
            blk = send(blk, lambda i, sign=sign: (i + sign) % n)
            hops.append((blk, sign, k))
    state = run([((cache_kv, span_kv, 0, False), length, own), ((part, part, srow, False), length_of(part), own ^ 1)], None)
    for blk, sign, k in hops:
        state, blk = lax.optimization_barrier((state, blk))
        origin = (own - sign * k) % n
        fwd = send(blk, lambda i: i ^ 1)
        state = run([((blk, blk, srow, False), length_of(blk), origin), ((fwd, fwd, srow, True), 0, origin ^ 1)], state)
    return state


def solution(mesh):
    in_specs = (
        P(("rep", "seq"), "head"),
        P(None, ("rep", "seq"), "head"),
        P(None, ("rep", "seq"), "head"),
        P(("rep", "seq")),
    )
    out_specs = P(("rep", "seq"), "head")
    return jax.shard_map(body, mesh=mesh, in_specs=in_specs, out_specs=out_specs, check_vma=False)
```

```python
import functools

import jax
import jax.numpy as jnp
from jax import lax
from jax.experimental import pallas as pl
from jax.experimental.pallas import tpu as pltpu
from jax.sharding import PartitionSpec as P

HD = 128
NEG = -1e30
BK = 256
BIG = 512


def step_kernel(sc_ref, q_ref, *refs, ninst, t_rows, group, first, last):
    inst_refs = [refs[4 * i:4 * i + 4] for i in range(ninst)]
    rest = refs[4 * ninst:]
    if first:
        state_in = None
    else:
        state_in, rest = rest[:3], rest[3:]
    if first and last:
        o_refs, (qs_ref, m_ref, l_ref, acc_ref) = rest[:-4], rest[-4:]
    else:
        o_refs, qs_ref = rest[:-1], rest[-1]
        if last:
            m_ref, l_ref, acc_ref = state_in
        else:
            m_ref, l_ref, acc_ref = o_refs
    own = sc_ref[2 * ninst]
    scale = HD ** (-0.5) * 1.4426950408889634
    rows_all = group * t_rows
    reps = BK // 128
    for g in range(group):
        qs_ref[g * t_rows:(g + 1) * t_rows, :] = q_ref[:, g * HD:(g + 1) * HD]
    if first:
        m_ref[...] = jnp.full(m_ref.shape, NEG, jnp.float32)
        l_ref[...] = jnp.zeros(l_ref.shape, jnp.float32)
        acc_ref[...] = jnp.zeros(acc_ref.shape, jnp.float32)
    elif not last:
        m_ref[...] = state_in[0][...]
        l_ref[...] = state_in[1][...]
        acc_ref[...] = state_in[2][...]

    def step(start, k_ref, v_ref, limit=None, causal=False, bk=BK):
        reps = bk // 128
        k = k_ref[pl.ds(start, bk), :]
        v = v_ref[pl.ds(start, bk), :]
        s = lax.dot_general(qs_ref[...], k, (((1,), (1,)), ((), ())), preferred_element_type=jnp.float32) * scale
        if limit is not None:
            mask = lax.broadcasted_iota(jnp.int32, (rows_all, bk), 1) < limit
            s = jnp.where(mask, s, NEG)
        if causal:
            cols = lax.broadcasted_iota(jnp.int32, (t_rows, BK), 1) + start
            rows = lax.broadcasted_iota(jnp.int32, (t_rows, BK), 0)
            mask = jnp.concatenate([cols <= rows] * group, axis=0)
            s = jnp.where(mask, s, NEG)
        m_prev = m_ref[...]
        m_new = jnp.maximum(m_prev, jnp.max(s, axis=1, keepdims=True))
        alpha = jnp.exp2(m_prev - m_new)
        m_wide = m_new if reps == 1 else jnp.concatenate([m_new] * reps, axis=1)
        p = jnp.exp2(s - m_wide)
        p_sum = p[:, :128]
        for r in range(1, reps):
            p_sum = p_sum + p[:, r * 128:(r + 1) * 128]
        l_ref[...] = alpha * l_ref[...] + p_sum
        acc_ref[...] = alpha * acc_ref[...] + jnp.dot(p.astype(v.dtype), v, preferred_element_type=jnp.float32)
        m_ref[...] = m_new

    for i, (ck_ref, cv_ref, sk_ref, sv_ref) in enumerate(inst_refs):
        length = sc_ref[i]
        origin = sc_ref[ninst + i]
        c_rows = ck_ref.shape[0]
        full = length == c_rows
        if c_rows % BIG == 0:
            @pl.when(full)
            def _(ck_ref=ck_ref, cv_ref=cv_ref):
                for b in range(c_rows // BIG):
                    step(b * BIG, ck_ref, cv_ref, bk=BIG)
        else:
            full = length < 0
        n_full = jnp.where(full, 0, length // BK)
        rem = jnp.where(full, 0, length - (length // BK) * BK)

        def loop_body(b, c, ck_ref=ck_ref, cv_ref=cv_ref):
            step(pl.multiple_of(b * BK, BK), ck_ref, cv_ref)
            return c

        lax.fori_loop(0, n_full, loop_body, 0)

        @pl.when(rem > 0)
        def _(ck_ref=ck_ref, cv_ref=cv_ref, n_full=n_full, rem=rem):
            step(pl.multiple_of(n_full * BK, BK), ck_ref, cv_ref, limit=rem)

        @pl.when(origin < own)
        def _(sk_ref=sk_ref, sv_ref=sv_ref):
            for d in range(t_rows // BK):
                step(d * BK, sk_ref, sv_ref)

        @pl.when(origin == own)
        def _(sk_ref=sk_ref, sv_ref=sv_ref):
            for d in range(t_rows // BK):
                step(d * BK, sk_ref, sv_ref, causal=True)

    if last:
        (o_ref,) = o_refs
        out = acc_ref[...] / jnp.sum(l_ref[...], axis=1, keepdims=True)
        for g in range(group):
            o_ref[:, g * HD:(g + 1) * HD] = out[g * t_rows:(g + 1) * t_rows].astype(o_ref.dtype)


def attn_call(sc, q, insts, rows, state, first, last):
    t_rows, q_width = q.shape
    kv_width = insts[0][0].shape[2]
    kv_local = kv_width // HD
    group = q_width // kv_width
    c_rows, s_rows = rows
    rows_all = group * t_rows
    ninst = len(insts)
    kernel = functools.partial(step_kernel, ninst=ninst, t_rows=t_rows, group=group, first=first, last=last)
    st_spec = pl.BlockSpec((rows_all, 128), lambda k, *_: (k, 0))
    st_shape = jax.ShapeDtypeStruct((kv_local * rows_all, 128), jnp.float32)
    in_specs = [pl.BlockSpec((t_rows, group * HD), lambda k, *_: (0, k))]
    args = [sc, q]
    for cache, span, srow in insts:
        in_specs += [
            pl.BlockSpec((None, c_rows, HD), lambda k, *_: (0, 0, k)),
            pl.BlockSpec((None, c_rows, HD), lambda k, *_: (1, 0, k)),
            pl.BlockSpec((None, s_rows, HD), lambda k, *_, srow=srow: (0, srow, k)),
            pl.BlockSpec((None, s_rows, HD), lambda k, *_, srow=srow: (1, srow, k)),
        ]
        args += [cache, cache, span, span]
    if not first:
        in_specs += [st_spec] * 3
        args += list(state)
    if last:
        out_specs = pl.BlockSpec((t_rows, group * HD), lambda k, *_: (0, k))
        out_shape = jax.ShapeDtypeStruct((t_rows, q_width), q.dtype)
    else:
        out_specs = [st_spec] * 3
        out_shape = [st_shape] * 3
    keys = ninst * (c_rows + s_rows)
    heads = kv_local * group
    cost = pl.CostEstimate(
        flops=4 * heads * t_rows * keys * HD,
        transcendentals=heads * t_rows * keys,
        bytes_accessed=2 * t_rows * q_width + 4 * keys * kv_width + 24 * kv_local * rows_all * 128,
    )
    grid_spec = pltpu.PrefetchScalarGridSpec(
        num_scalar_prefetch=1,
        grid=(kv_local,),
        in_specs=in_specs,
        out_specs=out_specs,
        scratch_shapes=[pltpu.VMEM((rows_all, HD), q.dtype)] + ([
            pltpu.VMEM((rows_all, 128), jnp.float32),
            pltpu.VMEM((rows_all, 128), jnp.float32),
            pltpu.VMEM((rows_all, HD), jnp.float32),
        ] if first and last else []),
    )
    return pl.pallas_call(
        kernel,
        out_shape=out_shape,
        grid_spec=grid_spec,
        compiler_params=pltpu.CompilerParams(dimension_semantics=("arbitrary",)),
        cost_estimate=cost,
    )(*args)


def chain_need(n, first_pairs, hops):
    need = []
    for k in range(len(hops)):
        keep = []
        for src in range(n):
            origin = first_pairs[src]
            dst = src
            for j in range(k + 1):
                dst = hops[j](dst)
            later = [dst, dst ^ 1]
            d = dst
            for j in range(k + 1, len(hops)):
                d = hops[j](d)
                later += [d, d ^ 1]
            if any(x > origin for x in later):
                keep.append(src)
        need.append(keep)
    return need


def body(query_rows, span_kv, cache_kv, cache_len):
    n = lax.psum(1, "seq")
    own = lax.axis_index("seq").astype(jnp.int32)
    n_chips = n // 2
    c_rows = cache_kv.shape[1]
    s_rows = span_kv.shape[1]
    kv_width = cache_kv.shape[2]
    length = cache_len.reshape(())
    tag = jnp.zeros((2, 16, kv_width), cache_kv.dtype)
    tag = tag.at[0, 0, 0].set((length // 64).astype(cache_kv.dtype))
    tag = tag.at[0, 0, 1].set((length % 64).astype(cache_kv.dtype))
    merged = jnp.concatenate([cache_kv, span_kv, tag], axis=1)
    srow = c_rows // s_rows

    def send(x, fn):
        return lax.ppermute(x, "seq", [(i, fn(i)) for i in range(n)])

    def length_of(blk):
        hi = blk[0, c_rows + s_rows, 0].astype(jnp.int32)
        lo = blk[0, c_rows + s_rows, 1].astype(jnp.int32)
        return hi * 64 + lo

    calls = [0]

    def run(phase, state):
        vals = [ln for _, ln, _ in phase] + [o for _, _, o in phase] + [own]
        slots = jnp.arange(len(vals), dtype=jnp.int32)
        sc = sum(jnp.where(slots == j, jnp.asarray(v, jnp.int32).reshape(()), 0) for j, v in enumerate(vals))
        insts = [b for b, _, _ in phase]
        first = calls[0] == 0
        calls[0] += 1
        return attn_call(sc, query_rows, insts, (c_rows, s_rows), state, first=first, last=(calls[0] == n_chips))

    part = send(merged, lambda i: i ^ 1)
    k_right = n_chips // 2
    k_left = n_chips - 1 - k_right
    hops = []
    for sign, count in ((2, k_right), (-2, k_left)):
        blk = merged
        for k in range(1, count + 1):
            blk = send(blk, lambda i, sign=sign: (i + sign) % n)
            hops.append((blk, sign, k))
    state = run([((cache_kv, span_kv, 0), length, own), ((part, part, srow), length_of(part), own ^ 1)], None)
    for blk, sign, k in hops:
        state, blk = lax.optimization_barrier((state, blk))
        origin = (own - sign * k) % n
        fwd = send(blk, lambda i: i ^ 1)
        state = run([((blk, blk, srow), length_of(blk), origin), ((fwd, fwd, srow), length_of(fwd), origin ^ 1)], state)
    return state


def solution(mesh):
    in_specs = (
        P(("rep", "seq"), "head"),
        P(None, ("rep", "seq"), "head"),
        P(None, ("rep", "seq"), "head"),
        P(("rep", "seq")),
    )
    out_specs = P(("rep", "seq"), "head")
    return jax.shard_map(body, mesh=mesh, in_specs=in_specs, out_specs=out_specs, check_vma=False)
```

```python
import functools

import jax
import jax.numpy as jnp
from jax import lax
from jax.experimental import pallas as pl
from jax.experimental.pallas import tpu as pltpu
from jax.sharding import PartitionSpec as P

HD = 128
NEG = -1e30
BK = 256


def step_kernel(sc_ref, qs_ref, *refs, ninst, t_rows, group, first, last):
    inst_refs = [refs[4 * i:4 * i + 4] for i in range(ninst)]
    rest = refs[4 * ninst:]
    if first:
        state_in = None
    else:
        state_in, rest = rest[:3], rest[3:]
    if first and last:
        o_refs, (m_ref, l_ref, acc_ref) = rest[:-3], rest[-3:]
    else:
        o_refs = rest
        if last:
            m_ref, l_ref, acc_ref = state_in
        else:
            m_ref, l_ref, acc_ref = o_refs
    own = sc_ref[2 * ninst]
    scale = HD ** (-0.5) * 1.4426950408889634
    rows_all = group * t_rows
    reps = BK // 128
    if first:
        m_ref[...] = jnp.full(m_ref.shape, NEG, jnp.float32)
        l_ref[...] = jnp.zeros(l_ref.shape, jnp.float32)
        acc_ref[...] = jnp.zeros(acc_ref.shape, jnp.float32)
    elif not last:
        m_ref[...] = state_in[0][...]
        l_ref[...] = state_in[1][...]
        acc_ref[...] = state_in[2][...]

    def step(start, k_ref, v_ref, limit=None, causal=False):
        k = k_ref[pl.ds(start, BK), :]
        v = v_ref[pl.ds(start, BK), :]
        s = lax.dot_general(qs_ref[...], k, (((1,), (1,)), ((), ())), preferred_element_type=jnp.float32) * scale
        if limit is not None:
            mask = lax.broadcasted_iota(jnp.int32, (rows_all, BK), 1) < limit
            s = jnp.where(mask, s, NEG)
        if causal:
            cols = lax.broadcasted_iota(jnp.int32, (t_rows, BK), 1) + start
            rows = lax.broadcasted_iota(jnp.int32, (t_rows, BK), 0)
            mask = jnp.concatenate([cols <= rows] * group, axis=0)
            s = jnp.where(mask, s, NEG)
        m_prev = m_ref[...]
        m_new = jnp.maximum(m_prev, jnp.max(s, axis=1, keepdims=True))
        alpha = jnp.exp2(m_prev - m_new)
        m_wide = m_new if reps == 1 else jnp.concatenate([m_new] * reps, axis=1)
        p = jnp.exp2(s - m_wide)
        p_sum = p[:, :128]
        for r in range(1, reps):
            p_sum = p_sum + p[:, r * 128:(r + 1) * 128]
        l_ref[...] = alpha * l_ref[...] + p_sum
        acc_ref[...] = alpha * acc_ref[...] + jnp.dot(p.astype(v.dtype), v, preferred_element_type=jnp.float32)
        m_ref[...] = m_new

    for i, (ck_ref, cv_ref, sk_ref, sv_ref) in enumerate(inst_refs):
        length = sc_ref[i]
        origin = sc_ref[ninst + i]
        n_full = length // BK
        rem = length - n_full * BK

        def loop_body(b, c, ck_ref=ck_ref, cv_ref=cv_ref):
            step(pl.multiple_of(b * BK, BK), ck_ref, cv_ref)
            return c

        lax.fori_loop(0, n_full, loop_body, 0)

        @pl.when(rem > 0)
        def _(ck_ref=ck_ref, cv_ref=cv_ref, n_full=n_full, rem=rem):
            step(pl.multiple_of(n_full * BK, BK), ck_ref, cv_ref, limit=rem)

        @pl.when(origin < own)
        def _(sk_ref=sk_ref, sv_ref=sv_ref):
            for d in range(t_rows // BK):
                step(d * BK, sk_ref, sv_ref)

        @pl.when(origin == own)
        def _(sk_ref=sk_ref, sv_ref=sv_ref):
            for d in range(t_rows // BK):
                step(d * BK, sk_ref, sv_ref, causal=True)

    if last:
        (o_ref,) = o_refs
        out = acc_ref[...] / jnp.sum(l_ref[...], axis=1, keepdims=True)
        for g in range(group):
            o_ref[:, g * HD:(g + 1) * HD] = out[g * t_rows:(g + 1) * t_rows].astype(o_ref.dtype)


def attn_call(sc, q, insts, rows, state, first, last):
    q_width = q.shape[1]
    t_rows = q.shape[0]
    kv_width = insts[0][0].shape[2]
    kv_local = kv_width // HD
    group = q_width // kv_width
    c_rows, s_rows = rows
    rows_all = group * t_rows
    ninst = len(insts)
    kernel = functools.partial(step_kernel, ninst=ninst, t_rows=t_rows, group=group, first=first, last=last)
    st_spec = pl.BlockSpec((rows_all, 128), lambda k, *_: (k, 0))
    st_shape = jax.ShapeDtypeStruct((kv_local * rows_all, 128), jnp.float32)
    q_stacked = q.reshape(t_rows, kv_local * group, HD).transpose(1, 0, 2).reshape(kv_local * rows_all, HD)
    in_specs = [pl.BlockSpec((rows_all, HD), lambda k, *_: (k, 0))]
    args = [sc, q_stacked]
    for cache, span, srow in insts:
        in_specs += [
            pl.BlockSpec((None, c_rows, HD), lambda k, *_: (0, 0, k)),
            pl.BlockSpec((None, c_rows, HD), lambda k, *_: (1, 0, k)),
            pl.BlockSpec((None, s_rows, HD), lambda k, *_, srow=srow: (0, srow, k)),
            pl.BlockSpec((None, s_rows, HD), lambda k, *_, srow=srow: (1, srow, k)),
        ]
        args += [cache, cache, span, span]
    if not first:
        in_specs += [st_spec] * 3
        args += list(state)
    if last:
        out_specs = pl.BlockSpec((t_rows, group * HD), lambda k, *_: (0, k))
        out_shape = jax.ShapeDtypeStruct((t_rows, q_width), q.dtype)
    else:
        out_specs = [st_spec] * 3
        out_shape = [st_shape] * 3
    keys = ninst * (c_rows + s_rows)
    heads = kv_local * group
    cost = pl.CostEstimate(
        flops=4 * heads * t_rows * keys * HD,
        transcendentals=heads * t_rows * keys,
        bytes_accessed=2 * t_rows * q_width + 4 * keys * kv_width + 24 * kv_local * rows_all * 128,
    )
    grid_spec = pltpu.PrefetchScalarGridSpec(
        num_scalar_prefetch=1,
        grid=(kv_local,),
        in_specs=in_specs,
        out_specs=out_specs,
        scratch_shapes=[
            pltpu.VMEM((rows_all, 128), jnp.float32),
            pltpu.VMEM((rows_all, 128), jnp.float32),
            pltpu.VMEM((rows_all, HD), jnp.float32),
        ] if first and last else [],
    )
    return pl.pallas_call(
        kernel,
        out_shape=out_shape,
        grid_spec=grid_spec,
        compiler_params=pltpu.CompilerParams(dimension_semantics=("arbitrary",)),
        cost_estimate=cost,
    )(*args)


def chain_need(n, first_pairs, hops):
    need = []
    for k in range(len(hops)):
        keep = []
        for src in range(n):
            origin = first_pairs[src]
            dst = src
            for j in range(k + 1):
                dst = hops[j](dst)
            later = [dst, dst ^ 1]
            d = dst
            for j in range(k + 1, len(hops)):
                d = hops[j](d)
                later += [d, d ^ 1]
            if any(x > origin for x in later):
                keep.append(src)
        need.append(keep)
    return need


def body(query_rows, span_kv, cache_kv, cache_len):
    n = lax.psum(1, "seq")
    own = lax.axis_index("seq").astype(jnp.int32)
    n_chips = n // 2
    c_rows = cache_kv.shape[1]
    s_rows = span_kv.shape[1]
    kv_width = cache_kv.shape[2]
    length = cache_len.reshape(())
    tag = jnp.zeros((2, 16, kv_width), cache_kv.dtype)
    tag = tag.at[0, 0, 0].set((length // 64).astype(cache_kv.dtype))
    tag = tag.at[0, 0, 1].set((length % 64).astype(cache_kv.dtype))
    merged = jnp.concatenate([cache_kv, span_kv, tag], axis=1)
    srow = c_rows // s_rows

    def send(x, fn):
        return lax.ppermute(x, "seq", [(i, fn(i)) for i in range(n)])

    def length_of(blk):
        hi = blk[0, c_rows + s_rows, 0].astype(jnp.int32)
        lo = blk[0, c_rows + s_rows, 1].astype(jnp.int32)
        return hi * 64 + lo

    calls = [0]

    def run(phase, state):
        vals = [ln for _, ln, _ in phase] + [o for _, _, o in phase] + [own]
        slots = jnp.arange(len(vals), dtype=jnp.int32)
        sc = sum(jnp.where(slots == j, jnp.asarray(v, jnp.int32).reshape(()), 0) for j, v in enumerate(vals))
        insts = [b for b, _, _ in phase]
        first = calls[0] == 0
        calls[0] += 1
        return attn_call(sc, query_rows, insts, (c_rows, s_rows), state, first=first, last=(calls[0] == n_chips))

    part = send(merged, lambda i: i ^ 1)
    k_right = n_chips // 2
    k_left = n_chips - 1 - k_right
    hops = []
    for sign, count in ((2, k_right), (-2, k_left)):
        blk = merged
        for k in range(1, count + 1):
            blk = send(blk, lambda i, sign=sign: (i + sign) % n)
            hops.append((blk, sign, k))
    state = run([((cache_kv, span_kv, 0), length, own), ((part, part, srow), length_of(part), own ^ 1)], None)
    for blk, sign, k in hops:
        state, blk = lax.optimization_barrier((state, blk))
        origin = (own - sign * k) % n
        fwd = send(blk, lambda i: i ^ 1)
        state = run([((blk, blk, srow), length_of(blk), origin), ((fwd, fwd, srow), length_of(fwd), origin ^ 1)], state)
    return state


def solution(mesh):
    in_specs = (
        P(("rep", "seq"), "head"),
        P(None, ("rep", "seq"), "head"),
        P(None, ("rep", "seq"), "head"),
        P(("rep", "seq")),
    )
    out_specs = P(("rep", "seq"), "head")
    return jax.shard_map(body, mesh=mesh, in_specs=in_specs, out_specs=out_specs, check_vma=False)
```

```python
import functools

import jax
import jax.numpy as jnp
from jax import lax
from jax.experimental import pallas as pl
from jax.experimental.pallas import tpu as pltpu
from jax.sharding import PartitionSpec as P

HD = 128
NEG = -1e30
BK = 256


def step_kernel(sc_ref, q_ref, *refs, ninst, t_rows, group, first, last):
    inst_refs = [refs[4 * i:4 * i + 4] for i in range(ninst)]
    rest = refs[4 * ninst:]
    if first:
        state_in = None
    else:
        state_in, rest = rest[:3], rest[3:]
    if first and last:
        o_refs, (qs_ref, m_ref, l_ref, acc_ref) = rest[:-4], rest[-4:]
    else:
        o_refs, qs_ref = rest[:-1], rest[-1]
        if last:
            m_ref, l_ref, acc_ref = state_in
        else:
            m_ref, l_ref, acc_ref = o_refs
    own = sc_ref[2 * ninst]
    scale = HD ** (-0.5) * 1.4426950408889634
    rows_all = group * t_rows
    reps = BK // 128
    for g in range(group):
        qs_ref[g * t_rows:(g + 1) * t_rows, :] = q_ref[:, g * HD:(g + 1) * HD]
    if first:
        m_ref[...] = jnp.full(m_ref.shape, NEG, jnp.float32)
        l_ref[...] = jnp.zeros(l_ref.shape, jnp.float32)
        acc_ref[...] = jnp.zeros(acc_ref.shape, jnp.float32)
    elif not last:
        m_ref[...] = state_in[0][...]
        l_ref[...] = state_in[1][...]
        acc_ref[...] = state_in[2][...]

    def step(start, k_ref, v_ref, limit=None, causal=False):
        k = k_ref[pl.ds(start, BK), :]
        v = v_ref[pl.ds(start, BK), :]
        s = lax.dot_general(qs_ref[...], k, (((1,), (1,)), ((), ())), preferred_element_type=jnp.float32) * scale
        if limit is not None:
            mask = lax.broadcasted_iota(jnp.int32, (rows_all, BK), 1) < limit
            s = jnp.where(mask, s, NEG)
        if causal:
            cols = lax.broadcasted_iota(jnp.int32, (t_rows, BK), 1) + start
            rows = lax.broadcasted_iota(jnp.int32, (t_rows, BK), 0)
            mask = jnp.concatenate([cols <= rows] * group, axis=0)
            s = jnp.where(mask, s, NEG)
        m_prev = m_ref[...]
        m_new = jnp.maximum(m_prev, jnp.max(s, axis=1, keepdims=True))
        alpha = jnp.exp2(m_prev - m_new)
        m_wide = m_new if reps == 1 else jnp.concatenate([m_new] * reps, axis=1)
        p = jnp.exp2(s - m_wide)
        p_sum = p[:, :128]
        for r in range(1, reps):
            p_sum = p_sum + p[:, r * 128:(r + 1) * 128]
        l_ref[...] = alpha * l_ref[...] + p_sum
        acc_ref[...] = alpha * acc_ref[...] + jnp.dot(p.astype(v.dtype), v, preferred_element_type=jnp.float32)
        m_ref[...] = m_new

    for i, (ck_ref, cv_ref, sk_ref, sv_ref) in enumerate(inst_refs):
        length = sc_ref[i]
        origin = sc_ref[ninst + i]
        n_full = length // BK
        rem = length - n_full * BK

        def loop_body(b, c, ck_ref=ck_ref, cv_ref=cv_ref):
            step(pl.multiple_of(b * BK, BK), ck_ref, cv_ref)
            return c

        lax.fori_loop(0, n_full, loop_body, 0)

        @pl.when(rem > 0)
        def _(ck_ref=ck_ref, cv_ref=cv_ref, n_full=n_full, rem=rem):
            step(pl.multiple_of(n_full * BK, BK), ck_ref, cv_ref, limit=rem)

        @pl.when(origin < own)
        def _(sk_ref=sk_ref, sv_ref=sv_ref):
            for d in range(t_rows // BK):
                step(d * BK, sk_ref, sv_ref)

        @pl.when(origin == own)
        def _(sk_ref=sk_ref, sv_ref=sv_ref):
            for d in range(t_rows // BK):
                step(d * BK, sk_ref, sv_ref, causal=True)

    if last:
        (o_ref,) = o_refs
        out = acc_ref[...] / jnp.sum(l_ref[...], axis=1, keepdims=True)
        for g in range(group):
            o_ref[:, g * HD:(g + 1) * HD] = out[g * t_rows:(g + 1) * t_rows].astype(o_ref.dtype)


def attn_call(sc, q, insts, rows, state, first, last):
    t_rows, q_width = q.shape
    kv_width = insts[0][0].shape[2]
    kv_local = kv_width // HD
    group = q_width // kv_width
    c_rows, s_rows = rows
    rows_all = group * t_rows
    ninst = len(insts)
    kernel = functools.partial(step_kernel, ninst=ninst, t_rows=t_rows, group=group, first=first, last=last)
    st_spec = pl.BlockSpec((rows_all, 128), lambda k, *_: (k, 0))
    st_shape = jax.ShapeDtypeStruct((kv_local * rows_all, 128), jnp.float32)
    in_specs = [pl.BlockSpec((t_rows, group * HD), lambda k, *_: (0, k))]
    args = [sc, q]
    for cache, span, srow in insts:
        in_specs += [
            pl.BlockSpec((None, c_rows, HD), lambda k, *_: (0, 0, k)),
            pl.BlockSpec((None, c_rows, HD), lambda k, *_: (1, 0, k)),
            pl.BlockSpec((None, s_rows, HD), lambda k, *_, srow=srow: (0, srow, k)),
            pl.BlockSpec((None, s_rows, HD), lambda k, *_, srow=srow: (1, srow, k)),
        ]
        args += [cache, cache, span, span]
    if not first:
        in_specs += [st_spec] * 3
        args += list(state)
    if last:
        out_specs = pl.BlockSpec((t_rows, group * HD), lambda k, *_: (0, k))
        out_shape = jax.ShapeDtypeStruct((t_rows, q_width), q.dtype)
    else:
        out_specs = [st_spec] * 3
        out_shape = [st_shape] * 3
    keys = ninst * (c_rows + s_rows)
    heads = kv_local * group
    cost = pl.CostEstimate(
        flops=4 * heads * t_rows * keys * HD,
        transcendentals=heads * t_rows * keys,
        bytes_accessed=2 * t_rows * q_width + 4 * keys * kv_width + 24 * kv_local * rows_all * 128,
    )
    grid_spec = pltpu.PrefetchScalarGridSpec(
        num_scalar_prefetch=1,
        grid=(kv_local,),
        in_specs=in_specs,
        out_specs=out_specs,
        scratch_shapes=[pltpu.VMEM((rows_all, HD), q.dtype)] + ([
            pltpu.VMEM((rows_all, 128), jnp.float32),
            pltpu.VMEM((rows_all, 128), jnp.float32),
            pltpu.VMEM((rows_all, HD), jnp.float32),
        ] if first and last else []),
    )
    return pl.pallas_call(
        kernel,
        out_shape=out_shape,
        grid_spec=grid_spec,
        compiler_params=pltpu.CompilerParams(dimension_semantics=("arbitrary",), vmem_limit_bytes=24 * 1024 * 1024),
        cost_estimate=cost,
    )(*args)


def chain_need(n, first_pairs, hops):
    need = []
    for k in range(len(hops)):
        keep = []
        for src in range(n):
            origin = first_pairs[src]
            dst = src
            for j in range(k + 1):
                dst = hops[j](dst)
            later = [dst, dst ^ 1]
            d = dst
            for j in range(k + 1, len(hops)):
                d = hops[j](d)
                later += [d, d ^ 1]
            if any(x > origin for x in later):
                keep.append(src)
        need.append(keep)
    return need


def body(query_rows, span_kv, cache_kv, cache_len):
    n = lax.psum(1, "seq")
    own = lax.axis_index("seq").astype(jnp.int32)
    n_chips = n // 2
    c_rows = cache_kv.shape[1]
    s_rows = span_kv.shape[1]
    kv_width = cache_kv.shape[2]
    length = cache_len.reshape(())
    tag = jnp.zeros((2, 16, kv_width), cache_kv.dtype)
    tag = tag.at[0, 0, 0].set((length // 64).astype(cache_kv.dtype))
    tag = tag.at[0, 0, 1].set((length % 64).astype(cache_kv.dtype))
    merged = jnp.concatenate([cache_kv, span_kv, tag], axis=1)
    srow = c_rows // s_rows

    def send(x, fn):
        return lax.ppermute(x, "seq", [(i, fn(i)) for i in range(n)])

    def length_of(blk):
        hi = blk[0, c_rows + s_rows, 0].astype(jnp.int32)
        lo = blk[0, c_rows + s_rows, 1].astype(jnp.int32)
        return hi * 64 + lo

    calls = [0]

    def run(phase, state):
        vals = [ln for _, ln, _ in phase] + [o for _, _, o in phase] + [own]
        slots = jnp.arange(len(vals), dtype=jnp.int32)
        sc = sum(jnp.where(slots == j, jnp.asarray(v, jnp.int32).reshape(()), 0) for j, v in enumerate(vals))
        insts = [b for b, _, _ in phase]
        first = calls[0] == 0
        calls[0] += 1
        return attn_call(sc, query_rows, insts, (c_rows, s_rows), state, first=first, last=(calls[0] == n_chips))

    part = send(merged, lambda i: i ^ 1)
    k_right = n_chips // 2
    k_left = n_chips - 1 - k_right
    hops = []
    for sign, count in ((2, k_right), (-2, k_left)):
        blk = merged
        for k in range(1, count + 1):
            blk = send(blk, lambda i, sign=sign: (i + sign) % n)
            hops.append((blk, sign, k))
    state = run([((cache_kv, span_kv, 0), length, own), ((part, part, srow), length_of(part), own ^ 1)], None)
    for blk, sign, k in hops:
        state, blk = lax.optimization_barrier((state, blk))
        origin = (own - sign * k) % n
        fwd = send(blk, lambda i: i ^ 1)
        state = run([((blk, blk, srow), length_of(blk), origin), ((fwd, fwd, srow), length_of(fwd), origin ^ 1)], state)
    return state


def solution(mesh):
    in_specs = (
        P(("rep", "seq"), "head"),
        P(None, ("rep", "seq"), "head"),
        P(None, ("rep", "seq"), "head"),
        P(("rep", "seq")),
    )
    out_specs = P(("rep", "seq"), "head")
    return jax.shard_map(body, mesh=mesh, in_specs=in_specs, out_specs=out_specs, check_vma=False)
```

```python
import functools

import jax
import jax.numpy as jnp
from jax import lax
from jax.experimental import pallas as pl
from jax.experimental.pallas import tpu as pltpu
from jax.sharding import PartitionSpec as P

HD = 128
NEG = -1e30
BK = 256


def step_kernel(sc_ref, q_ref, *refs, ninst, t_rows, group, first, last):
    inst_refs = [refs[4 * i:4 * i + 4] for i in range(ninst)]
    rest = refs[4 * ninst:]
    if first:
        state_in = None
    else:
        state_in, rest = rest[:3], rest[3:]
    if first and last:
        o_refs, (qs_ref, m_ref, l_ref, acc_ref) = rest[:-4], rest[-4:]
    else:
        o_refs, qs_ref = rest[:-1], rest[-1]
        if last:
            m_ref, l_ref, acc_ref = state_in
        else:
            m_ref, l_ref, acc_ref = o_refs
    own = sc_ref[2 * ninst]
    scale = HD ** (-0.5) * 1.4426950408889634
    rows_all = group * t_rows
    reps = BK // 128
    for g in range(group):
        qs_ref[g * t_rows:(g + 1) * t_rows, :] = q_ref[:, g * HD:(g + 1) * HD]
    if first:
        m_ref[...] = jnp.full(m_ref.shape, NEG, jnp.float32)
        l_ref[...] = jnp.zeros(l_ref.shape, jnp.float32)
        acc_ref[...] = jnp.zeros(acc_ref.shape, jnp.float32)
    elif not last:
        m_ref[...] = state_in[0][...]
        l_ref[...] = state_in[1][...]
        acc_ref[...] = state_in[2][...]

    def step(start, k_ref, v_ref, limit=None, causal=False):
        k = k_ref[pl.ds(start, BK), :]
        v = v_ref[pl.ds(start, BK), :]
        s = lax.dot_general(qs_ref[...], k, (((1,), (1,)), ((), ())), preferred_element_type=jnp.float32) * scale
        if limit is not None:
            mask = lax.broadcasted_iota(jnp.int32, (rows_all, BK), 1) < limit
            s = jnp.where(mask, s, NEG)
        if causal:
            cols = lax.broadcasted_iota(jnp.int32, (t_rows, BK), 1) + start
            rows = lax.broadcasted_iota(jnp.int32, (t_rows, BK), 0)
            mask = jnp.concatenate([cols <= rows] * group, axis=0)
            s = jnp.where(mask, s, NEG)
        m_prev = m_ref[...]
        m_new = jnp.maximum(m_prev, jnp.max(s, axis=1, keepdims=True))
        alpha = jnp.exp2(m_prev - m_new)
        m_wide = m_new if reps == 1 else jnp.concatenate([m_new] * reps, axis=1)
        p = jnp.exp2(s - m_wide)
        p_sum = p[:, :128]
        for r in range(1, reps):
            p_sum = p_sum + p[:, r * 128:(r + 1) * 128]
        l_ref[...] = alpha * l_ref[...] + p_sum
        acc_ref[...] = alpha * acc_ref[...] + jnp.dot(p.astype(v.dtype), v, preferred_element_type=jnp.float32)
        m_ref[...] = m_new

    for i, (ck_ref, cv_ref, sk_ref, sv_ref) in enumerate(inst_refs):
        length = sc_ref[i]
        origin = sc_ref[ninst + i]
        n_full = length // BK
        rem = length - n_full * BK

        def loop_body(b, c, ck_ref=ck_ref, cv_ref=cv_ref):
            step(pl.multiple_of(b * BK, BK), ck_ref, cv_ref)
            return c

        lax.fori_loop(0, n_full, loop_body, 0)

        @pl.when(rem > 0)
        def _(ck_ref=ck_ref, cv_ref=cv_ref, n_full=n_full, rem=rem):
            step(pl.multiple_of(n_full * BK, BK), ck_ref, cv_ref, limit=rem)

        @pl.when(origin < own)
        def _(sk_ref=sk_ref, sv_ref=sv_ref):
            for d in range(t_rows // BK):
                step(d * BK, sk_ref, sv_ref)

        @pl.when(origin == own)
        def _(sk_ref=sk_ref, sv_ref=sv_ref):
            for d in range(t_rows // BK):
                step(d * BK, sk_ref, sv_ref, causal=True)

    if last:
        (o_ref,) = o_refs
        out = acc_ref[...] / jnp.sum(l_ref[...], axis=1, keepdims=True)
        for g in range(group):
            o_ref[:, g * HD:(g + 1) * HD] = out[g * t_rows:(g + 1) * t_rows].astype(o_ref.dtype)


def attn_call(sc, q, insts, rows, state, first, last):
    t_rows, q_width = q.shape
    kv_width = insts[0][0].shape[2]
    kv_local = kv_width // HD
    group = q_width // kv_width
    c_rows, s_rows = rows
    rows_all = group * t_rows
    ninst = len(insts)
    kernel = functools.partial(step_kernel, ninst=ninst, t_rows=t_rows, group=group, first=first, last=last)
    st_spec = pl.BlockSpec((rows_all, 128), lambda k, *_: (k, 0))
    st_shape = jax.ShapeDtypeStruct((kv_local * rows_all, 128), jnp.float32)
    in_specs = [pl.BlockSpec((t_rows, group * HD), lambda k, *_: (0, k))]
    args = [sc, q]
    for cache, span, srow in insts:
        in_specs += [
            pl.BlockSpec((None, c_rows, HD), lambda k, *_: (0, 0, k)),
            pl.BlockSpec((None, c_rows, HD), lambda k, *_: (1, 0, k)),
            pl.BlockSpec((None, s_rows, HD), lambda k, *_, srow=srow: (0, srow, k)),
            pl.BlockSpec((None, s_rows, HD), lambda k, *_, srow=srow: (1, srow, k)),
        ]
        args += [cache, cache, span, span]
    if not first:
        in_specs += [st_spec] * 3
        args += list(state)
    if last:
        out_specs = pl.BlockSpec((t_rows, group * HD), lambda k, *_: (0, k))
        out_shape = jax.ShapeDtypeStruct((t_rows, q_width), q.dtype)
    else:
        out_specs = [st_spec] * 3
        out_shape = [st_shape] * 3
    keys = ninst * (c_rows + s_rows)
    heads = kv_local * group
    cost = pl.CostEstimate(
        flops=4 * heads * t_rows * keys * HD,
        transcendentals=heads * t_rows * keys,
        bytes_accessed=2 * t_rows * q_width + 4 * keys * kv_width + 24 * kv_local * rows_all * 128,
    )
    grid_spec = pltpu.PrefetchScalarGridSpec(
        num_scalar_prefetch=1,
        grid=(kv_local,),
        in_specs=in_specs,
        out_specs=out_specs,
        scratch_shapes=[pltpu.VMEM((rows_all, HD), q.dtype)] + ([
            pltpu.VMEM((rows_all, 128), jnp.float32),
            pltpu.VMEM((rows_all, 128), jnp.float32),
            pltpu.VMEM((rows_all, HD), jnp.float32),
        ] if first and last else []),
    )
    return pl.pallas_call(
        kernel,
        out_shape=out_shape,
        grid_spec=grid_spec,
        compiler_params=pltpu.CompilerParams(dimension_semantics=("arbitrary",), vmem_limit_bytes=64 * 1024 * 1024),
        cost_estimate=cost,
    )(*args)


def chain_need(n, first_pairs, hops):
    need = []
    for k in range(len(hops)):
        keep = []
        for src in range(n):
            origin = first_pairs[src]
            dst = src
            for j in range(k + 1):
                dst = hops[j](dst)
            later = [dst, dst ^ 1]
            d = dst
            for j in range(k + 1, len(hops)):
                d = hops[j](d)
                later += [d, d ^ 1]
            if any(x > origin for x in later):
                keep.append(src)
        need.append(keep)
    return need


def body(query_rows, span_kv, cache_kv, cache_len):
    n = lax.psum(1, "seq")
    own = lax.axis_index("seq").astype(jnp.int32)
    n_chips = n // 2
    c_rows = cache_kv.shape[1]
    s_rows = span_kv.shape[1]
    kv_width = cache_kv.shape[2]
    length = cache_len.reshape(())
    tag = jnp.zeros((2, 16, kv_width), cache_kv.dtype)
    tag = tag.at[0, 0, 0].set((length // 64).astype(cache_kv.dtype))
    tag = tag.at[0, 0, 1].set((length % 64).astype(cache_kv.dtype))
    merged = jnp.concatenate([cache_kv, span_kv, tag], axis=1)
    srow = c_rows // s_rows

    def send(x, fn):
        return lax.ppermute(x, "seq", [(i, fn(i)) for i in range(n)])

    def length_of(blk):
        hi = blk[0, c_rows + s_rows, 0].astype(jnp.int32)
        lo = blk[0, c_rows + s_rows, 1].astype(jnp.int32)
        return hi * 64 + lo

    calls = [0]

    def run(phase, state):
        vals = [ln for _, ln, _ in phase] + [o for _, _, o in phase] + [own]
        slots = jnp.arange(len(vals), dtype=jnp.int32)
        sc = sum(jnp.where(slots == j, jnp.asarray(v, jnp.int32).reshape(()), 0) for j, v in enumerate(vals))
        insts = [b for b, _, _ in phase]
        first = calls[0] == 0
        calls[0] += 1
        return attn_call(sc, query_rows, insts, (c_rows, s_rows), state, first=first, last=(calls[0] == n_chips))

    part = send(merged, lambda i: i ^ 1)
    k_right = n_chips // 2
    k_left = n_chips - 1 - k_right
    hops = []
    for sign, count in ((2, k_right), (-2, k_left)):
        blk = merged
        for k in range(1, count + 1):
            blk = send(blk, lambda i, sign=sign: (i + sign) % n)
            hops.append((blk, sign, k))
    state = run([((cache_kv, span_kv, 0), length, own), ((part, part, srow), length_of(part), own ^ 1)], None)
    for blk, sign, k in hops:
        state, blk = lax.optimization_barrier((state, blk))
        origin = (own - sign * k) % n
        fwd = send(blk, lambda i: i ^ 1)
        state = run([((blk, blk, srow), length_of(blk), origin), ((fwd, fwd, srow), length_of(fwd), origin ^ 1)], state)
    return state


def solution(mesh):
    in_specs = (
        P(("rep", "seq"), "head"),
        P(None, ("rep", "seq"), "head"),
        P(None, ("rep", "seq"), "head"),
        P(("rep", "seq")),
    )
    out_specs = P(("rep", "seq"), "head")
    return jax.shard_map(body, mesh=mesh, in_specs=in_specs, out_specs=out_specs, check_vma=False)
```
